256 devices in a mesh: gx: 32 (over z_lo, y, core), gy: 4 (over x), gz: 2 (over z_hi).
Axes of the slice: x: 4, y: 4, z: 8 (z_hi: 2, z_lo: 4; z = z_hi * 4 + z_lo), core: 2. Of those that a mesh axis runs over, the one named last changes fastest.
Arguments:
- f_pop: float32 [19, 128, 64, 256], P(None, 'gx', 'gy', 'gz'), may hold values from 0.02 to 0.1
- g_pop: float32 [19, 128, 64, 256], P(None, 'gx', 'gy', 'gz'), may hold values from -0.2 to 0.2
- displacement: int32 [1], replicated, may hold values from 33 to 47
Outputs:
- f_new: float32 [19, 128, 64, 256], P(None, 'gx', 'gy', 'gz')
- g_new: float32 [19, 128, 64, 256], P(None, 'gx', 'gy', 'gz')
The draws below stay inside these ranges and needn't reach their ends.
All inputs are finite; a program needn't handle non-finite values.
Results may differ from the reference program's by a relative error of at most 0.0001.
Values sent between devices are 32-bit elements; how exact they have to be, the bound alone decides.
No kernel may reach another device: no remote copies, remote signals or barrier semaphores. Data moves between devices by JAX's collectives and lax.ppermute only.
A program may use at most 64 MiB of HBM per device.

```python
import jax
import jax.numpy as jnp

CX = 4
CY = 16
POPS = 19
NX = 128
NY = 64
NZ = 256


def steps_of(stream_key, dims, pieces, low, top_value):
    loudness, own = 1.0, jax.random.fold_in(stream_key, 6)
    for position, parts in pieces:
        draws = jnp.exp(jax.random.uniform(jax.random.fold_in(own, position), (parts,), jnp.float32, low / len(pieces), top_value / len(pieces)))
        loudness = loudness * jnp.repeat(draws, dims[position] // parts).reshape([-1 if axis == position else 1 for axis in range(len(dims))])
    return loudness


def setup_inputs(seed: int = 0) -> dict:
    key_list = jax.random.split(jax.random.key(seed), 4)
    return {
        "f_pop": jnp.clip(0.02 + 0.08 * jax.random.uniform(key_list[0], (POPS, NX, NY, NZ), jnp.float32) ** steps_of(key_list[0], (POPS, NX, NY, NZ), ((1, 32), (2, 4), (3, 2)), -0.2, 0.2), 0.02, 0.1),
        "g_pop": jnp.clip(jax.random.uniform(key_list[1], (POPS, NX, NY, NZ), jnp.float32, -0.2, 0.2) * steps_of(key_list[1], (POPS, NX, NY, NZ), ((1, 32), (2, 4), (3, 2)), -0.4, 0.0), -0.2, 0.2),
        "displacement": jax.random.randint(key_list[2], (1,), NY // 2 + 1, NY // 2 + CY).astype(jnp.int32),
    }


VELOCITIES = [(0, 0, 0), (1, 0, 0), (1, 1, 0), (1, -1, 0), (1, 0, 1), (1, 0, -1),
              (-1, 0, 0), (-1, -1, 0), (-1, 1, 0), (-1, 0, -1), (-1, 0, 1),
              (0, 1, 0), (0, -1, 0), (0, 0, 1), (0, 0, -1), (0, 1, 1), (0, -1, -1), (0, 1, -1), (0, -1, 1)]
BULK_COEF = 0.5
STIFFNESS = 0.5
TAU_FLUID = 0.8
TAU_ORDER = 0.9


def lattice_weight(number):
    steps_sq = sum(abs(comp) for comp in VELOCITIES[number])
    if steps_sq == 0:
        return 1.0 / 3.0
    if steps_sq == 1:
        return 1.0 / 18.0
    return 1.0 / 36.0


def along(number, values, base):
    result = jnp.zeros_like(base)
    for axis_id in range(3):
        comp = VELOCITIES[number][axis_id]
        if comp != 0:
            result = result + comp * values[axis_id]
    return result


def collide(f_pop, g_pop, order_field, laplace, slopes):
    density = jnp.sum(f_pop, axis=0)
    chemical = BULK_COEF * (order_field * order_field * order_field - order_field) - STIFFNESS * laplace
    forces = [chemical * slope for slope in slopes]
    moments = []
    for axis_id in range(3):
        moment = jnp.zeros_like(density)
        for number in range(19):
            comp = VELOCITIES[number][axis_id]
            if comp != 0:
                moment = moment + comp * f_pop[number]
        moments.append(moment)
    flows = [(moments[axis_id] + 0.5 * forces[axis_id]) / density for axis_id in range(3)]
    speed_sq = flows[0] * flows[0] + flows[1] * flows[1] + flows[2] * flows[2]
    flow_force = flows[0] * forces[0] + flows[1] * forces[1] + flows[2] * forces[2]
    f_posts = []
    g_eqs = []
    for number in range(19):
        weight = lattice_weight(number)
        proj_flow = along(number, flows, density)
        proj_force = along(number, forces, density)
        shape_term = 3.0 * proj_flow + 4.5 * proj_flow * proj_flow - 1.5 * speed_sq
        f_eq = weight * density * (1.0 + shape_term)
        source = (1.0 - 0.5 / TAU_FLUID) * weight * (3.0 * (proj_force - flow_force) + 9.0 * proj_flow * proj_force)
        f_posts.append(f_pop[number] - (f_pop[number] - f_eq) / TAU_FLUID + source)
        g_eqs.append(weight * (3.0 * chemical + order_field * shape_term))
    rest_eq = order_field
    for number in range(1, 19):
        rest_eq = rest_eq - g_eqs[number]
    g_eqs[0] = rest_eq
    g_posts = [g_pop[number] - (g_pop[number] - g_eqs[number]) / TAU_ORDER for number in range(19)]
    return f_posts, g_posts


def stream(posts, shift, at_low, at_high):
    results = []
    for number in range(19):
        vel_x, vel_y, vel_z = VELOCITIES[number]
        plain = jnp.roll(posts[number], (vel_x, vel_y, vel_z), (0, 1, 2))
        if vel_x == 1:
            plain = jnp.where(at_low, jnp.roll(plain, shift, 1), plain)
        if vel_x == -1:
            plain = jnp.where(at_high, jnp.roll(plain, -shift, 1), plain)
        results.append(plain)
    return jnp.stack(results)


def reference(f_pop, g_pop, displacement):
    shift = displacement[0]
    order_field = jnp.sum(g_pop, axis=0)
    plane = jnp.arange(order_field.shape[0]) % CX
    at_low = (plane == 0)[:, None, None]
    at_high = (plane == CX - 1)[:, None, None]
    back_x = jnp.roll(order_field, 1, 0)
    neigh_xm = jnp.where(at_low, jnp.roll(back_x, shift, 1), back_x)
    fore_x = jnp.roll(order_field, -1, 0)
    neigh_xp = jnp.where(at_high, jnp.roll(fore_x, -shift, 1), fore_x)
    neigh_ym = jnp.roll(order_field, 1, 1)
    neigh_yp = jnp.roll(order_field, -1, 1)
    neigh_zm = jnp.roll(order_field, 1, 2)
    neigh_zp = jnp.roll(order_field, -1, 2)
    laplace = neigh_xm + neigh_xp + neigh_ym + neigh_yp + neigh_zm + neigh_zp - 6.0 * order_field
    slopes = [0.5 * (neigh_xp - neigh_xm), 0.5 * (neigh_yp - neigh_ym), 0.5 * (neigh_zp - neigh_zm)]
    f_posts, g_posts = collide(f_pop, g_pop, order_field, laplace, slopes)
    f_new = stream(f_posts, shift, at_low, at_high)
    g_new = stream(g_posts, shift, at_low, at_high)
    return f_new, g_new
```

```python
import jax
import jax.numpy as jnp
from jax import lax
from jax.sharding import PartitionSpec as P

VELOCITIES = [
    (0, 0, 0),
    (1, 0, 0),
    (1, 1, 0),
    (1, -1, 0),
    (1, 0, 1),
    (1, 0, -1),
    (-1, 0, 0),
    (-1, -1, 0),
    (-1, 1, 0),
    (-1, 0, -1),
    (-1, 0, 1),
    (0, 1, 0),
    (0, -1, 0),
    (0, 0, 1),
    (0, 0, -1),
    (0, 1, 1),
    (0, -1, -1),
    (0, 1, -1),
    (0, -1, 1),
]
BULK_COEF = 0.5
STIFFNESS = 0.5
TAU_FLUID = 0.8
TAU_ORDER = 0.9
SHIFT_MIN = 33
SHIFT_MAX = 47
AXES = ("gx", "gy", "gz")


def lattice_weight(number):
    steps_sq = sum((abs(comp) for comp in VELOCITIES[number]))
    if steps_sq == 0:
        return 1.0 / 3.0
    if steps_sq == 1:
        return 1.0 / 18.0
    return 1.0 / 36.0


def along(number, values, base):
    result = jnp.zeros_like(base)
    for axis_id in range(3):
        comp = VELOCITIES[number][axis_id]
        if comp != 0:
            result = result + comp * values[axis_id]
    return result


def collide(f_pop, g_pop, order_field, laplace, slopes):
    density = jnp.sum(f_pop, axis=0)
    chemical = (
        BULK_COEF * (order_field * order_field * order_field - order_field) - STIFFNESS * laplace
    )
    forces = [chemical * slope for slope in slopes]
    moments = []
    for axis_id in range(3):
        moment = jnp.zeros_like(density)
        for number in range(19):
            comp = VELOCITIES[number][axis_id]
            if comp != 0:
                moment = moment + comp * f_pop[number]
        moments.append(moment)
    flows = [(moments[axis_id] + 0.5 * forces[axis_id]) / density for axis_id in range(3)]
    speed_sq = flows[0] * flows[0] + flows[1] * flows[1] + flows[2] * flows[2]
    flow_force = flows[0] * forces[0] + flows[1] * forces[1] + flows[2] * forces[2]
    f_posts = []
    g_eqs = []
    for number in range(19):
        weight = lattice_weight(number)
        proj_flow = along(number, flows, density)
        proj_force = along(number, forces, density)
        shape_term = 3.0 * proj_flow + 4.5 * proj_flow * proj_flow - 1.5 * speed_sq
        f_eq = weight * density * (1.0 + shape_term)
        source = (
            (1.0 - 0.5 / TAU_FLUID)
            * weight
            * (3.0 * (proj_force - flow_force) + 9.0 * proj_flow * proj_force)
        )
        f_posts.append(f_pop[number] - (f_pop[number] - f_eq) / TAU_FLUID + source)
        g_eqs.append(weight * (3.0 * chemical + order_field * shape_term))
    rest_eq = order_field
    for number in range(1, 19):
        rest_eq = rest_eq - g_eqs[number]
    g_eqs[0] = rest_eq
    g_posts = [g_pop[number] - (g_pop[number] - g_eqs[number]) / TAU_ORDER for number in range(19)]
    return (jnp.stack(f_posts), jnp.stack(g_posts))


def exchange(sends):
    sizes = [lax.axis_size(a) for a in AXES]
    groups = {}
    order = []
    for index, (value, offset) in enumerate(sends):
        key = (tuple(o % n for o, n in zip(offset, sizes)), value.shape[1:])
        if key not in groups:
            groups[key] = []
            order.append(key)
        groups[key].append(index)
    results = [None] * len(sends)
    for key in order:
        members = groups[key]
        offset = key[0]
        pairs = []
        for i in range(sizes[0]):
            for j in range(sizes[1]):
                for k in range(sizes[2]):
                    src = (i * sizes[1] + j) * sizes[2] + k
                    ti, tj, tk = [(c + o) % n for c, o, n in zip((i, j, k), offset, sizes)]
                    pairs.append((src, (ti * sizes[1] + tj) * sizes[2] + tk))
        payload = [sends[m][0] for m in members]
        joined = payload[0] if len(payload) == 1 else jnp.concatenate(payload, axis=0)
        got = lax.ppermute(joined, AXES, pairs)
        start = 0
        for m in members:
            count = sends[m][0].shape[0]
            results[m] = got[start : start + count]
            start += count
    return results


def local(f_pop, g_pop, displacement):
    shift = displacement[0]
    nx, ny, nz = (f_pop.shape[1], f_pop.shape[2], f_pop.shape[3])
    q = SHIFT_MIN // ny
    assert SHIFT_MAX // ny == q and SHIFT_MIN % ny != 0
    rem = shift - q * ny

    phi = jnp.sum(g_pop, axis=0)
    pa, pb, pc, pd, pym, pyp, pzm, pzp = exchange(
        [
            (phi[-1:], (1, q + 1, 0)),
            (phi[-1:], (1, q, 0)),
            (phi[:1], (-1, -q, 0)),
            (phi[:1], (-1, -q - 1, 0)),
            (phi[:, -1:], (0, 1, 0)),
            (phi[:, :1], (0, -1, 0)),
            (jnp.transpose(phi[:, :, -1:], (2, 0, 1)), (0, 0, 1)),
            (jnp.transpose(phi[:, :, :1], (2, 0, 1)), (0, 0, -1)),
        ]
    )
    low = lax.dynamic_slice_in_dim(jnp.concatenate([pa, pb], axis=1), ny - rem, ny, 1)
    high = lax.dynamic_slice_in_dim(jnp.concatenate([pc, pd], axis=1), rem, ny, 1)
    neigh_xm = jnp.concatenate([low, phi[:-1]], axis=0)
    neigh_xp = jnp.concatenate([phi[1:], high], axis=0)
    neigh_ym = jnp.concatenate([pym, phi[:, :-1]], axis=1)
    neigh_yp = jnp.concatenate([phi[:, 1:], pyp], axis=1)
    neigh_zm = jnp.concatenate([jnp.transpose(pzm, (1, 2, 0)), phi[:, :, :-1]], axis=2)
    neigh_zp = jnp.concatenate([phi[:, :, 1:], jnp.transpose(pzp, (1, 2, 0))], axis=2)
    laplace = neigh_xm + neigh_xp + neigh_ym + neigh_yp + neigh_zm + neigh_zp - 6.0 * phi
    slopes = [0.5 * (neigh_xp - neigh_xm), 0.5 * (neigh_yp - neigh_ym), 0.5 * (neigh_zp - neigh_zm)]
    f_post, g_post = collide(f_pop, g_pop, phi, laplace, slopes)
    post = jnp.concatenate([f_post, g_post], axis=0)

    vel = [VELOCITIES[n % 19] for n in range(38)]

    def pick(cond):
        return [n for n in range(38) if cond(vel[n])]

    x_up = pick(lambda c: c[0] == 1)
    x_dn = pick(lambda c: c[0] == -1)
    y_up = pick(lambda c: c[1] == 1)
    y_dn = pick(lambda c: c[1] == -1)
    z_up = pick(lambda c: c[2] == 1)
    z_dn = pick(lambda c: c[2] == -1)
    xz = {(cx, cz): pick(lambda c, cx=cx, cz=cz: c[0] == cx and c[2] == cz) for cx in (1, -1) for cz in (1, -1)}
    yz = {(cy, cz): pick(lambda c, cy=cy, cz=cz: c[1] == cy and c[2] == cz) for cy in (1, -1) for cz in (1, -1)}

    def rows(idx):
        return jnp.stack([post[n] for n in idx])

    last_x = rows(x_up)[:, -1]
    first_x = rows(x_dn)[:, 0]
    sends = [
        (last_x, (1, q + 1, 0)),
        (last_x, (1, q, 0)),
        (first_x, (-1, -q, 0)),
        (first_x, (-1, -q - 1, 0)),
        (rows(y_up)[:, :, -1], (0, 1, 0)),
        (rows(y_dn)[:, :, 0], (0, -1, 0)),
        (rows(z_up)[:, :, :, -1], (0, 0, 1)),
        (rows(z_dn)[:, :, :, 0], (0, 0, -1)),
    ]
    xz_keys = []
    for (cx, cz), idx in xz.items():
        plane = rows(idx)[:, -1 if cx == 1 else 0, :, -1 if cz == 1 else 0]
        for dy in ((q + 1, q) if cx == 1 else (-q, -q - 1)):
            sends.append((plane, (cx, dy, cz)))
            xz_keys.append((cx, cz, dy))
    yz_keys = []
    for (cy, cz), idx in yz.items():
        line = rows(idx)[:, :, -1 if cy == 1 else 0, -1 if cz == 1 else 0]
        sends.append((line, (0, cy, cz)))
        yz_keys.append((cy, cz))
    got = exchange(sends)
    xa, xb, xc, xd, hy_m, hy_p, hz_m, hz_p = got[:8]
    xz_got = dict(zip(xz_keys, got[8 : 8 + len(xz_keys)]))
    yz_got = dict(zip(yz_keys, got[8 + len(xz_keys) :]))

    win_low = lax.dynamic_slice_in_dim(jnp.concatenate([xa, xb], axis=1), ny - rem - 1, ny + 2, 1)
    win_high = lax.dynamic_slice_in_dim(jnp.concatenate([xc, xd], axis=1), rem - 1, ny + 2, 1)
    xz_win = {}
    for (cx, cz) in xz:
        if cx == 1:
            both = jnp.concatenate([xz_got[(cx, cz, q + 1)], xz_got[(cx, cz, q)]], axis=1)
            xz_win[(cx, cz)] = lax.dynamic_slice_in_dim(both, ny - rem, ny, 1)
        else:
            both = jnp.concatenate([xz_got[(cx, cz, -q)], xz_got[(cx, cz, -q - 1)]], axis=1)
            xz_win[(cx, cz)] = lax.dynamic_slice_in_dim(both, rem, ny, 1)

    def shift_yz(t, cy, cz, ym, yp, zm, zp, corner):
        if cz == 1:
            t = jnp.concatenate([zm, t[:, :, :-1]], axis=2)
        elif cz == -1:
            t = jnp.concatenate([t[:, :, 1:], zp], axis=2)
        if cy != 0:
            edge = ym if cy == 1 else yp
            if cz == 1:
                edge = jnp.concatenate([corner, edge[:, :, :-1]], axis=2)
            elif cz == -1:
                edge = jnp.concatenate([edge[:, :, 1:], corner], axis=2)
            if cy == 1:
                t = jnp.concatenate([edge, t[:, :-1]], axis=1)
            else:
                t = jnp.concatenate([t[:, 1:], edge], axis=1)
        return t

    results = []
    for n in range(38):
        cx, cy, cz = vel[n]
        ym = yp = zm = zp = corner = None
        if cy == 1:
            ym = hy_m[y_up.index(n)][:, None, :]
        if cy == -1:
            yp = hy_p[y_dn.index(n)][:, None, :]
        if cz == 1:
            zm = hz_m[z_up.index(n)][:, :, None]
        if cz == -1:
            zp = hz_p[z_dn.index(n)][:, :, None]
        if cy != 0 and cz != 0:
            corner = yz_got[(cy, cz)][yz[(cy, cz)].index(n)][:, None, None]
        if cx == 0:
            results.append(shift_yz(post[n], cy, cz, ym, yp, zm, zp, corner))
            continue
        sl = slice(0, nx - 1) if cx == 1 else slice(1, nx)
        inner = shift_yz(
            post[n][sl],
            cy,
            cz,
            None if ym is None else ym[sl],
            None if yp is None else yp[sl],
            None if zm is None else zm[sl],
            None if zp is None else zp[sl],
            corner,
        )
        if cx == 1:
            win = win_low[x_up.index(n)]
        else:
            win = win_high[x_dn.index(n)]
        plane = win[1 - cy : 1 - cy + ny]
        if cz == 1:
            col = xz_win[(cx, cz)][xz[(cx, cz)].index(n)]
            plane = jnp.concatenate([col[:, None], plane[:, :-1]], axis=1)
        elif cz == -1:
            col = xz_win[(cx, cz)][xz[(cx, cz)].index(n)]
            plane = jnp.concatenate([plane[:, 1:], col[:, None]], axis=1)
        if cx == 1:
            results.append(jnp.concatenate([plane[None], inner], axis=0))
        else:
            results.append(jnp.concatenate([inner, plane[None]], axis=0))
    f_new = jnp.stack(results[:19])
    g_new = jnp.stack(results[19:])
    return (f_new, g_new)


def solution(mesh):
    return jax.shard_map(
        local,
        mesh=mesh,
        in_specs=(P(None, "gx", "gy", "gz"), P(None, "gx", "gy", "gz"), P()),
        out_specs=(P(None, "gx", "gy", "gz"), P(None, "gx", "gy", "gz")),
        check_vma=False,
    )
```

```python
import jax
import jax.numpy as jnp
from jax import lax
from jax.sharding import PartitionSpec as P

VELOCITIES = [
    (0, 0, 0),
    (1, 0, 0),
    (1, 1, 0),
    (1, -1, 0),
    (1, 0, 1),
    (1, 0, -1),
    (-1, 0, 0),
    (-1, -1, 0),
    (-1, 1, 0),
    (-1, 0, -1),
    (-1, 0, 1),
    (0, 1, 0),
    (0, -1, 0),
    (0, 0, 1),
    (0, 0, -1),
    (0, 1, 1),
    (0, -1, -1),
    (0, 1, -1),
    (0, -1, 1),
]
BULK_COEF = 0.5
STIFFNESS = 0.5
TAU_FLUID = 0.8
TAU_ORDER = 0.9
SHIFT_MIN = 33
SHIFT_MAX = 47
AXES = ("gx", "gy", "gz")


def lattice_weight(number):
    steps_sq = sum((abs(comp) for comp in VELOCITIES[number]))
    if steps_sq == 0:
        return 1.0 / 3.0
    if steps_sq == 1:
        return 1.0 / 18.0
    return 1.0 / 36.0


def along(number, values, base):
    result = jnp.zeros_like(base)
    for axis_id in range(3):
        comp = VELOCITIES[number][axis_id]
        if comp != 0:
            result = result + comp * values[axis_id]
    return result


def collide(f_pop, g_pop, order_field, laplace, slopes):
    density = jnp.sum(f_pop, axis=0)
    chemical = (
        BULK_COEF * (order_field * order_field * order_field - order_field) - STIFFNESS * laplace
    )
    forces = [chemical * slope for slope in slopes]
    moments = []
    for axis_id in range(3):
        moment = jnp.zeros_like(density)
        for number in range(19):
            comp = VELOCITIES[number][axis_id]
            if comp != 0:
                moment = moment + comp * f_pop[number]
        moments.append(moment)
    flows = [(moments[axis_id] + 0.5 * forces[axis_id]) / density for axis_id in range(3)]
    speed_sq = flows[0] * flows[0] + flows[1] * flows[1] + flows[2] * flows[2]
    flow_force = flows[0] * forces[0] + flows[1] * forces[1] + flows[2] * forces[2]
    f_posts = []
    g_eqs = []
    for number in range(19):
        weight = lattice_weight(number)
        proj_flow = along(number, flows, density)
        proj_force = along(number, forces, density)
        shape_term = 3.0 * proj_flow + 4.5 * proj_flow * proj_flow - 1.5 * speed_sq
        f_eq = weight * density * (1.0 + shape_term)
        source = (
            (1.0 - 0.5 / TAU_FLUID)
            * weight
            * (3.0 * (proj_force - flow_force) + 9.0 * proj_flow * proj_force)
        )
        f_posts.append(f_pop[number] - (f_pop[number] - f_eq) / TAU_FLUID + source)
        g_eqs.append(weight * (3.0 * chemical + order_field * shape_term))
    rest_eq = order_field
    for number in range(1, 19):
        rest_eq = rest_eq - g_eqs[number]
    g_eqs[0] = rest_eq
    g_posts = [g_pop[number] - (g_pop[number] - g_eqs[number]) / TAU_ORDER for number in range(19)]
    return (jnp.stack(f_posts), jnp.stack(g_posts))


def exchange(sends):
    sizes = [lax.axis_size(a) for a in AXES]
    groups = {}
    order = []
    for index, (value, offset) in enumerate(sends):
        key = (tuple(o % n for o, n in zip(offset, sizes)), value.shape[1:])
        if key not in groups:
            groups[key] = []
            order.append(key)
        groups[key].append(index)
    results = [None] * len(sends)
    for key in order:
        members = groups[key]
        offset = key[0]
        pairs = []
        for i in range(sizes[0]):
            for j in range(sizes[1]):
                for k in range(sizes[2]):
                    src = (i * sizes[1] + j) * sizes[2] + k
                    ti, tj, tk = [(c + o) % n for c, o, n in zip((i, j, k), offset, sizes)]
                    pairs.append((src, (ti * sizes[1] + tj) * sizes[2] + tk))
        payload = [sends[m][0] for m in members]
        joined = payload[0] if len(payload) == 1 else jnp.concatenate(payload, axis=0)
        got = lax.ppermute(joined, AXES, pairs)
        start = 0
        for m in members:
            count = sends[m][0].shape[0]
            results[m] = got[start : start + count]
            start += count
    return results


def local(f_pop, g_pop, displacement):
    shift = displacement[0]
    nx, ny, nz = (f_pop.shape[1], f_pop.shape[2], f_pop.shape[3])
    q = SHIFT_MIN // ny
    assert SHIFT_MAX // ny == q and SHIFT_MIN % ny != 0
    rem = shift - q * ny

    phi = jnp.sum(g_pop, axis=0)
    pa, pb, pc, pd, pym, pyp, pzm, pzp = exchange(
        [
            (phi[-1:], (1, q + 1, 0)),
            (phi[-1:], (1, q, 0)),
            (phi[:1], (-1, -q, 0)),
            (phi[:1], (-1, -q - 1, 0)),
            (phi[:, -1:], (0, 1, 0)),
            (phi[:, :1], (0, -1, 0)),
            (jnp.transpose(phi[:, :, -1:], (2, 0, 1)), (0, 0, 1)),
            (jnp.transpose(phi[:, :, :1], (2, 0, 1)), (0, 0, -1)),
        ]
    )
    low = lax.dynamic_slice_in_dim(jnp.concatenate([pa, pb], axis=1), ny - rem, ny, 1)
    high = lax.dynamic_slice_in_dim(jnp.concatenate([pc, pd], axis=1), rem, ny, 1)
    neigh_xm = jnp.concatenate([low, phi[:-1]], axis=0)
    neigh_xp = jnp.concatenate([phi[1:], high], axis=0)
    neigh_ym = jnp.concatenate([pym, phi[:, :-1]], axis=1)
    neigh_yp = jnp.concatenate([phi[:, 1:], pyp], axis=1)
    neigh_zm = jnp.concatenate([jnp.transpose(pzm, (1, 2, 0)), phi[:, :, :-1]], axis=2)
    neigh_zp = jnp.concatenate([phi[:, :, 1:], jnp.transpose(pzp, (1, 2, 0))], axis=2)
    laplace = neigh_xm + neigh_xp + neigh_ym + neigh_yp + neigh_zm + neigh_zp - 6.0 * phi
    slopes = [0.5 * (neigh_xp - neigh_xm), 0.5 * (neigh_yp - neigh_ym), 0.5 * (neigh_zp - neigh_zm)]
    f_post, g_post = collide(f_pop, g_pop, phi, laplace, slopes)
    post = jnp.concatenate([f_post, g_post], axis=0)

    vel = [VELOCITIES[n % 19] for n in range(38)]

    def pick(cond, among=range(38)):
        return [n for n in among if cond(vel[n])]

    x_up = pick(lambda c: c[0] == 1)
    x_dn = pick(lambda c: c[0] == -1)
    y_up = pick(lambda c: c[1] == 1)
    y_dn = pick(lambda c: c[1] == -1)
    z_up = pick(lambda c: c[2] == 1)
    z_dn = pick(lambda c: c[2] == -1)
    xz_up = pick(lambda c: c[2] != 0, x_up)
    xz_dn = pick(lambda c: c[2] != 0, x_dn)
    yz_up = pick(lambda c: c[2] != 0, y_up)
    yz_dn = pick(lambda c: c[2] != 0, y_dn)

    def rows(idx):
        return jnp.stack([post[n] for n in idx])

    hz_m, hz_p = exchange(
        [(rows(z_up)[:, :, :, -1], (0, 0, 1)), (rows(z_dn)[:, :, :, 0], (0, 0, -1))]
    )

    def zhalo(n):
        return hz_m[z_up.index(n)] if vel[n][2] == 1 else hz_p[z_dn.index(n)]

    def lanes(a):
        return jnp.pad(a, ((0, 0), (0, nz - a.shape[1])))

    def packed(face, extra):
        return jnp.concatenate([face.reshape(-1, nz), lanes(jnp.stack(extra))], axis=0)

    send_up = packed(rows(x_up)[:, -1], [zhalo(n)[-1] for n in xz_up])
    send_dn = packed(rows(x_dn)[:, 0], [zhalo(n)[0] for n in xz_dn])
    send_yu = packed(rows(y_up)[:, :, -1], [zhalo(n)[:, -1] for n in yz_up])
    send_yd = packed(rows(y_dn)[:, :, 0], [zhalo(n)[:, 0] for n in yz_dn])
    xa, xb, xc, xd, hy_m, hy_p = exchange(
        [
            (send_up, (1, q + 1, 0)),
            (send_up, (1, q, 0)),
            (send_dn, (-1, -q, 0)),
            (send_dn, (-1, -q - 1, 0)),
            (send_yu, (0, 1, 0)),
            (send_yd, (0, -1, 0)),
        ]
    )

    def unpack_x(got, count):
        return got[: count * ny].reshape(count, ny, nz), got[count * ny :, :ny]

    def unpack_y(got, count):
        return got[: count * nx].reshape(count, nx, nz), got[count * nx :, :nx]

    pa2, ca = unpack_x(xa, len(x_up))
    pb2, cb = unpack_x(xb, len(x_up))
    pc2, cc = unpack_x(xc, len(x_dn))
    pd2, cd = unpack_x(xd, len(x_dn))
    hy_m, cy_m = unpack_y(hy_m, len(y_up))
    hy_p, cy_p = unpack_y(hy_p, len(y_dn))
    win_low = lax.dynamic_slice_in_dim(jnp.concatenate([pa2, pb2], axis=1), ny - rem - 1, ny + 2, 1)
    win_high = lax.dynamic_slice_in_dim(jnp.concatenate([pc2, pd2], axis=1), rem - 1, ny + 2, 1)
    xzw_low = lax.dynamic_slice_in_dim(jnp.concatenate([ca, cb], axis=1), ny - rem, ny, 1)
    xzw_high = lax.dynamic_slice_in_dim(jnp.concatenate([cc, cd], axis=1), rem, ny, 1)

    def shift_yz(t, cy, cz, ym, yp, zm, zp, corner):
        if cz == 1:
            t = jnp.concatenate([zm, t[:, :, :-1]], axis=2)
        elif cz == -1:
            t = jnp.concatenate([t[:, :, 1:], zp], axis=2)
        if cy != 0:
            edge = ym if cy == 1 else yp
            if cz == 1:
                edge = jnp.concatenate([corner, edge[:, :, :-1]], axis=2)
            elif cz == -1:
                edge = jnp.concatenate([edge[:, :, 1:], corner], axis=2)
            if cy == 1:
                t = jnp.concatenate([edge, t[:, :-1]], axis=1)
            else:
                t = jnp.concatenate([t[:, 1:], edge], axis=1)
        return t

    results = []
    for n in range(38):
        cx, cy, cz = vel[n]
        ym = yp = zm = zp = corner = None
        if cy == 1:
            ym = hy_m[y_up.index(n)][:, None, :]
        if cy == -1:
            yp = hy_p[y_dn.index(n)][:, None, :]
        if cz == 1:
            zm = hz_m[z_up.index(n)][:, :, None]
        if cz == -1:
            zp = hz_p[z_dn.index(n)][:, :, None]
        if cy == 1 and cz != 0:
            corner = cy_m[yz_up.index(n)][:, None, None]
        if cy == -1 and cz != 0:
            corner = cy_p[yz_dn.index(n)][:, None, None]
        if cx == 0:
            results.append(shift_yz(post[n], cy, cz, ym, yp, zm, zp, corner))
            continue
        sl = slice(0, nx - 1) if cx == 1 else slice(1, nx)
        inner = shift_yz(
            post[n][sl],
            cy,
            cz,
            None if ym is None else ym[sl],
            None if yp is None else yp[sl],
            None if zm is None else zm[sl],
            None if zp is None else zp[sl],
            corner,
        )
        if cx == 1:
            win = win_low[x_up.index(n)]
        else:
            win = win_high[x_dn.index(n)]
        plane = win[1 - cy : 1 - cy + ny]
        if cz != 0:
            col = xzw_low[xz_up.index(n)] if cx == 1 else xzw_high[xz_dn.index(n)]
        if cz == 1:
            plane = jnp.concatenate([col[:, None], plane[:, :-1]], axis=1)
        elif cz == -1:
            plane = jnp.concatenate([plane[:, 1:], col[:, None]], axis=1)
        if cx == 1:
            results.append(jnp.concatenate([plane[None], inner], axis=0))
        else:
            results.append(jnp.concatenate([inner, plane[None]], axis=0))
    f_new = jnp.stack(results[:19])
    g_new = jnp.stack(results[19:])
    return (f_new, g_new)


def solution(mesh):
    return jax.shard_map(
        local,
        mesh=mesh,
        in_specs=(P(None, "gx", "gy", "gz"), P(None, "gx", "gy", "gz"), P()),
        out_specs=(P(None, "gx", "gy", "gz"), P(None, "gx", "gy", "gz")),
        check_vma=False,
    )
```

```python
import jax
import jax.numpy as jnp
from jax import lax
from jax.sharding import PartitionSpec as P
from jax.experimental import pallas as pl
from jax.experimental.pallas import tpu as pltpu

VELOCITIES = [
    (0, 0, 0),
    (1, 0, 0),
    (1, 1, 0),
    (1, -1, 0),
    (1, 0, 1),
    (1, 0, -1),
    (-1, 0, 0),
    (-1, -1, 0),
    (-1, 1, 0),
    (-1, 0, -1),
    (-1, 0, 1),
    (0, 1, 0),
    (0, -1, 0),
    (0, 0, 1),
    (0, 0, -1),
    (0, 1, 1),
    (0, -1, -1),
    (0, 1, -1),
    (0, -1, 1),
]
BULK_COEF = 0.5
STIFFNESS = 0.5
TAU_FLUID = 0.8
TAU_ORDER = 0.9
SHIFT_MIN = 33
SHIFT_MAX = 47
AXES = ("gx", "gy", "gz")
INTERPRET = False


def lattice_weight(number):
    steps_sq = sum((abs(comp) for comp in VELOCITIES[number]))
    if steps_sq == 0:
        return 1.0 / 3.0
    if steps_sq == 1:
        return 1.0 / 18.0
    return 1.0 / 36.0


def along(number, values, base):
    result = jnp.zeros_like(base)
    for axis_id in range(3):
        comp = VELOCITIES[number][axis_id]
        if comp != 0:
            result = result + comp * values[axis_id]
    return result


def collide(f_pop, g_pop, order_field, laplace, slopes):
    density = jnp.sum(f_pop, axis=0)
    chemical = (
        BULK_COEF * (order_field * order_field * order_field - order_field) - STIFFNESS * laplace
    )
    forces = [chemical * slope for slope in slopes]
    moments = []
    for axis_id in range(3):
        moment = jnp.zeros_like(density)
        for number in range(19):
            comp = VELOCITIES[number][axis_id]
            if comp != 0:
                moment = moment + comp * f_pop[number]
        moments.append(moment)
    flows = [(moments[axis_id] + 0.5 * forces[axis_id]) / density for axis_id in range(3)]
    speed_sq = flows[0] * flows[0] + flows[1] * flows[1] + flows[2] * flows[2]
    flow_force = flows[0] * forces[0] + flows[1] * forces[1] + flows[2] * forces[2]
    f_posts = []
    g_eqs = []
    for number in range(19):
        weight = lattice_weight(number)
        proj_flow = along(number, flows, density)
        proj_force = along(number, forces, density)
        shape_term = 3.0 * proj_flow + 4.5 * proj_flow * proj_flow - 1.5 * speed_sq
        f_eq = weight * density * (1.0 + shape_term)
        source = (
            (1.0 - 0.5 / TAU_FLUID)
            * weight
            * (3.0 * (proj_force - flow_force) + 9.0 * proj_flow * proj_force)
        )
        f_posts.append(f_pop[number] - (f_pop[number] - f_eq) / TAU_FLUID + source)
        g_eqs.append(weight * (3.0 * chemical + order_field * shape_term))
    rest_eq = order_field
    for number in range(1, 19):
        rest_eq = rest_eq - g_eqs[number]
    g_eqs[0] = rest_eq
    g_posts = [g_pop[number] - (g_pop[number] - g_eqs[number]) / TAU_ORDER for number in range(19)]
    return (jnp.stack(f_posts), jnp.stack(g_posts))


def collide_lists(f_pop, g_pop, order_field, laplace, slopes):
    density = f_pop[0]
    for number in range(1, 19):
        density = density + f_pop[number]
    chemical = (
        BULK_COEF * (order_field * order_field * order_field - order_field) - STIFFNESS * laplace
    )
    forces = [chemical * slope for slope in slopes]
    moments = []
    for axis_id in range(3):
        moment = jnp.zeros_like(density)
        for number in range(19):
            comp = VELOCITIES[number][axis_id]
            if comp != 0:
                moment = moment + comp * f_pop[number]
        moments.append(moment)
    flows = [(moments[axis_id] + 0.5 * forces[axis_id]) / density for axis_id in range(3)]
    speed_sq = flows[0] * flows[0] + flows[1] * flows[1] + flows[2] * flows[2]
    flow_force = flows[0] * forces[0] + flows[1] * forces[1] + flows[2] * forces[2]
    f_posts = []
    g_eqs = []
    for number in range(19):
        weight = lattice_weight(number)
        proj_flow = along(number, flows, density)
        proj_force = along(number, forces, density)
        shape_term = 3.0 * proj_flow + 4.5 * proj_flow * proj_flow - 1.5 * speed_sq
        f_eq = weight * density * (1.0 + shape_term)
        source = (
            (1.0 - 0.5 / TAU_FLUID)
            * weight
            * (3.0 * (proj_force - flow_force) + 9.0 * proj_flow * proj_force)
        )
        f_posts.append(f_pop[number] - (f_pop[number] - f_eq) / TAU_FLUID + source)
        g_eqs.append(weight * (3.0 * chemical + order_field * shape_term))
    rest_eq = order_field
    for number in range(1, 19):
        rest_eq = rest_eq - g_eqs[number]
    g_eqs[0] = rest_eq
    g_posts = [g_pop[number] - (g_pop[number] - g_eqs[number]) / TAU_ORDER for number in range(19)]
    return (f_posts, g_posts)


def collide_kernel(f_ref, g_ref, nb_ref, post_ref):
    pops = f_ref.shape[0]
    for x in range(f_ref.shape[1]):
        f_planes = [f_ref[n, x] for n in range(pops)]
        g_planes = [g_ref[n, x] for n in range(pops)]
        slopes = [nb_ref[2 + a, x] for a in range(3)]
        f_posts, g_posts = collide_lists(f_planes, g_planes, nb_ref[0, x], nb_ref[1, x], slopes)
        for n in range(pops):
            post_ref[n, x] = f_posts[n]
            post_ref[pops + n, x] = g_posts[n]


def stream_kernel(post_ref, xlow_ref, xhigh_ref, hym_ref, hyp_ref, col_ref, f_ref, g_ref):
    pops = f_ref.shape[0]
    nx, ny, nz = f_ref.shape[1:]
    row = lax.broadcasted_iota(jnp.int32, (ny, nz), 0)
    lane = lax.broadcasted_iota(jnp.int32, (ny, nz), 1)
    vel = [VELOCITIES[n % pops] for n in range(2 * pops)]
    x_up = [n for n in range(2 * pops) if vel[n][0] == 1]
    x_dn = [n for n in range(2 * pops) if vel[n][0] == -1]
    y_up = [n for n in range(2 * pops) if vel[n][1] == 1]
    y_dn = [n for n in range(2 * pops) if vel[n][1] == -1]
    z_any = [n for n in range(2 * pops) if vel[n][2] != 0]
    for n in range(2 * pops):
        cx, cy, cz = vel[n]
        out = f_ref if n < pops else g_ref
        for x in range(nx):
            src = x - cx
            if src < 0:
                tile = xlow_ref[x_up.index(n)]
            elif src >= nx:
                tile = xhigh_ref[x_dn.index(n)]
            else:
                tile = post_ref[n, src]
                if cy == 1:
                    edge = jnp.broadcast_to(hym_ref[y_up.index(n), pl.ds(src, 1), :], (ny, nz))
                    tile = jnp.where(row == 0, edge, pltpu.roll(tile, 1, 0))
                elif cy == -1:
                    edge = jnp.broadcast_to(hyp_ref[y_dn.index(n), pl.ds(src, 1), :], (ny, nz))
                    tile = jnp.where(row == ny - 1, edge, pltpu.roll(tile, ny - 1, 0))
            if cz == 1:
                tile = jnp.where(lane == 0, col_ref[z_any.index(n), x], pltpu.roll(tile, 1, 1))
            elif cz == -1:
                tile = jnp.where(lane == nz - 1, col_ref[z_any.index(n), x], pltpu.roll(tile, nz - 1, 1))
            out[n % pops, x] = tile


def exchange(sends):
    sizes = [lax.axis_size(a) for a in AXES]
    groups = {}
    order = []
    for index, (value, offset) in enumerate(sends):
        key = (tuple(o % n for o, n in zip(offset, sizes)), value.shape[1:])
        if key not in groups:
            groups[key] = []
            order.append(key)
        groups[key].append(index)
    results = [None] * len(sends)
    for key in order:
        members = groups[key]
        offset = key[0]
        pairs = []
        for i in range(sizes[0]):
            for j in range(sizes[1]):
                for k in range(sizes[2]):
                    src = (i * sizes[1] + j) * sizes[2] + k
                    ti, tj, tk = [(c + o) % n for c, o, n in zip((i, j, k), offset, sizes)]
                    pairs.append((src, (ti * sizes[1] + tj) * sizes[2] + tk))
        payload = [sends[m][0] for m in members]
        joined = payload[0] if len(payload) == 1 else jnp.concatenate(payload, axis=0)
        got = lax.ppermute(joined, AXES, pairs)
        start = 0
        for m in members:
            count = sends[m][0].shape[0]
            results[m] = got[start : start + count]
            start += count
    return results


def local(f_pop, g_pop, displacement):
    shift = displacement[0]
    nx, ny, nz = (f_pop.shape[1], f_pop.shape[2], f_pop.shape[3])
    q = SHIFT_MIN // ny
    assert SHIFT_MAX // ny == q and SHIFT_MIN % ny != 0
    rem = shift - q * ny

    phi = jnp.sum(g_pop, axis=0)
    pa, pb, pc, pd, pym, pyp, pzm, pzp = exchange(
        [
            (phi[-1:], (1, q + 1, 0)),
            (phi[-1:], (1, q, 0)),
            (phi[:1], (-1, -q, 0)),
            (phi[:1], (-1, -q - 1, 0)),
            (phi[:, -1:], (0, 1, 0)),
            (phi[:, :1], (0, -1, 0)),
            (jnp.transpose(phi[:, :, -1:], (2, 0, 1)), (0, 0, 1)),
            (jnp.transpose(phi[:, :, :1], (2, 0, 1)), (0, 0, -1)),
        ]
    )
    low = lax.dynamic_slice_in_dim(jnp.concatenate([pa, pb], axis=1), ny - rem, ny, 1)
    high = lax.dynamic_slice_in_dim(jnp.concatenate([pc, pd], axis=1), rem, ny, 1)
    neigh_xm = jnp.concatenate([low, phi[:-1]], axis=0)
    neigh_xp = jnp.concatenate([phi[1:], high], axis=0)
    neigh_ym = jnp.concatenate([pym, phi[:, :-1]], axis=1)
    neigh_yp = jnp.concatenate([phi[:, 1:], pyp], axis=1)
    neigh_zm = jnp.concatenate([jnp.transpose(pzm, (1, 2, 0)), phi[:, :, :-1]], axis=2)
    neigh_zp = jnp.concatenate([phi[:, :, 1:], jnp.transpose(pzp, (1, 2, 0))], axis=2)
    laplace = neigh_xm + neigh_xp + neigh_ym + neigh_yp + neigh_zm + neigh_zp - 6.0 * phi
    slopes = [0.5 * (neigh_xp - neigh_xm), 0.5 * (neigh_yp - neigh_ym), 0.5 * (neigh_zp - neigh_zm)]
    nb = jnp.stack([phi, laplace] + slopes)
    post = pl.pallas_call(
        collide_kernel,
        out_shape=jax.ShapeDtypeStruct((2 * f_pop.shape[0], nx, ny, nz), jnp.float32),
        interpret=INTERPRET,
    )(f_pop, g_pop, nb)

    vel = [VELOCITIES[n % 19] for n in range(38)]

    def pick(cond, among=range(38)):
        return [n for n in among if cond(vel[n])]

    x_up = pick(lambda c: c[0] == 1)
    x_dn = pick(lambda c: c[0] == -1)
    y_up = pick(lambda c: c[1] == 1)
    y_dn = pick(lambda c: c[1] == -1)
    z_up = pick(lambda c: c[2] == 1)
    z_dn = pick(lambda c: c[2] == -1)
    xz_up = pick(lambda c: c[2] != 0, x_up)
    xz_dn = pick(lambda c: c[2] != 0, x_dn)
    yz_up = pick(lambda c: c[2] != 0, y_up)
    yz_dn = pick(lambda c: c[2] != 0, y_dn)

    def rows(idx):
        return jnp.stack([post[n] for n in idx])

    hz_m, hz_p = exchange(
        [(rows(z_up)[:, :, :, -1], (0, 0, 1)), (rows(z_dn)[:, :, :, 0], (0, 0, -1))]
    )

    def zhalo(n):
        return hz_m[z_up.index(n)] if vel[n][2] == 1 else hz_p[z_dn.index(n)]

    def lanes(a):
        return jnp.pad(a, ((0, 0), (0, nz - a.shape[1])))

    def packed(face, extra):
        return jnp.concatenate([face.reshape(-1, nz), lanes(jnp.stack(extra))], axis=0)

    send_up = packed(rows(x_up)[:, -1], [zhalo(n)[-1] for n in xz_up])
    send_dn = packed(rows(x_dn)[:, 0], [zhalo(n)[0] for n in xz_dn])
    send_yu = packed(rows(y_up)[:, :, -1], [zhalo(n)[:, -1] for n in yz_up])
    send_yd = packed(rows(y_dn)[:, :, 0], [zhalo(n)[:, 0] for n in yz_dn])
    xa, xb, xc, xd, hy_m, hy_p = exchange(
        [
            (send_up, (1, q + 1, 0)),
            (send_up, (1, q, 0)),
            (send_dn, (-1, -q, 0)),
            (send_dn, (-1, -q - 1, 0)),
            (send_yu, (0, 1, 0)),
            (send_yd, (0, -1, 0)),
        ]
    )

    def unpack_x(got, count):
        return got[: count * ny].reshape(count, ny, nz), got[count * ny :, :ny]

    def unpack_y(got, count):
        return got[: count * nx].reshape(count, nx, nz), got[count * nx :, :nx]

    pa2, ca = unpack_x(xa, len(x_up))
    pb2, cb = unpack_x(xb, len(x_up))
    pc2, cc = unpack_x(xc, len(x_dn))
    pd2, cd = unpack_x(xd, len(x_dn))
    hy_m, cy_m = unpack_y(hy_m, len(y_up))
    hy_p, cy_p = unpack_y(hy_p, len(y_dn))
    win_low = lax.dynamic_slice_in_dim(jnp.concatenate([pa2, pb2], axis=1), ny - rem - 1, ny + 2, 1)
    win_high = lax.dynamic_slice_in_dim(jnp.concatenate([pc2, pd2], axis=1), rem - 1, ny + 2, 1)
    xzw_low = lax.dynamic_slice_in_dim(jnp.concatenate([ca, cb], axis=1), ny - rem, ny, 1)
    xzw_high = lax.dynamic_slice_in_dim(jnp.concatenate([cc, cd], axis=1), rem, ny, 1)

    xlow = jnp.stack([win_low[a, 1 - vel[n][1] : 1 - vel[n][1] + ny] for a, n in enumerate(x_up)])
    xhigh = jnp.stack([win_high[a, 1 - vel[n][1] : 1 - vel[n][1] + ny] for a, n in enumerate(x_dn)])
    z_any = pick(lambda c: c[2] != 0)
    cols = []
    for n in z_any:
        cx, cy, cz = vel[n]
        per_x = []
        for x in range(nx):
            src_x = x - cx
            if src_x < 0:
                per_x.append(xzw_low[xz_up.index(n)])
                continue
            if src_x >= nx:
                per_x.append(xzw_high[xz_dn.index(n)])
                continue
            line = zhalo(n)[src_x]
            if cy == 1:
                line = jnp.concatenate([cy_m[yz_up.index(n), src_x : src_x + 1], line[:-1]])
            elif cy == -1:
                line = jnp.concatenate([line[1:], cy_p[yz_dn.index(n), src_x : src_x + 1]])
            per_x.append(line)
        cols.append(jnp.stack(per_x))
    cols = jnp.broadcast_to(jnp.stack(cols)[:, :, :, None], (len(z_any), nx, ny, nz))
    pops = f_pop.shape[0]
    f_new, g_new = pl.pallas_call(
        stream_kernel,
        out_shape=(
            jax.ShapeDtypeStruct((pops, nx, ny, nz), jnp.float32),
            jax.ShapeDtypeStruct((pops, nx, ny, nz), jnp.float32),
        ),
        interpret=INTERPRET,
    )(post, xlow, xhigh, hy_m, hy_p, cols)
    return (f_new, g_new)


def solution(mesh):
    return jax.shard_map(
        local,
        mesh=mesh,
        in_specs=(P(None, "gx", "gy", "gz"), P(None, "gx", "gy", "gz"), P()),
        out_specs=(P(None, "gx", "gy", "gz"), P(None, "gx", "gy", "gz")),
        check_vma=False,
    )
```

```python
import jax
import jax.numpy as jnp
from jax import lax
from jax.sharding import PartitionSpec as P
from jax.experimental import pallas as pl
from jax.experimental.pallas import tpu as pltpu

VELOCITIES = [
    (0, 0, 0),
    (1, 0, 0),
    (1, 1, 0),
    (1, -1, 0),
    (1, 0, 1),
    (1, 0, -1),
    (-1, 0, 0),
    (-1, -1, 0),
    (-1, 1, 0),
    (-1, 0, -1),
    (-1, 0, 1),
    (0, 1, 0),
    (0, -1, 0),
    (0, 0, 1),
    (0, 0, -1),
    (0, 1, 1),
    (0, -1, -1),
    (0, 1, -1),
    (0, -1, 1),
]
BULK_COEF = 0.5
STIFFNESS = 0.5
TAU_FLUID = 0.8
TAU_ORDER = 0.9
SHIFT_MIN = 33
SHIFT_MAX = 47
AXES = ("gx", "gy", "gz")
INTERPRET = False


def lattice_weight(number):
    steps_sq = sum((abs(comp) for comp in VELOCITIES[number]))
    if steps_sq == 0:
        return 1.0 / 3.0
    if steps_sq == 1:
        return 1.0 / 18.0
    return 1.0 / 36.0


def along(number, values, base):
    result = jnp.zeros_like(base)
    for axis_id in range(3):
        comp = VELOCITIES[number][axis_id]
        if comp != 0:
            result = result + comp * values[axis_id]
    return result


def collide(f_pop, g_pop, order_field, laplace, slopes):
    density = jnp.sum(f_pop, axis=0)
    chemical = (
        BULK_COEF * (order_field * order_field * order_field - order_field) - STIFFNESS * laplace
    )
    forces = [chemical * slope for slope in slopes]
    moments = []
    for axis_id in range(3):
        moment = jnp.zeros_like(density)
        for number in range(19):
            comp = VELOCITIES[number][axis_id]
            if comp != 0:
                moment = moment + comp * f_pop[number]
        moments.append(moment)
    flows = [(moments[axis_id] + 0.5 * forces[axis_id]) / density for axis_id in range(3)]
    speed_sq = flows[0] * flows[0] + flows[1] * flows[1] + flows[2] * flows[2]
    flow_force = flows[0] * forces[0] + flows[1] * forces[1] + flows[2] * forces[2]
    f_posts = []
    g_eqs = []
    for number in range(19):
        weight = lattice_weight(number)
        proj_flow = along(number, flows, density)
        proj_force = along(number, forces, density)
        shape_term = 3.0 * proj_flow + 4.5 * proj_flow * proj_flow - 1.5 * speed_sq
        f_eq = weight * density * (1.0 + shape_term)
        source = (
            (1.0 - 0.5 / TAU_FLUID)
            * weight
            * (3.0 * (proj_force - flow_force) + 9.0 * proj_flow * proj_force)
        )
        f_posts.append(f_pop[number] - (f_pop[number] - f_eq) / TAU_FLUID + source)
        g_eqs.append(weight * (3.0 * chemical + order_field * shape_term))
    rest_eq = order_field
    for number in range(1, 19):
        rest_eq = rest_eq - g_eqs[number]
    g_eqs[0] = rest_eq
    g_posts = [g_pop[number] - (g_pop[number] - g_eqs[number]) / TAU_ORDER for number in range(19)]
    return (jnp.stack(f_posts), jnp.stack(g_posts))


def collide_lists(f_pop, g_pop, order_field, laplace, slopes):
    density = f_pop[0]
    for number in range(1, 19):
        density = density + f_pop[number]
    chemical = (
        BULK_COEF * (order_field * order_field * order_field - order_field) - STIFFNESS * laplace
    )
    forces = [chemical * slope for slope in slopes]
    moments = []
    for axis_id in range(3):
        moment = jnp.zeros_like(density)
        for number in range(19):
            comp = VELOCITIES[number][axis_id]
            if comp != 0:
                moment = moment + comp * f_pop[number]
        moments.append(moment)
    flows = [(moments[axis_id] + 0.5 * forces[axis_id]) / density for axis_id in range(3)]
    speed_sq = flows[0] * flows[0] + flows[1] * flows[1] + flows[2] * flows[2]
    flow_force = flows[0] * forces[0] + flows[1] * forces[1] + flows[2] * forces[2]
    f_posts = []
    g_eqs = []
    for number in range(19):
        weight = lattice_weight(number)
        proj_flow = along(number, flows, density)
        proj_force = along(number, forces, density)
        shape_term = 3.0 * proj_flow + 4.5 * proj_flow * proj_flow - 1.5 * speed_sq
        f_eq = weight * density * (1.0 + shape_term)
        source = (
            (1.0 - 0.5 / TAU_FLUID)
            * weight
            * (3.0 * (proj_force - flow_force) + 9.0 * proj_flow * proj_force)
        )
        f_posts.append(f_pop[number] - (f_pop[number] - f_eq) / TAU_FLUID + source)
        g_eqs.append(weight * (3.0 * chemical + order_field * shape_term))
    rest_eq = order_field
    for number in range(1, 19):
        rest_eq = rest_eq - g_eqs[number]
    g_eqs[0] = rest_eq
    g_posts = [g_pop[number] - (g_pop[number] - g_eqs[number]) / TAU_ORDER for number in range(19)]
    return (f_posts, g_posts)


def collide_kernel(f_ref, g_ref, nb_ref, post_ref):
    pops = f_ref.shape[0]
    for x in range(f_ref.shape[1]):
        f_planes = [f_ref[n, x] for n in range(pops)]
        g_planes = [g_ref[n, x] for n in range(pops)]
        slopes = [nb_ref[2 + a, x] for a in range(3)]
        f_posts, g_posts = collide_lists(f_planes, g_planes, nb_ref[0, x], nb_ref[1, x], slopes)
        for n in range(pops):
            post_ref[n, x] = f_posts[n]
            post_ref[pops + n, x] = g_posts[n]


def stream_kernel(post_ref, xlow_ref, xhigh_ref, hym_ref, hyp_ref, col_ref, f_ref, g_ref):
    pops = f_ref.shape[0]
    nx, ny, nz = f_ref.shape[1:]
    row = lax.broadcasted_iota(jnp.int32, (ny, nz), 0)
    lane = lax.broadcasted_iota(jnp.int32, (ny, nz), 1)
    vel = [VELOCITIES[n % pops] for n in range(2 * pops)]
    x_up = [n for n in range(2 * pops) if vel[n][0] == 1]
    x_dn = [n for n in range(2 * pops) if vel[n][0] == -1]
    y_up = [n for n in range(2 * pops) if vel[n][1] == 1]
    y_dn = [n for n in range(2 * pops) if vel[n][1] == -1]
    z_any = [n for n in range(2 * pops) if vel[n][2] != 0]
    for n in range(2 * pops):
        cx, cy, cz = vel[n]
        out = f_ref if n < pops else g_ref
        for x in range(nx):
            src = x - cx
            if src < 0:
                tile = xlow_ref[x_up.index(n)]
            elif src >= nx:
                tile = xhigh_ref[x_dn.index(n)]
            else:
                tile = post_ref[n, src]
                if cy == 1:
                    edge = jnp.broadcast_to(hym_ref[y_up.index(n), pl.ds(src, 1), :], (ny, nz))
                    tile = jnp.where(row == 0, edge, pltpu.roll(tile, 1, 0))
                elif cy == -1:
                    edge = jnp.broadcast_to(hyp_ref[y_dn.index(n), pl.ds(src, 1), :], (ny, nz))
                    tile = jnp.where(row == ny - 1, edge, pltpu.roll(tile, ny - 1, 0))
            if cz == 1:
                tile = jnp.where(lane == 0, col_ref[z_any.index(n), x], pltpu.roll(tile, 1, 1))
            elif cz == -1:
                tile = jnp.where(lane == nz - 1, col_ref[z_any.index(n), x], pltpu.roll(tile, nz - 1, 1))
            out[n % pops, x] = tile


def exchange(sends):
    sizes = [lax.axis_size(a) for a in AXES]
    groups = {}
    order = []
    for index, (value, offset) in enumerate(sends):
        key = (tuple(o % n for o, n in zip(offset, sizes)), value.shape[1:])
        if key not in groups:
            groups[key] = []
            order.append(key)
        groups[key].append(index)
    results = [None] * len(sends)
    for key in order:
        members = groups[key]
        offset = key[0]
        pairs = []
        for i in range(sizes[0]):
            for j in range(sizes[1]):
                for k in range(sizes[2]):
                    src = (i * sizes[1] + j) * sizes[2] + k
                    ti, tj, tk = [(c + o) % n for c, o, n in zip((i, j, k), offset, sizes)]
                    pairs.append((src, (ti * sizes[1] + tj) * sizes[2] + tk))
        payload = [sends[m][0] for m in members]
        joined = payload[0] if len(payload) == 1 else jnp.concatenate(payload, axis=0)
        got = lax.ppermute(joined, AXES, pairs)
        start = 0
        for m in members:
            count = sends[m][0].shape[0]
            results[m] = got[start : start + count]
            start += count
    return results


def local(f_pop, g_pop, displacement):
    shift = displacement[0]
    nx, ny, nz = (f_pop.shape[1], f_pop.shape[2], f_pop.shape[3])
    q = SHIFT_MIN // ny
    assert SHIFT_MAX // ny == q and SHIFT_MIN % ny != 0
    rem = shift - q * ny

    phi = jnp.sum(g_pop, axis=0)
    pa, pb, pc, pd, pym, pyp, pzm, pzp = exchange(
        [
            (phi[-1:], (1, q + 1, 0)),
            (phi[-1:], (1, q, 0)),
            (phi[:1], (-1, -q, 0)),
            (phi[:1], (-1, -q - 1, 0)),
            (phi[:, -1:], (0, 1, 0)),
            (phi[:, :1], (0, -1, 0)),
            (jnp.transpose(phi[:, :, -1:], (2, 0, 1)), (0, 0, 1)),
            (jnp.transpose(phi[:, :, :1], (2, 0, 1)), (0, 0, -1)),
        ]
    )
    low = lax.dynamic_slice_in_dim(jnp.concatenate([pa, pb], axis=1), ny - rem, ny, 1)
    high = lax.dynamic_slice_in_dim(jnp.concatenate([pc, pd], axis=1), rem, ny, 1)
    neigh_xm = jnp.concatenate([low, phi[:-1]], axis=0)
    neigh_xp = jnp.concatenate([phi[1:], high], axis=0)
    neigh_ym = jnp.concatenate([pym, phi[:, :-1]], axis=1)
    neigh_yp = jnp.concatenate([phi[:, 1:], pyp], axis=1)
    neigh_zm = jnp.concatenate([jnp.transpose(pzm, (1, 2, 0)), phi[:, :, :-1]], axis=2)
    neigh_zp = jnp.concatenate([phi[:, :, 1:], jnp.transpose(pzp, (1, 2, 0))], axis=2)
    laplace = neigh_xm + neigh_xp + neigh_ym + neigh_yp + neigh_zm + neigh_zp - 6.0 * phi
    slopes = [0.5 * (neigh_xp - neigh_xm), 0.5 * (neigh_yp - neigh_ym), 0.5 * (neigh_zp - neigh_zm)]
    nb = jnp.stack([phi, laplace] + slopes)
    post = pl.pallas_call(
        collide_kernel,
        out_shape=jax.ShapeDtypeStruct((2 * f_pop.shape[0], nx, ny, nz), jnp.float32),
        interpret=INTERPRET,
    )(f_pop, g_pop, nb)

    vel = [VELOCITIES[n % 19] for n in range(38)]

    def pick(cond, among=range(38)):
        return [n for n in among if cond(vel[n])]

    x_up = pick(lambda c: c[0] == 1)
    x_dn = pick(lambda c: c[0] == -1)
    y_up = pick(lambda c: c[1] == 1)
    y_dn = pick(lambda c: c[1] == -1)
    z_up = pick(lambda c: c[2] == 1)
    z_dn = pick(lambda c: c[2] == -1)
    xz_up = pick(lambda c: c[2] != 0, x_up)
    xz_dn = pick(lambda c: c[2] != 0, x_dn)
    yz_up = pick(lambda c: c[2] != 0, y_up)
    yz_dn = pick(lambda c: c[2] != 0, y_dn)

    def rows(idx):
        return jnp.stack([post[n] for n in idx])

    hz_m, hz_p = exchange(
        [(rows(z_up)[:, :, :, -1], (0, 0, 1)), (rows(z_dn)[:, :, :, 0], (0, 0, -1))]
    )

    def zhalo(n):
        return hz_m[z_up.index(n)] if vel[n][2] == 1 else hz_p[z_dn.index(n)]

    def lanes(a):
        return jnp.pad(a, ((0, 0), (0, nz - a.shape[1])))

    def packed(face, extra):
        return jnp.concatenate([face.reshape(-1, nz), lanes(jnp.stack(extra))], axis=0)

    send_up = packed(rows(x_up)[:, -1], [zhalo(n)[-1] for n in xz_up])
    send_dn = packed(rows(x_dn)[:, 0], [zhalo(n)[0] for n in xz_dn])
    send_yu = packed(rows(y_up)[:, :, -1], [zhalo(n)[:, -1] for n in yz_up])
    send_yd = packed(rows(y_dn)[:, :, 0], [zhalo(n)[:, 0] for n in yz_dn])
    xa, xb, xc, xd, hy_m, hy_p = exchange(
        [
            (send_up, (1, q + 1, 0)),
            (send_up, (1, q, 0)),
            (send_dn, (-1, -q, 0)),
            (send_dn, (-1, -q - 1, 0)),
            (send_yu, (0, 1, 0)),
            (send_yd, (0, -1, 0)),
        ]
    )

    def unpack_x(got, count):
        return got[: count * ny].reshape(count, ny, nz), got[count * ny :, :ny]

    def unpack_y(got, count):
        return got[: count * nx].reshape(count, nx, nz), got[count * nx :, :nx]

    pa2, ca = unpack_x(xa, len(x_up))
    pb2, cb = unpack_x(xb, len(x_up))
    pc2, cc = unpack_x(xc, len(x_dn))
    pd2, cd = unpack_x(xd, len(x_dn))
    hy_m, cy_m = unpack_y(hy_m, len(y_up))
    hy_p, cy_p = unpack_y(hy_p, len(y_dn))
    win_low = lax.dynamic_slice_in_dim(jnp.concatenate([pa2, pb2], axis=1), ny - rem - 1, ny + 2, 1)
    win_high = lax.dynamic_slice_in_dim(jnp.concatenate([pc2, pd2], axis=1), rem - 1, ny + 2, 1)
    xzw_low = lax.dynamic_slice_in_dim(jnp.concatenate([ca, cb], axis=1), ny - rem, ny, 1)
    xzw_high = lax.dynamic_slice_in_dim(jnp.concatenate([cc, cd], axis=1), rem, ny, 1)

    def by_pop(idx, axis_id, shape):
        return jnp.array([vel[n][axis_id] for n in idx], jnp.int32).reshape(shape)

    def pick_y(win, idx):
        cy = by_pop(idx, 1, (-1, 1, 1))
        return jnp.where(cy == 1, win[:, :ny], jnp.where(cy == -1, win[:, 2:], win[:, 1 : ny + 1]))

    xlow = pick_y(win_low, x_up)
    xhigh = pick_y(win_high, x_dn)
    z_any = pick(lambda c: c[2] != 0)
    zh = jnp.concatenate([hz_m, hz_p])[jnp.array([z_up.index(n) if vel[n][2] == 1 else len(z_up) + z_dn.index(n) for n in z_any])]

    def spread(values, idx):
        zero = jnp.zeros((1,) + values.shape[1:], values.dtype)
        both = jnp.concatenate([values, zero])
        return both[jnp.array([idx.index(n) if n in idx else len(idx) for n in z_any])]

    corner_m = spread(cy_m, yz_up)[:, :, None]
    corner_p = spread(cy_p, yz_dn)[:, :, None]
    cy = by_pop(z_any, 1, (-1, 1, 1))
    cx = by_pop(z_any, 0, (-1, 1, 1))
    down = jnp.concatenate([corner_m, zh[:, :, :-1]], axis=2)
    up = jnp.concatenate([zh[:, :, 1:], corner_p], axis=2)
    zy = jnp.where(cy == 1, down, jnp.where(cy == -1, up, zh))
    edge_low = spread(xzw_low, xz_up)[:, None]
    edge_high = spread(xzw_high, xz_dn)[:, None]
    cols = jnp.where(
        cx == 1,
        jnp.concatenate([edge_low, zy[:, :-1]], axis=1),
        jnp.where(cx == -1, jnp.concatenate([zy[:, 1:], edge_high], axis=1), zy),
    )
    cols = jnp.broadcast_to(cols[:, :, :, None], (len(z_any), nx, ny, nz))
    pops = f_pop.shape[0]
    f_new, g_new = pl.pallas_call(
        stream_kernel,
        out_shape=(
            jax.ShapeDtypeStruct((pops, nx, ny, nz), jnp.float32),
            jax.ShapeDtypeStruct((pops, nx, ny, nz), jnp.float32),
        ),
        interpret=INTERPRET,
    )(post, xlow, xhigh, hy_m, hy_p, cols)
    return (f_new, g_new)


def solution(mesh):
    return jax.shard_map(
        local,
        mesh=mesh,
        in_specs=(P(None, "gx", "gy", "gz"), P(None, "gx", "gy", "gz"), P()),
        out_specs=(P(None, "gx", "gy", "gz"), P(None, "gx", "gy", "gz")),
        check_vma=False,
    )
```

```python
import jax
import jax.numpy as jnp
from jax import lax
from jax.sharding import PartitionSpec as P
from jax.experimental import pallas as pl
from jax.experimental.pallas import tpu as pltpu

VELOCITIES = [
    (0, 0, 0),
    (1, 0, 0),
    (1, 1, 0),
    (1, -1, 0),
    (1, 0, 1),
    (1, 0, -1),
    (-1, 0, 0),
    (-1, -1, 0),
    (-1, 1, 0),
    (-1, 0, -1),
    (-1, 0, 1),
    (0, 1, 0),
    (0, -1, 0),
    (0, 0, 1),
    (0, 0, -1),
    (0, 1, 1),
    (0, -1, -1),
    (0, 1, -1),
    (0, -1, 1),
]
BULK_COEF = 0.5
STIFFNESS = 0.5
TAU_FLUID = 0.8
TAU_ORDER = 0.9
SHIFT_MIN = 33
SHIFT_MAX = 47
AXES = ("gx", "gy", "gz")
INTERPRET = False


def lattice_weight(number):
    steps_sq = sum((abs(comp) for comp in VELOCITIES[number]))
    if steps_sq == 0:
        return 1.0 / 3.0
    if steps_sq == 1:
        return 1.0 / 18.0
    return 1.0 / 36.0


def along(number, values, base):
    result = jnp.zeros_like(base)
    for axis_id in range(3):
        comp = VELOCITIES[number][axis_id]
        if comp != 0:
            result = result + comp * values[axis_id]
    return result


def collide(f_pop, g_pop, order_field, laplace, slopes):
    density = jnp.sum(f_pop, axis=0)
    chemical = (
        BULK_COEF * (order_field * order_field * order_field - order_field) - STIFFNESS * laplace
    )
    forces = [chemical * slope for slope in slopes]
    moments = []
    for axis_id in range(3):
        moment = jnp.zeros_like(density)
        for number in range(19):
            comp = VELOCITIES[number][axis_id]
            if comp != 0:
                moment = moment + comp * f_pop[number]
        moments.append(moment)
    flows = [(moments[axis_id] + 0.5 * forces[axis_id]) / density for axis_id in range(3)]
    speed_sq = flows[0] * flows[0] + flows[1] * flows[1] + flows[2] * flows[2]
    flow_force = flows[0] * forces[0] + flows[1] * forces[1] + flows[2] * forces[2]
    f_posts = []
    g_eqs = []
    for number in range(19):
        weight = lattice_weight(number)
        proj_flow = along(number, flows, density)
        proj_force = along(number, forces, density)
        shape_term = 3.0 * proj_flow + 4.5 * proj_flow * proj_flow - 1.5 * speed_sq
        f_eq = weight * density * (1.0 + shape_term)
        source = (
            (1.0 - 0.5 / TAU_FLUID)
            * weight
            * (3.0 * (proj_force - flow_force) + 9.0 * proj_flow * proj_force)
        )
        f_posts.append(f_pop[number] - (f_pop[number] - f_eq) / TAU_FLUID + source)
        g_eqs.append(weight * (3.0 * chemical + order_field * shape_term))
    rest_eq = order_field
    for number in range(1, 19):
        rest_eq = rest_eq - g_eqs[number]
    g_eqs[0] = rest_eq
    g_posts = [g_pop[number] - (g_pop[number] - g_eqs[number]) / TAU_ORDER for number in range(19)]
    return (jnp.stack(f_posts), jnp.stack(g_posts))


def collide_lists(f_pop, g_pop, order_field, laplace, slopes):
    density = f_pop[0]
    for number in range(1, 19):
        density = density + f_pop[number]
    chemical = (
        BULK_COEF * (order_field * order_field * order_field - order_field) - STIFFNESS * laplace
    )
    forces = [chemical * slope for slope in slopes]
    moments = []
    for axis_id in range(3):
        moment = jnp.zeros_like(density)
        for number in range(19):
            comp = VELOCITIES[number][axis_id]
            if comp != 0:
                moment = moment + comp * f_pop[number]
        moments.append(moment)
    flows = [(moments[axis_id] + 0.5 * forces[axis_id]) / density for axis_id in range(3)]
    speed_sq = flows[0] * flows[0] + flows[1] * flows[1] + flows[2] * flows[2]
    flow_force = flows[0] * forces[0] + flows[1] * forces[1] + flows[2] * forces[2]
    f_posts = []
    g_eqs = []
    for number in range(19):
        weight = lattice_weight(number)
        proj_flow = along(number, flows, density)
        proj_force = along(number, forces, density)
        shape_term = 3.0 * proj_flow + 4.5 * proj_flow * proj_flow - 1.5 * speed_sq
        f_eq = weight * density * (1.0 + shape_term)
        source = (
            (1.0 - 0.5 / TAU_FLUID)
            * weight
            * (3.0 * (proj_force - flow_force) + 9.0 * proj_flow * proj_force)
        )
        f_posts.append(f_pop[number] - (f_pop[number] - f_eq) / TAU_FLUID + source)
        g_eqs.append(weight * (3.0 * chemical + order_field * shape_term))
    rest_eq = order_field
    for number in range(1, 19):
        rest_eq = rest_eq - g_eqs[number]
    g_eqs[0] = rest_eq
    g_posts = [g_pop[number] - (g_pop[number] - g_eqs[number]) / TAU_ORDER for number in range(19)]
    return (f_posts, g_posts)


def collide_kernel(f_ref, g_ref, nb_ref, post_ref):
    pops = f_ref.shape[0]
    for x in range(f_ref.shape[1]):
        f_planes = [f_ref[n, x] for n in range(pops)]
        g_planes = [g_ref[n, x] for n in range(pops)]
        slopes = [nb_ref[2 + a, x] for a in range(3)]
        f_posts, g_posts = collide_lists(f_planes, g_planes, nb_ref[0, x], nb_ref[1, x], slopes)
        for n in range(pops):
            post_ref[n, x] = f_posts[n]
            post_ref[pops + n, x] = g_posts[n]


def stream_kernel(post_ref, xlow_ref, xhigh_ref, hym_ref, hyp_ref, col_ref, f_ref, g_ref):
    pops = f_ref.shape[0]
    nx, ny, nz = f_ref.shape[1:]
    row = lax.broadcasted_iota(jnp.int32, (ny, nz), 0)
    lane = lax.broadcasted_iota(jnp.int32, (ny, nz), 1)
    vel = [VELOCITIES[n % pops] for n in range(2 * pops)]
    x_up = [n for n in range(2 * pops) if vel[n][0] == 1]
    x_dn = [n for n in range(2 * pops) if vel[n][0] == -1]
    y_up = [n for n in range(2 * pops) if vel[n][1] == 1]
    y_dn = [n for n in range(2 * pops) if vel[n][1] == -1]
    z_any = [n for n in range(2 * pops) if vel[n][2] != 0]
    for n in range(2 * pops):
        cx, cy, cz = vel[n]
        out = f_ref if n < pops else g_ref
        for x in range(nx):
            src = x - cx
            if src < 0:
                tile = xlow_ref[x_up.index(n)]
            elif src >= nx:
                tile = xhigh_ref[x_dn.index(n)]
            else:
                tile = post_ref[n, src]
                if cy == 1:
                    edge = jnp.broadcast_to(hym_ref[y_up.index(n), pl.ds(src, 1), :], (ny, nz))
                    tile = jnp.where(row == 0, edge, pltpu.roll(tile, 1, 0))
                elif cy == -1:
                    edge = jnp.broadcast_to(hyp_ref[y_dn.index(n), pl.ds(src, 1), :], (ny, nz))
                    tile = jnp.where(row == ny - 1, edge, pltpu.roll(tile, ny - 1, 0))
            if cz == 1:
                tile = jnp.where(lane == 0, col_ref[z_any.index(n), x], pltpu.roll(tile, 1, 1))
            elif cz == -1:
                tile = jnp.where(lane == nz - 1, col_ref[z_any.index(n), x], pltpu.roll(tile, nz - 1, 1))
            out[n % pops, x] = tile


def exchange(sends):
    sizes = [lax.axis_size(a) for a in AXES]
    groups = {}
    order = []
    for index, (value, offset) in enumerate(sends):
        key = (tuple(o % n for o, n in zip(offset, sizes)), value.shape[1:])
        if key not in groups:
            groups[key] = []
            order.append(key)
        groups[key].append(index)
    results = [None] * len(sends)
    for key in order:
        members = groups[key]
        offset = key[0]
        pairs = []
        for i in range(sizes[0]):
            for j in range(sizes[1]):
                for k in range(sizes[2]):
                    src = (i * sizes[1] + j) * sizes[2] + k
                    ti, tj, tk = [(c + o) % n for c, o, n in zip((i, j, k), offset, sizes)]
                    pairs.append((src, (ti * sizes[1] + tj) * sizes[2] + tk))
        payload = [sends[m][0] for m in members]
        joined = payload[0] if len(payload) == 1 else jnp.concatenate(payload, axis=0)
        got = lax.ppermute(joined, AXES, pairs)
        start = 0
        for m in members:
            count = sends[m][0].shape[0]
            results[m] = got[start : start + count]
            start += count
    return results


def local(f_pop, g_pop, displacement):
    shift = displacement[0]
    nx, ny, nz = (f_pop.shape[1], f_pop.shape[2], f_pop.shape[3])
    q = SHIFT_MIN // ny
    assert SHIFT_MAX // ny == q and SHIFT_MIN % ny != 0
    rem = shift - q * ny

    phi = jnp.sum(g_pop, axis=0)
    up1, dn1, pzm, pzp = exchange(
        [
            (jnp.concatenate([phi[:, -1], phi[-1]]), (0, 1, 0)),
            (jnp.concatenate([phi[:, 0], phi[0]]), (0, -1, 0)),
            (phi[:, :, -1][None], (0, 0, 1)),
            (phi[:, :, 0][None], (0, 0, -1)),
        ]
    )
    low_pair, high_pair = exchange(
        [
            (jnp.concatenate([up1[nx:], phi[-1]]), (1, q, 0)),
            (jnp.concatenate([phi[0], dn1[nx:]]), (-1, -q, 0)),
        ]
    )
    low = lax.dynamic_slice_in_dim(low_pair, ny - rem, ny, 0)[None]
    high = lax.dynamic_slice_in_dim(high_pair, rem, ny, 0)[None]
    neigh_xm = jnp.concatenate([low, phi[:-1]], axis=0)
    neigh_xp = jnp.concatenate([phi[1:], high], axis=0)
    neigh_ym = jnp.concatenate([up1[:nx][:, None], phi[:, :-1]], axis=1)
    neigh_yp = jnp.concatenate([phi[:, 1:], dn1[:nx][:, None]], axis=1)
    neigh_zm = jnp.concatenate([pzm[0][:, :, None], phi[:, :, :-1]], axis=2)
    neigh_zp = jnp.concatenate([phi[:, :, 1:], pzp[0][:, :, None]], axis=2)
    laplace = neigh_xm + neigh_xp + neigh_ym + neigh_yp + neigh_zm + neigh_zp - 6.0 * phi
    slopes = [0.5 * (neigh_xp - neigh_xm), 0.5 * (neigh_yp - neigh_ym), 0.5 * (neigh_zp - neigh_zm)]
    nb = jnp.stack([phi, laplace] + slopes)
    post = pl.pallas_call(
        collide_kernel,
        out_shape=jax.ShapeDtypeStruct((2 * f_pop.shape[0], nx, ny, nz), jnp.float32),
        interpret=INTERPRET,
    )(f_pop, g_pop, nb)

    vel = [VELOCITIES[n % 19] for n in range(38)]

    def pick(cond, among=range(38)):
        return [n for n in among if cond(vel[n])]

    x_up = pick(lambda c: c[0] == 1)
    x_dn = pick(lambda c: c[0] == -1)
    y_up = pick(lambda c: c[1] == 1)
    y_dn = pick(lambda c: c[1] == -1)
    z_up = pick(lambda c: c[2] == 1)
    z_dn = pick(lambda c: c[2] == -1)
    xz_up = pick(lambda c: c[2] != 0, x_up)
    xz_dn = pick(lambda c: c[2] != 0, x_dn)
    yz_up = pick(lambda c: c[2] != 0, y_up)
    yz_dn = pick(lambda c: c[2] != 0, y_dn)

    def rows(idx):
        return jnp.stack([post[n] for n in idx])

    hz_m, hz_p = exchange(
        [(rows(z_up)[:, :, :, -1], (0, 0, 1)), (rows(z_dn)[:, :, :, 0], (0, 0, -1))]
    )

    def zhalo(n):
        return hz_m[z_up.index(n)] if vel[n][2] == 1 else hz_p[z_dn.index(n)]

    def lanes(a):
        return jnp.pad(a, ((0, 0), (0, nz - a.shape[1])))

    def packed(face, extra):
        return jnp.concatenate([face.reshape(-1, nz), lanes(jnp.stack(extra))], axis=0)

    send_up = packed(rows(x_up)[:, -1], [zhalo(n)[-1] for n in xz_up])
    send_dn = packed(rows(x_dn)[:, 0], [zhalo(n)[0] for n in xz_dn])
    send_yu = packed(rows(y_up)[:, :, -1], [zhalo(n)[:, -1] for n in yz_up])
    send_yd = packed(rows(y_dn)[:, :, 0], [zhalo(n)[:, 0] for n in yz_dn])
    n_yu, n_yd = send_yu.shape[0], send_yd.shape[0]
    up2, dn2 = exchange(
        [
            (jnp.concatenate([send_yu, send_up]), (0, 1, 0)),
            (jnp.concatenate([send_yd, send_dn]), (0, -1, 0)),
        ]
    )
    hy_m, hy_p = up2[:n_yu], dn2[:n_yd]
    low2, high2 = exchange(
        [
            (jnp.concatenate([up2[n_yu:], send_up]), (1, q, 0)),
            (jnp.concatenate([send_dn, dn2[n_yd:]]), (-1, -q, 0)),
        ]
    )
    n_up, n_dn = send_up.shape[0], send_dn.shape[0]
    xa, xb, xc, xd = low2[:n_up], low2[n_up:], high2[:n_dn], high2[n_dn:]

    def unpack_x(got, count):
        return got[: count * ny].reshape(count, ny, nz), got[count * ny :, :ny]

    def unpack_y(got, count):
        return got[: count * nx].reshape(count, nx, nz), got[count * nx :, :nx]

    pa2, ca = unpack_x(xa, len(x_up))
    pb2, cb = unpack_x(xb, len(x_up))
    pc2, cc = unpack_x(xc, len(x_dn))
    pd2, cd = unpack_x(xd, len(x_dn))
    hy_m, cy_m = unpack_y(hy_m, len(y_up))
    hy_p, cy_p = unpack_y(hy_p, len(y_dn))
    win_low = lax.dynamic_slice_in_dim(jnp.concatenate([pa2, pb2], axis=1), ny - rem - 1, ny + 2, 1)
    win_high = lax.dynamic_slice_in_dim(jnp.concatenate([pc2, pd2], axis=1), rem - 1, ny + 2, 1)
    xzw_low = lax.dynamic_slice_in_dim(jnp.concatenate([ca, cb], axis=1), ny - rem, ny, 1)
    xzw_high = lax.dynamic_slice_in_dim(jnp.concatenate([cc, cd], axis=1), rem, ny, 1)

    def by_pop(idx, axis_id, shape):
        return jnp.array([vel[n][axis_id] for n in idx], jnp.int32).reshape(shape)

    def pick_y(win, idx):
        cy = by_pop(idx, 1, (-1, 1, 1))
        return jnp.where(cy == 1, win[:, :ny], jnp.where(cy == -1, win[:, 2:], win[:, 1 : ny + 1]))

    xlow = pick_y(win_low, x_up)
    xhigh = pick_y(win_high, x_dn)
    z_any = pick(lambda c: c[2] != 0)
    zh = jnp.concatenate([hz_m, hz_p])[jnp.array([z_up.index(n) if vel[n][2] == 1 else len(z_up) + z_dn.index(n) for n in z_any])]

    def spread(values, idx):
        zero = jnp.zeros((1,) + values.shape[1:], values.dtype)
        both = jnp.concatenate([values, zero])
        return both[jnp.array([idx.index(n) if n in idx else len(idx) for n in z_any])]

    corner_m = spread(cy_m, yz_up)[:, :, None]
    corner_p = spread(cy_p, yz_dn)[:, :, None]
    cy = by_pop(z_any, 1, (-1, 1, 1))
    cx = by_pop(z_any, 0, (-1, 1, 1))
    down = jnp.concatenate([corner_m, zh[:, :, :-1]], axis=2)
    up = jnp.concatenate([zh[:, :, 1:], corner_p], axis=2)
    zy = jnp.where(cy == 1, down, jnp.where(cy == -1, up, zh))
    edge_low = spread(xzw_low, xz_up)[:, None]
    edge_high = spread(xzw_high, xz_dn)[:, None]
    cols = jnp.where(
        cx == 1,
        jnp.concatenate([edge_low, zy[:, :-1]], axis=1),
        jnp.where(cx == -1, jnp.concatenate([zy[:, 1:], edge_high], axis=1), zy),
    )
    cols = jnp.broadcast_to(cols[:, :, :, None], (len(z_any), nx, ny, nz))
    pops = f_pop.shape[0]
    f_new, g_new = pl.pallas_call(
        stream_kernel,
        out_shape=(
            jax.ShapeDtypeStruct((pops, nx, ny, nz), jnp.float32),
            jax.ShapeDtypeStruct((pops, nx, ny, nz), jnp.float32),
        ),
        interpret=INTERPRET,
    )(post, xlow, xhigh, hy_m, hy_p, cols)
    return (f_new, g_new)


def solution(mesh):
    return jax.shard_map(
        local,
        mesh=mesh,
        in_specs=(P(None, "gx", "gy", "gz"), P(None, "gx", "gy", "gz"), P()),
        out_specs=(P(None, "gx", "gy", "gz"), P(None, "gx", "gy", "gz")),
        check_vma=False,
    )
```

```python
import jax
import jax.numpy as jnp
from jax import lax
from jax.sharding import PartitionSpec as P
from jax.experimental import pallas as pl
from jax.experimental.pallas import tpu as pltpu

VELOCITIES = [
    (0, 0, 0),
    (1, 0, 0),
    (1, 1, 0),
    (1, -1, 0),
    (1, 0, 1),
    (1, 0, -1),
    (-1, 0, 0),
    (-1, -1, 0),
    (-1, 1, 0),
    (-1, 0, -1),
    (-1, 0, 1),
    (0, 1, 0),
    (0, -1, 0),
    (0, 0, 1),
    (0, 0, -1),
    (0, 1, 1),
    (0, -1, -1),
    (0, 1, -1),
    (0, -1, 1),
]
BULK_COEF = 0.5
STIFFNESS = 0.5
TAU_FLUID = 0.8
TAU_ORDER = 0.9
SHIFT_MIN = 33
SHIFT_MAX = 47
AXES = ("gx", "gy", "gz")
INTERPRET = False


def lattice_weight(number):
    steps_sq = sum((abs(comp) for comp in VELOCITIES[number]))
    if steps_sq == 0:
        return 1.0 / 3.0
    if steps_sq == 1:
        return 1.0 / 18.0
    return 1.0 / 36.0


def along(number, values, base):
    result = jnp.zeros_like(base)
    for axis_id in range(3):
        comp = VELOCITIES[number][axis_id]
        if comp != 0:
            result = result + comp * values[axis_id]
    return result


def collide(f_pop, g_pop, order_field, laplace, slopes):
    density = jnp.sum(f_pop, axis=0)
    chemical = (
        BULK_COEF * (order_field * order_field * order_field - order_field) - STIFFNESS * laplace
    )
    forces = [chemical * slope for slope in slopes]
    moments = []
    for axis_id in range(3):
        moment = jnp.zeros_like(density)
        for number in range(19):
            comp = VELOCITIES[number][axis_id]
            if comp != 0:
                moment = moment + comp * f_pop[number]
        moments.append(moment)
    flows = [(moments[axis_id] + 0.5 * forces[axis_id]) / density for axis_id in range(3)]
    speed_sq = flows[0] * flows[0] + flows[1] * flows[1] + flows[2] * flows[2]
    flow_force = flows[0] * forces[0] + flows[1] * forces[1] + flows[2] * forces[2]
    f_posts = []
    g_eqs = []
    for number in range(19):
        weight = lattice_weight(number)
        proj_flow = along(number, flows, density)
        proj_force = along(number, forces, density)
        shape_term = 3.0 * proj_flow + 4.5 * proj_flow * proj_flow - 1.5 * speed_sq
        f_eq = weight * density * (1.0 + shape_term)
        source = (
            (1.0 - 0.5 / TAU_FLUID)
            * weight
            * (3.0 * (proj_force - flow_force) + 9.0 * proj_flow * proj_force)
        )
        f_posts.append(f_pop[number] - (f_pop[number] - f_eq) / TAU_FLUID + source)
        g_eqs.append(weight * (3.0 * chemical + order_field * shape_term))
    rest_eq = order_field
    for number in range(1, 19):
        rest_eq = rest_eq - g_eqs[number]
    g_eqs[0] = rest_eq
    g_posts = [g_pop[number] - (g_pop[number] - g_eqs[number]) / TAU_ORDER for number in range(19)]
    return (jnp.stack(f_posts), jnp.stack(g_posts))


def collide_lists(f_pop, g_pop, order_field, laplace, slopes):
    density = f_pop[0]
    for number in range(1, 19):
        density = density + f_pop[number]
    chemical = (
        BULK_COEF * (order_field * order_field * order_field - order_field) - STIFFNESS * laplace
    )
    forces = [chemical * slope for slope in slopes]
    moments = []
    for axis_id in range(3):
        moment = jnp.zeros_like(density)
        for number in range(19):
            comp = VELOCITIES[number][axis_id]
            if comp != 0:
                moment = moment + comp * f_pop[number]
        moments.append(moment)
    flows = [(moments[axis_id] + 0.5 * forces[axis_id]) / density for axis_id in range(3)]
    speed_sq = flows[0] * flows[0] + flows[1] * flows[1] + flows[2] * flows[2]
    flow_force = flows[0] * forces[0] + flows[1] * forces[1] + flows[2] * forces[2]
    f_posts = []
    g_eqs = []
    for number in range(19):
        weight = lattice_weight(number)
        proj_flow = along(number, flows, density)
        proj_force = along(number, forces, density)
        shape_term = 3.0 * proj_flow + 4.5 * proj_flow * proj_flow - 1.5 * speed_sq
        f_eq = weight * density * (1.0 + shape_term)
        source = (
            (1.0 - 0.5 / TAU_FLUID)
            * weight
            * (3.0 * (proj_force - flow_force) + 9.0 * proj_flow * proj_force)
        )
        f_posts.append(f_pop[number] - (f_pop[number] - f_eq) / TAU_FLUID + source)
        g_eqs.append(weight * (3.0 * chemical + order_field * shape_term))
    rest_eq = order_field
    for number in range(1, 19):
        rest_eq = rest_eq - g_eqs[number]
    g_eqs[0] = rest_eq
    g_posts = [g_pop[number] - (g_pop[number] - g_eqs[number]) / TAU_ORDER for number in range(19)]
    return (f_posts, g_posts)


def collide_kernel(f_ref, g_ref, nb_ref, post_ref):
    pops = f_ref.shape[0]
    for x in range(f_ref.shape[1]):
        f_planes = [f_ref[n, x] for n in range(pops)]
        g_planes = [g_ref[n, x] for n in range(pops)]
        slopes = [nb_ref[2 + a, x] for a in range(3)]
        f_posts, g_posts = collide_lists(f_planes, g_planes, nb_ref[0, x], nb_ref[1, x], slopes)
        for n in range(pops):
            post_ref[n, x] = f_posts[n]
            post_ref[pops + n, x] = g_posts[n]


def stream_kernel(post_ref, xlow_ref, xhigh_ref, hym_ref, hyp_ref, col_ref, f_ref, g_ref):
    pops = f_ref.shape[0]
    nx, ny, nz = f_ref.shape[1:]
    row = lax.broadcasted_iota(jnp.int32, (ny, nz), 0)
    lane = lax.broadcasted_iota(jnp.int32, (ny, nz), 1)
    vel = [VELOCITIES[n % pops] for n in range(2 * pops)]
    x_up = [n for n in range(2 * pops) if vel[n][0] == 1]
    x_dn = [n for n in range(2 * pops) if vel[n][0] == -1]
    y_up = [n for n in range(2 * pops) if vel[n][1] == 1]
    y_dn = [n for n in range(2 * pops) if vel[n][1] == -1]
    z_any = [n for n in range(2 * pops) if vel[n][2] != 0]
    for n in range(2 * pops):
        cx, cy, cz = vel[n]
        out = f_ref if n < pops else g_ref
        for x in range(nx):
            src = x - cx
            if src < 0:
                tile = xlow_ref[x_up.index(n)]
            elif src >= nx:
                tile = xhigh_ref[x_dn.index(n)]
            else:
                tile = post_ref[n, src]
                if cy == 1:
                    edge = jnp.broadcast_to(hym_ref[y_up.index(n), pl.ds(src, 1), :], (ny, nz))
                    tile = jnp.where(row == 0, edge, pltpu.roll(tile, 1, 0))
                elif cy == -1:
                    edge = jnp.broadcast_to(hyp_ref[y_dn.index(n), pl.ds(src, 1), :], (ny, nz))
                    tile = jnp.where(row == ny - 1, edge, pltpu.roll(tile, ny - 1, 0))
            if cz == 1:
                tile = jnp.where(lane == 0, col_ref[z_any.index(n), x], pltpu.roll(tile, 1, 1))
            elif cz == -1:
                tile = jnp.where(lane == nz - 1, col_ref[z_any.index(n), x], pltpu.roll(tile, nz - 1, 1))
            out[n % pops, x] = tile


def exchange(sends):
    sizes = [lax.axis_size(a) for a in AXES]
    groups = {}
    order = []
    for index, (value, offset) in enumerate(sends):
        key = (tuple(o % n for o, n in zip(offset, sizes)), value.shape[1:])
        if key not in groups:
            groups[key] = []
            order.append(key)
        groups[key].append(index)
    results = [None] * len(sends)
    for key in order:
        members = groups[key]
        offset = key[0]
        pairs = []
        for i in range(sizes[0]):
            for j in range(sizes[1]):
                for k in range(sizes[2]):
                    src = (i * sizes[1] + j) * sizes[2] + k
                    ti, tj, tk = [(c + o) % n for c, o, n in zip((i, j, k), offset, sizes)]
                    pairs.append((src, (ti * sizes[1] + tj) * sizes[2] + tk))
        payload = [sends[m][0] for m in members]
        joined = payload[0] if len(payload) == 1 else jnp.concatenate(payload, axis=0)
        got = lax.ppermute(joined, AXES, pairs)
        start = 0
        for m in members:
            count = sends[m][0].shape[0]
            results[m] = got[start : start + count]
            start += count
    return results


def local(f_pop, g_pop, displacement):
    shift = displacement[0]
    nx, ny, nz = (f_pop.shape[1], f_pop.shape[2], f_pop.shape[3])
    q = SHIFT_MIN // ny
    assert SHIFT_MAX // ny == q and SHIFT_MIN % ny != 0
    rem = shift - q * ny

    phi = jnp.sum(g_pop, axis=0)
    up1, dn1, pzm, pzp = exchange(
        [
            (jnp.concatenate([phi[:, -1], phi[-1]]), (0, 1, 0)),
            (jnp.concatenate([phi[:, 0], phi[0]]), (0, -1, 0)),
            (phi[:, :, -1][None], (0, 0, 1)),
            (phi[:, :, 0][None], (0, 0, -1)),
        ]
    )
    low_pair, high_pair = exchange(
        [
            (jnp.concatenate([up1[nx:], phi[-1]]), (1, q, 0)),
            (jnp.concatenate([phi[0], dn1[nx:]]), (-1, -q, 0)),
        ]
    )
    low = lax.dynamic_slice_in_dim(low_pair, ny - rem, ny, 0)[None]
    high = lax.dynamic_slice_in_dim(high_pair, rem, ny, 0)[None]
    neigh_xm = jnp.concatenate([low, phi[:-1]], axis=0)
    neigh_xp = jnp.concatenate([phi[1:], high], axis=0)
    neigh_ym = jnp.concatenate([up1[:nx][:, None], phi[:, :-1]], axis=1)
    neigh_yp = jnp.concatenate([phi[:, 1:], dn1[:nx][:, None]], axis=1)
    neigh_zm = jnp.concatenate([pzm[0][:, :, None], phi[:, :, :-1]], axis=2)
    neigh_zp = jnp.concatenate([phi[:, :, 1:], pzp[0][:, :, None]], axis=2)
    laplace = neigh_xm + neigh_xp + neigh_ym + neigh_yp + neigh_zm + neigh_zp - 6.0 * phi
    slopes = [0.5 * (neigh_xp - neigh_xm), 0.5 * (neigh_yp - neigh_ym), 0.5 * (neigh_zp - neigh_zm)]
    nb = jnp.stack([phi, laplace] + slopes)
    post = pl.pallas_call(
        collide_kernel,
        out_shape=jax.ShapeDtypeStruct((2 * f_pop.shape[0], nx, ny, nz), jnp.float32),
        interpret=INTERPRET,
    )(f_pop, g_pop, nb)

    vel = [VELOCITIES[n % 19] for n in range(38)]

    def pick(cond, among=range(38)):
        return [n for n in among if cond(vel[n])]

    x_up = pick(lambda c: c[0] == 1)
    x_dn = pick(lambda c: c[0] == -1)
    y_up = pick(lambda c: c[1] == 1)
    y_dn = pick(lambda c: c[1] == -1)
    z_up = pick(lambda c: c[2] == 1)
    z_dn = pick(lambda c: c[2] == -1)
    xz_up = pick(lambda c: c[2] != 0, x_up)
    xz_dn = pick(lambda c: c[2] != 0, x_dn)
    yz_up = pick(lambda c: c[2] != 0, y_up)
    yz_dn = pick(lambda c: c[2] != 0, y_dn)

    def rows(idx):
        return jnp.stack([post[n] for n in idx])

    hz_m, hz_p = exchange(
        [(rows(z_up)[:, :, :, -1], (0, 0, 1)), (rows(z_dn)[:, :, :, 0], (0, 0, -1))]
    )

    def zhalo(n):
        return hz_m[z_up.index(n)] if vel[n][2] == 1 else hz_p[z_dn.index(n)]

    def lanes(a):
        return jnp.pad(a, ((0, 0), (0, nz - a.shape[1])))

    def packed(face, extra):
        return jnp.concatenate([face.reshape(-1, nz), lanes(jnp.stack(extra))], axis=0)

    send_up = packed(rows(x_up)[:, -1], [zhalo(n)[-1] for n in xz_up])
    send_dn = packed(rows(x_dn)[:, 0], [zhalo(n)[0] for n in xz_dn])
    send_yu = packed(rows(y_up)[:, :, -1], [zhalo(n)[:, -1] for n in yz_up])
    send_yd = packed(rows(y_dn)[:, :, 0], [zhalo(n)[:, 0] for n in yz_dn])
    xa, xb, xc, xd, hy_m, hy_p = exchange(
        [
            (send_up, (1, q + 1, 0)),
            (send_up, (1, q, 0)),
            (send_dn, (-1, -q, 0)),
            (send_dn, (-1, -q - 1, 0)),
            (send_yu, (0, 1, 0)),
            (send_yd, (0, -1, 0)),
        ]
    )

    def unpack_x(got, count):
        return got[: count * ny].reshape(count, ny, nz), got[count * ny :, :ny]

    def unpack_y(got, count):
        return got[: count * nx].reshape(count, nx, nz), got[count * nx :, :nx]

    pa2, ca = unpack_x(xa, len(x_up))
    pb2, cb = unpack_x(xb, len(x_up))
    pc2, cc = unpack_x(xc, len(x_dn))
    pd2, cd = unpack_x(xd, len(x_dn))
    hy_m, cy_m = unpack_y(hy_m, len(y_up))
    hy_p, cy_p = unpack_y(hy_p, len(y_dn))
    win_low = lax.dynamic_slice_in_dim(jnp.concatenate([pa2, pb2], axis=1), ny - rem - 1, ny + 2, 1)
    win_high = lax.dynamic_slice_in_dim(jnp.concatenate([pc2, pd2], axis=1), rem - 1, ny + 2, 1)
    xzw_low = lax.dynamic_slice_in_dim(jnp.concatenate([ca, cb], axis=1), ny - rem, ny, 1)
    xzw_high = lax.dynamic_slice_in_dim(jnp.concatenate([cc, cd], axis=1), rem, ny, 1)

    def by_pop(idx, axis_id, shape):
        return jnp.array([vel[n][axis_id] for n in idx], jnp.int32).reshape(shape)

    def pick_y(win, idx):
        cy = by_pop(idx, 1, (-1, 1, 1))
        return jnp.where(cy == 1, win[:, :ny], jnp.where(cy == -1, win[:, 2:], win[:, 1 : ny + 1]))

    xlow = pick_y(win_low, x_up)
    xhigh = pick_y(win_high, x_dn)
    z_any = pick(lambda c: c[2] != 0)
    zh = jnp.concatenate([hz_m, hz_p])[jnp.array([z_up.index(n) if vel[n][2] == 1 else len(z_up) + z_dn.index(n) for n in z_any])]

    def spread(values, idx):
        zero = jnp.zeros((1,) + values.shape[1:], values.dtype)
        both = jnp.concatenate([values, zero])
        return both[jnp.array([idx.index(n) if n in idx else len(idx) for n in z_any])]

    corner_m = spread(cy_m, yz_up)[:, :, None]
    corner_p = spread(cy_p, yz_dn)[:, :, None]
    cy = by_pop(z_any, 1, (-1, 1, 1))
    cx = by_pop(z_any, 0, (-1, 1, 1))
    down = jnp.concatenate([corner_m, zh[:, :, :-1]], axis=2)
    up = jnp.concatenate([zh[:, :, 1:], corner_p], axis=2)
    zy = jnp.where(cy == 1, down, jnp.where(cy == -1, up, zh))
    edge_low = spread(xzw_low, xz_up)[:, None]
    edge_high = spread(xzw_high, xz_dn)[:, None]
    cols = jnp.where(
        cx == 1,
        jnp.concatenate([edge_low, zy[:, :-1]], axis=1),
        jnp.where(cx == -1, jnp.concatenate([zy[:, 1:], edge_high], axis=1), zy),
    )
    cols = jnp.broadcast_to(cols[:, :, :, None], (len(z_any), nx, ny, nz))
    pops = f_pop.shape[0]
    f_new, g_new = pl.pallas_call(
        stream_kernel,
        out_shape=(
            jax.ShapeDtypeStruct((pops, nx, ny, nz), jnp.float32),
            jax.ShapeDtypeStruct((pops, nx, ny, nz), jnp.float32),
        ),
        interpret=INTERPRET,
    )(post, xlow, xhigh, hy_m, hy_p, cols)
    return (f_new, g_new)


def solution(mesh):
    return jax.shard_map(
        local,
        mesh=mesh,
        in_specs=(P(None, "gx", "gy", "gz"), P(None, "gx", "gy", "gz"), P()),
        out_specs=(P(None, "gx", "gy", "gz"), P(None, "gx", "gy", "gz")),
        check_vma=False,
    )
```

```python
import jax
import jax.numpy as jnp
from jax import lax
from jax.sharding import PartitionSpec as P
from jax.experimental import pallas as pl
from jax.experimental.pallas import tpu as pltpu

VELOCITIES = [
    (0, 0, 0),
    (1, 0, 0),
    (1, 1, 0),
    (1, -1, 0),
    (1, 0, 1),
    (1, 0, -1),
    (-1, 0, 0),
    (-1, -1, 0),
    (-1, 1, 0),
    (-1, 0, -1),
    (-1, 0, 1),
    (0, 1, 0),
    (0, -1, 0),
    (0, 0, 1),
    (0, 0, -1),
    (0, 1, 1),
    (0, -1, -1),
    (0, 1, -1),
    (0, -1, 1),
]
BULK_COEF = 0.5
STIFFNESS = 0.5
TAU_FLUID = 0.8
TAU_ORDER = 0.9
SHIFT_MIN = 33
SHIFT_MAX = 47
AXES = ("gx", "gy", "gz")
INTERPRET = False


def lattice_weight(number):
    steps_sq = sum((abs(comp) for comp in VELOCITIES[number]))
    if steps_sq == 0:
        return 1.0 / 3.0
    if steps_sq == 1:
        return 1.0 / 18.0
    return 1.0 / 36.0


def along(number, values, base):
    result = jnp.zeros_like(base)
    for axis_id in range(3):
        comp = VELOCITIES[number][axis_id]
        if comp != 0:
            result = result + comp * values[axis_id]
    return result


def collide(f_pop, g_pop, order_field, laplace, slopes):
    density = jnp.sum(f_pop, axis=0)
    chemical = (
        BULK_COEF * (order_field * order_field * order_field - order_field) - STIFFNESS * laplace
    )
    forces = [chemical * slope for slope in slopes]
    moments = []
    for axis_id in range(3):
        moment = jnp.zeros_like(density)
        for number in range(19):
            comp = VELOCITIES[number][axis_id]
            if comp != 0:
                moment = moment + comp * f_pop[number]
        moments.append(moment)
    flows = [(moments[axis_id] + 0.5 * forces[axis_id]) / density for axis_id in range(3)]
    speed_sq = flows[0] * flows[0] + flows[1] * flows[1] + flows[2] * flows[2]
    flow_force = flows[0] * forces[0] + flows[1] * forces[1] + flows[2] * forces[2]
    f_posts = []
    g_eqs = []
    for number in range(19):
        weight = lattice_weight(number)
        proj_flow = along(number, flows, density)
        proj_force = along(number, forces, density)
        shape_term = 3.0 * proj_flow + 4.5 * proj_flow * proj_flow - 1.5 * speed_sq
        f_eq = weight * density * (1.0 + shape_term)
        source = (
            (1.0 - 0.5 / TAU_FLUID)
            * weight
            * (3.0 * (proj_force - flow_force) + 9.0 * proj_flow * proj_force)
        )
        f_posts.append(f_pop[number] - (f_pop[number] - f_eq) / TAU_FLUID + source)
        g_eqs.append(weight * (3.0 * chemical + order_field * shape_term))
    rest_eq = order_field
    for number in range(1, 19):
        rest_eq = rest_eq - g_eqs[number]
    g_eqs[0] = rest_eq
    g_posts = [g_pop[number] - (g_pop[number] - g_eqs[number]) / TAU_ORDER for number in range(19)]
    return (jnp.stack(f_posts), jnp.stack(g_posts))


def collide_lists(f_pop, g_pop, order_field, laplace, slopes):
    density = f_pop[0]
    for number in range(1, 19):
        density = density + f_pop[number]
    chemical = (
        BULK_COEF * (order_field * order_field * order_field - order_field) - STIFFNESS * laplace
    )
    forces = [chemical * slope for slope in slopes]
    moments = []
    for axis_id in range(3):
        moment = jnp.zeros_like(density)
        for number in range(19):
            comp = VELOCITIES[number][axis_id]
            if comp != 0:
                moment = moment + comp * f_pop[number]
        moments.append(moment)
    flows = [(moments[axis_id] + 0.5 * forces[axis_id]) / density for axis_id in range(3)]
    speed_sq = flows[0] * flows[0] + flows[1] * flows[1] + flows[2] * flows[2]
    flow_force = flows[0] * forces[0] + flows[1] * forces[1] + flows[2] * forces[2]
    f_posts = []
    g_eqs = []
    for number in range(19):
        weight = lattice_weight(number)
        proj_flow = along(number, flows, density)
        proj_force = along(number, forces, density)
        shape_term = 3.0 * proj_flow + 4.5 * proj_flow * proj_flow - 1.5 * speed_sq
        f_eq = weight * density * (1.0 + shape_term)
        source = (
            (1.0 - 0.5 / TAU_FLUID)
            * weight
            * (3.0 * (proj_force - flow_force) + 9.0 * proj_flow * proj_force)
        )
        f_posts.append(f_pop[number] - (f_pop[number] - f_eq) / TAU_FLUID + source)
        g_eqs.append(weight * (3.0 * chemical + order_field * shape_term))
    rest_eq = order_field
    for number in range(1, 19):
        rest_eq = rest_eq - g_eqs[number]
    g_eqs[0] = rest_eq
    g_posts = [g_pop[number] - (g_pop[number] - g_eqs[number]) / TAU_ORDER for number in range(19)]
    return (f_posts, g_posts)


def collide_kernel(f_ref, g_ref, nb_ref, post_ref):
    pops = f_ref.shape[0]
    for x in range(f_ref.shape[1]):
        f_planes = [f_ref[n, x] for n in range(pops)]
        g_planes = [g_ref[n, x] for n in range(pops)]
        slopes = [nb_ref[2 + a, x] for a in range(3)]
        f_posts, g_posts = collide_lists(f_planes, g_planes, nb_ref[0, x], nb_ref[1, x], slopes)
        for n in range(pops):
            post_ref[n, x] = f_posts[n]
            post_ref[pops + n, x] = g_posts[n]


def stream_kernel(post_ref, xlow_ref, xhigh_ref, hym_ref, hyp_ref, col_ref, f_ref, g_ref):
    pops = f_ref.shape[0]
    nx, ny, nz = f_ref.shape[1:]
    row = lax.broadcasted_iota(jnp.int32, (ny, nz), 0)
    lane = lax.broadcasted_iota(jnp.int32, (ny, nz), 1)
    vel = [VELOCITIES[n % pops] for n in range(2 * pops)]
    x_up = [n for n in range(2 * pops) if vel[n][0] == 1]
    x_dn = [n for n in range(2 * pops) if vel[n][0] == -1]
    y_up = [n for n in range(2 * pops) if vel[n][1] == 1]
    y_dn = [n for n in range(2 * pops) if vel[n][1] == -1]
    z_any = [n for n in range(2 * pops) if vel[n][2] != 0]
    for n in range(2 * pops):
        cx, cy, cz = vel[n]
        out = f_ref if n < pops else g_ref
        for x in range(nx):
            src = x - cx
            if src < 0:
                tile = xlow_ref[x_up.index(n)]
            elif src >= nx:
                tile = xhigh_ref[x_dn.index(n)]
            else:
                tile = post_ref[n, src]
                if cy == 1:
                    edge = jnp.broadcast_to(hym_ref[y_up.index(n), pl.ds(src, 1), :], (ny, nz))
                    tile = jnp.where(row == 0, edge, pltpu.roll(tile, 1, 0))
                elif cy == -1:
                    edge = jnp.broadcast_to(hyp_ref[y_dn.index(n), pl.ds(src, 1), :], (ny, nz))
                    tile = jnp.where(row == ny - 1, edge, pltpu.roll(tile, ny - 1, 0))
            if cz == 1:
                tile = jnp.where(lane == 0, col_ref[z_any.index(n), x], pltpu.roll(tile, 1, 1))
            elif cz == -1:
                tile = jnp.where(lane == nz - 1, col_ref[z_any.index(n), x], pltpu.roll(tile, nz - 1, 1))
            out[n % pops, x] = tile


def exchange(sends):
    sizes = [lax.axis_size(a) for a in AXES]
    groups = {}
    order = []
    for index, (value, offset) in enumerate(sends):
        key = (tuple(o % n for o, n in zip(offset, sizes)), value.shape[1:])
        if key not in groups:
            groups[key] = []
            order.append(key)
        groups[key].append(index)
    results = [None] * len(sends)
    for key in order:
        members = groups[key]
        offset = key[0]
        pairs = []
        for i in range(sizes[0]):
            for j in range(sizes[1]):
                for k in range(sizes[2]):
                    src = (i * sizes[1] + j) * sizes[2] + k
                    ti, tj, tk = [(c + o) % n for c, o, n in zip((i, j, k), offset, sizes)]
                    pairs.append((src, (ti * sizes[1] + tj) * sizes[2] + tk))
        payload = [sends[m][0] for m in members]
        joined = payload[0] if len(payload) == 1 else jnp.concatenate(payload, axis=0)
        got = lax.ppermute(joined, AXES, pairs)
        start = 0
        for m in members:
            count = sends[m][0].shape[0]
            results[m] = got[start : start + count]
            start += count
    return results


def local(f_pop, g_pop, displacement):
    shift = displacement[0]
    nx, ny, nz = (f_pop.shape[1], f_pop.shape[2], f_pop.shape[3])
    q = SHIFT_MIN // ny
    assert SHIFT_MAX // ny == q and SHIFT_MIN % ny != 0
    rem = shift - q * ny

    phi = jnp.sum(g_pop, axis=0)
    up1, dn1, pzm, pzp = exchange(
        [
            (jnp.concatenate([phi[:, -1], phi[-1]]), (0, 1, 0)),
            (jnp.concatenate([phi[:, 0], phi[0]]), (0, -1, 0)),
            (phi[:, :, -1][None], (0, 0, 1)),
            (phi[:, :, 0][None], (0, 0, -1)),
        ]
    )
    low_pair, high_pair = exchange(
        [
            (jnp.concatenate([up1[nx:], phi[-1]]), (1, q, 0)),
            (jnp.concatenate([phi[0], dn1[nx:]]), (-1, -q, 0)),
        ]
    )
    low = lax.dynamic_slice_in_dim(low_pair, ny - rem, ny, 0)[None]
    high = lax.dynamic_slice_in_dim(high_pair, rem, ny, 0)[None]
    neigh_xm = jnp.concatenate([low, phi[:-1]], axis=0)
    neigh_xp = jnp.concatenate([phi[1:], high], axis=0)
    neigh_ym = jnp.concatenate([up1[:nx][:, None], phi[:, :-1]], axis=1)
    neigh_yp = jnp.concatenate([phi[:, 1:], dn1[:nx][:, None]], axis=1)
    neigh_zm = jnp.concatenate([pzm[0][:, :, None], phi[:, :, :-1]], axis=2)
    neigh_zp = jnp.concatenate([phi[:, :, 1:], pzp[0][:, :, None]], axis=2)
    laplace = neigh_xm + neigh_xp + neigh_ym + neigh_yp + neigh_zm + neigh_zp - 6.0 * phi
    slopes = [0.5 * (neigh_xp - neigh_xm), 0.5 * (neigh_yp - neigh_ym), 0.5 * (neigh_zp - neigh_zm)]
    nb = jnp.stack([phi, laplace] + slopes)
    post = pl.pallas_call(
        collide_kernel,
        out_shape=jax.ShapeDtypeStruct((2 * f_pop.shape[0], nx, ny, nz), jnp.float32),
        interpret=INTERPRET,
    )(f_pop, g_pop, nb)

    vel = [VELOCITIES[n % 19] for n in range(38)]

    def pick(cond, among=range(38)):
        return [n for n in among if cond(vel[n])]

    x_up = pick(lambda c: c[0] == 1)
    x_dn = pick(lambda c: c[0] == -1)
    y_up = pick(lambda c: c[1] == 1)
    y_dn = pick(lambda c: c[1] == -1)
    z_up = pick(lambda c: c[2] == 1)
    z_dn = pick(lambda c: c[2] == -1)
    xz_up = pick(lambda c: c[2] != 0, x_up)
    xz_dn = pick(lambda c: c[2] != 0, x_dn)
    yz_up = pick(lambda c: c[2] != 0, y_up)
    yz_dn = pick(lambda c: c[2] != 0, y_dn)

    def rows(idx):
        return jnp.stack([post[n] for n in idx])

    hz_m, hz_p = exchange(
        [(rows(z_up)[:, :, :, -1], (0, 0, 1)), (rows(z_dn)[:, :, :, 0], (0, 0, -1))]
    )

    def zhalo(n):
        return hz_m[z_up.index(n)] if vel[n][2] == 1 else hz_p[z_dn.index(n)]

    def lanes(a):
        return jnp.pad(a, ((0, 0), (0, nz - a.shape[1])))

    def packed(face, extra):
        return jnp.concatenate([face.reshape(-1, nz), lanes(jnp.stack(extra))], axis=0)

    send_up = packed(rows(x_up)[:, -1], [zhalo(n)[-1] for n in xz_up])
    send_dn = packed(rows(x_dn)[:, 0], [zhalo(n)[0] for n in xz_dn])
    send_yu = packed(rows(y_up)[:, :, -1], [zhalo(n)[:, -1] for n in yz_up])
    send_yd = packed(rows(y_dn)[:, :, 0], [zhalo(n)[:, 0] for n in yz_dn])
    n_yu, n_yd = send_yu.shape[0], send_yd.shape[0]
    up2, dn2 = exchange(
        [
            (jnp.concatenate([send_yu, send_up]), (0, 1, 0)),
            (jnp.concatenate([send_yd, send_dn]), (0, -1, 0)),
        ]
    )
    hy_m, hy_p = up2[:n_yu], dn2[:n_yd]

    def unpack_x(got, count):
        return got[: count * ny].reshape(count, ny, nz), got[count * ny :, :ny]

    def unpack_y(got, count):
        return got[: count * nx].reshape(count, nx, nz), got[count * nx :, :nx]

    def window(first, second, count, start):
        pa, ca = unpack_x(first, count)
        pb, cb = unpack_x(second, count)
        planes = lax.dynamic_slice_in_dim(jnp.concatenate([pa, pb], axis=1), start - 1, ny + 2, 1)
        cols = lax.dynamic_slice_in_dim(jnp.concatenate([ca, cb], axis=1), start, ny, 1)
        return jnp.concatenate([planes.reshape(-1, nz), lanes(cols)], axis=0)

    low2, high2 = exchange(
        [
            (window(up2[n_yu:], send_up, len(x_up), ny - rem), (1, q, 0)),
            (window(send_dn, dn2[n_yd:], len(x_dn), rem), (-1, -q, 0)),
        ]
    )
    hy_m, cy_m = unpack_y(hy_m, len(y_up))
    hy_p, cy_p = unpack_y(hy_p, len(y_dn))
    n_lo, n_hi = len(x_up) * (ny + 2), len(x_dn) * (ny + 2)
    win_low = low2[:n_lo].reshape(len(x_up), ny + 2, nz)
    win_high = high2[:n_hi].reshape(len(x_dn), ny + 2, nz)
    xzw_low = low2[n_lo:, :ny]
    xzw_high = high2[n_hi:, :ny]

    def by_pop(idx, axis_id, shape):
        return jnp.array([vel[n][axis_id] for n in idx], jnp.int32).reshape(shape)

    def pick_y(win, idx):
        cy = by_pop(idx, 1, (-1, 1, 1))
        return jnp.where(cy == 1, win[:, :ny], jnp.where(cy == -1, win[:, 2:], win[:, 1 : ny + 1]))

    xlow = pick_y(win_low, x_up)
    xhigh = pick_y(win_high, x_dn)
    z_any = pick(lambda c: c[2] != 0)
    zh = jnp.concatenate([hz_m, hz_p])[jnp.array([z_up.index(n) if vel[n][2] == 1 else len(z_up) + z_dn.index(n) for n in z_any])]

    def spread(values, idx):
        zero = jnp.zeros((1,) + values.shape[1:], values.dtype)
        both = jnp.concatenate([values, zero])
        return both[jnp.array([idx.index(n) if n in idx else len(idx) for n in z_any])]

    corner_m = spread(cy_m, yz_up)[:, :, None]
    corner_p = spread(cy_p, yz_dn)[:, :, None]
    cy = by_pop(z_any, 1, (-1, 1, 1))
    cx = by_pop(z_any, 0, (-1, 1, 1))
    down = jnp.concatenate([corner_m, zh[:, :, :-1]], axis=2)
    up = jnp.concatenate([zh[:, :, 1:], corner_p], axis=2)
    zy = jnp.where(cy == 1, down, jnp.where(cy == -1, up, zh))
    edge_low = spread(xzw_low, xz_up)[:, None]
    edge_high = spread(xzw_high, xz_dn)[:, None]
    cols = jnp.where(
        cx == 1,
        jnp.concatenate([edge_low, zy[:, :-1]], axis=1),
        jnp.where(cx == -1, jnp.concatenate([zy[:, 1:], edge_high], axis=1), zy),
    )
    cols = jnp.broadcast_to(cols[:, :, :, None], (len(z_any), nx, ny, nz))
    pops = f_pop.shape[0]
    f_new, g_new = pl.pallas_call(
        stream_kernel,
        out_shape=(
            jax.ShapeDtypeStruct((pops, nx, ny, nz), jnp.float32),
            jax.ShapeDtypeStruct((pops, nx, ny, nz), jnp.float32),
        ),
        interpret=INTERPRET,
    )(post, xlow, xhigh, hy_m, hy_p, cols)
    return (f_new, g_new)


def solution(mesh):
    return jax.shard_map(
        local,
        mesh=mesh,
        in_specs=(P(None, "gx", "gy", "gz"), P(None, "gx", "gy", "gz"), P()),
        out_specs=(P(None, "gx", "gy", "gz"), P(None, "gx", "gy", "gz")),
        check_vma=False,
    )
```

```python
import jax
import jax.numpy as jnp
from jax import lax
from jax.sharding import PartitionSpec as P
from jax.experimental import pallas as pl
from jax.experimental.pallas import tpu as pltpu

VELOCITIES = [
    (0, 0, 0),
    (1, 0, 0),
    (1, 1, 0),
    (1, -1, 0),
    (1, 0, 1),
    (1, 0, -1),
    (-1, 0, 0),
    (-1, -1, 0),
    (-1, 1, 0),
    (-1, 0, -1),
    (-1, 0, 1),
    (0, 1, 0),
    (0, -1, 0),
    (0, 0, 1),
    (0, 0, -1),
    (0, 1, 1),
    (0, -1, -1),
    (0, 1, -1),
    (0, -1, 1),
]
BULK_COEF = 0.5
STIFFNESS = 0.5
TAU_FLUID = 0.8
TAU_ORDER = 0.9
SHIFT_MIN = 33
SHIFT_MAX = 47
AXES = ("gx", "gy", "gz")
INTERPRET = False


def lattice_weight(number):
    steps_sq = sum((abs(comp) for comp in VELOCITIES[number]))
    if steps_sq == 0:
        return 1.0 / 3.0
    if steps_sq == 1:
        return 1.0 / 18.0
    return 1.0 / 36.0


def along(number, values, base):
    result = jnp.zeros_like(base)
    for axis_id in range(3):
        comp = VELOCITIES[number][axis_id]
        if comp != 0:
            result = result + comp * values[axis_id]
    return result


def collide(f_pop, g_pop, order_field, laplace, slopes):
    density = jnp.sum(f_pop, axis=0)
    chemical = (
        BULK_COEF * (order_field * order_field * order_field - order_field) - STIFFNESS * laplace
    )
    forces = [chemical * slope for slope in slopes]
    moments = []
    for axis_id in range(3):
        moment = jnp.zeros_like(density)
        for number in range(19):
            comp = VELOCITIES[number][axis_id]
            if comp != 0:
                moment = moment + comp * f_pop[number]
        moments.append(moment)
    flows = [(moments[axis_id] + 0.5 * forces[axis_id]) / density for axis_id in range(3)]
    speed_sq = flows[0] * flows[0] + flows[1] * flows[1] + flows[2] * flows[2]
    flow_force = flows[0] * forces[0] + flows[1] * forces[1] + flows[2] * forces[2]
    f_posts = []
    g_eqs = []
    for number in range(19):
        weight = lattice_weight(number)
        proj_flow = along(number, flows, density)
        proj_force = along(number, forces, density)
        shape_term = 3.0 * proj_flow + 4.5 * proj_flow * proj_flow - 1.5 * speed_sq
        f_eq = weight * density * (1.0 + shape_term)
        source = (
            (1.0 - 0.5 / TAU_FLUID)
            * weight
            * (3.0 * (proj_force - flow_force) + 9.0 * proj_flow * proj_force)
        )
        f_posts.append(f_pop[number] - (f_pop[number] - f_eq) / TAU_FLUID + source)
        g_eqs.append(weight * (3.0 * chemical + order_field * shape_term))
    rest_eq = order_field
    for number in range(1, 19):
        rest_eq = rest_eq - g_eqs[number]
    g_eqs[0] = rest_eq
    g_posts = [g_pop[number] - (g_pop[number] - g_eqs[number]) / TAU_ORDER for number in range(19)]
    return (jnp.stack(f_posts), jnp.stack(g_posts))


def collide_lists(f_pop, g_pop, order_field, laplace, slopes):
    density = f_pop[0]
    for number in range(1, 19):
        density = density + f_pop[number]
    chemical = (
        BULK_COEF * (order_field * order_field * order_field - order_field) - STIFFNESS * laplace
    )
    forces = [chemical * slope for slope in slopes]
    moments = []
    for axis_id in range(3):
        moment = jnp.zeros_like(density)
        for number in range(19):
            comp = VELOCITIES[number][axis_id]
            if comp != 0:
                moment = moment + comp * f_pop[number]
        moments.append(moment)
    flows = [(moments[axis_id] + 0.5 * forces[axis_id]) / density for axis_id in range(3)]
    speed_sq = flows[0] * flows[0] + flows[1] * flows[1] + flows[2] * flows[2]
    flow_force = flows[0] * forces[0] + flows[1] * forces[1] + flows[2] * forces[2]
    f_posts = []
    g_eqs = []
    for number in range(19):
        weight = lattice_weight(number)
        proj_flow = along(number, flows, density)
        proj_force = along(number, forces, density)
        shape_term = 3.0 * proj_flow + 4.5 * proj_flow * proj_flow - 1.5 * speed_sq
        f_eq = weight * density * (1.0 + shape_term)
        source = (
            (1.0 - 0.5 / TAU_FLUID)
            * weight
            * (3.0 * (proj_force - flow_force) + 9.0 * proj_flow * proj_force)
        )
        f_posts.append(f_pop[number] - (f_pop[number] - f_eq) / TAU_FLUID + source)
        g_eqs.append(weight * (3.0 * chemical + order_field * shape_term))
    rest_eq = order_field
    for number in range(1, 19):
        rest_eq = rest_eq - g_eqs[number]
    g_eqs[0] = rest_eq
    g_posts = [g_pop[number] - (g_pop[number] - g_eqs[number]) / TAU_ORDER for number in range(19)]
    return (f_posts, g_posts)


def collide_kernel(f_ref, g_ref, nb_ref, post_ref):
    pops = f_ref.shape[0]
    for x in range(f_ref.shape[1]):
        f_planes = [f_ref[n, x] for n in range(pops)]
        g_planes = [g_ref[n, x] for n in range(pops)]
        slopes = [nb_ref[2 + a, x] for a in range(3)]
        f_posts, g_posts = collide_lists(f_planes, g_planes, nb_ref[0, x], nb_ref[1, x], slopes)
        for n in range(pops):
            post_ref[n, x] = f_posts[n]
            post_ref[pops + n, x] = g_posts[n]


def stream_kernel(post_ref, xlow_ref, xhigh_ref, hym_ref, hyp_ref, col_ref, f_ref, g_ref):
    pops = f_ref.shape[0]
    nx, ny, nz = f_ref.shape[1:]
    row = lax.broadcasted_iota(jnp.int32, (ny, nz), 0)
    lane = lax.broadcasted_iota(jnp.int32, (ny, nz), 1)
    vel = [VELOCITIES[n % pops] for n in range(2 * pops)]
    x_up = [n for n in range(2 * pops) if vel[n][0] == 1]
    x_dn = [n for n in range(2 * pops) if vel[n][0] == -1]
    y_up = [n for n in range(2 * pops) if vel[n][1] == 1]
    y_dn = [n for n in range(2 * pops) if vel[n][1] == -1]
    z_any = [n for n in range(2 * pops) if vel[n][2] != 0]
    for n in range(2 * pops):
        cx, cy, cz = vel[n]
        out = f_ref if n < pops else g_ref
        for x in range(nx):
            src = x - cx
            if src < 0:
                tile = xlow_ref[x_up.index(n)]
            elif src >= nx:
                tile = xhigh_ref[x_dn.index(n)]
            else:
                tile = post_ref[n, src]
                if cy == 1:
                    edge = jnp.broadcast_to(hym_ref[y_up.index(n), pl.ds(src, 1), :], (ny, nz))
                    tile = jnp.where(row == 0, edge, pltpu.roll(tile, 1, 0))
                elif cy == -1:
                    edge = jnp.broadcast_to(hyp_ref[y_dn.index(n), pl.ds(src, 1), :], (ny, nz))
                    tile = jnp.where(row == ny - 1, edge, pltpu.roll(tile, ny - 1, 0))
            if 0 <= src < nx and cz == 1:
                tile = jnp.where(lane == 0, col_ref[z_any.index(n), x], pltpu.roll(tile, 1, 1))
            elif 0 <= src < nx and cz == -1:
                tile = jnp.where(lane == nz - 1, col_ref[z_any.index(n), x], pltpu.roll(tile, nz - 1, 1))
            out[n % pops, x] = tile


def exchange(sends):
    sizes = [lax.axis_size(a) for a in AXES]
    groups = {}
    order = []
    for index, (value, offset) in enumerate(sends):
        key = (tuple(o % n for o, n in zip(offset, sizes)), value.shape[1:])
        if key not in groups:
            groups[key] = []
            order.append(key)
        groups[key].append(index)
    results = [None] * len(sends)
    for key in order:
        members = groups[key]
        offset = key[0]
        pairs = []
        for i in range(sizes[0]):
            for j in range(sizes[1]):
                for k in range(sizes[2]):
                    src = (i * sizes[1] + j) * sizes[2] + k
                    ti, tj, tk = [(c + o) % n for c, o, n in zip((i, j, k), offset, sizes)]
                    pairs.append((src, (ti * sizes[1] + tj) * sizes[2] + tk))
        payload = [sends[m][0] for m in members]
        joined = payload[0] if len(payload) == 1 else jnp.concatenate(payload, axis=0)
        got = lax.ppermute(joined, AXES, pairs)
        start = 0
        for m in members:
            count = sends[m][0].shape[0]
            results[m] = got[start : start + count]
            start += count
    return results


def local(f_pop, g_pop, displacement):
    shift = displacement[0]
    nx, ny, nz = (f_pop.shape[1], f_pop.shape[2], f_pop.shape[3])
    q = SHIFT_MIN // ny
    assert SHIFT_MAX // ny == q and SHIFT_MIN % ny != 0
    rem = shift - q * ny

    phi = jnp.sum(g_pop, axis=0)
    up1, dn1, pzm, pzp = exchange(
        [
            (jnp.concatenate([phi[:, -1], phi[-1]]), (0, 1, 0)),
            (jnp.concatenate([phi[:, 0], phi[0]]), (0, -1, 0)),
            (phi[:, :, -1][None], (0, 0, 1)),
            (phi[:, :, 0][None], (0, 0, -1)),
        ]
    )
    low_pair, high_pair = exchange(
        [
            (jnp.concatenate([up1[nx:], phi[-1]]), (1, q, 0)),
            (jnp.concatenate([phi[0], dn1[nx:]]), (-1, -q, 0)),
        ]
    )
    low = lax.dynamic_slice_in_dim(low_pair, ny - rem, ny, 0)[None]
    high = lax.dynamic_slice_in_dim(high_pair, rem, ny, 0)[None]
    neigh_xm = jnp.concatenate([low, phi[:-1]], axis=0)
    neigh_xp = jnp.concatenate([phi[1:], high], axis=0)
    neigh_ym = jnp.concatenate([up1[:nx][:, None], phi[:, :-1]], axis=1)
    neigh_yp = jnp.concatenate([phi[:, 1:], dn1[:nx][:, None]], axis=1)
    neigh_zm = jnp.concatenate([pzm[0][:, :, None], phi[:, :, :-1]], axis=2)
    neigh_zp = jnp.concatenate([phi[:, :, 1:], pzp[0][:, :, None]], axis=2)
    laplace = neigh_xm + neigh_xp + neigh_ym + neigh_yp + neigh_zm + neigh_zp - 6.0 * phi
    slopes = [0.5 * (neigh_xp - neigh_xm), 0.5 * (neigh_yp - neigh_ym), 0.5 * (neigh_zp - neigh_zm)]
    nb = jnp.stack([phi, laplace] + slopes)
    post = pl.pallas_call(
        collide_kernel,
        out_shape=jax.ShapeDtypeStruct((2 * f_pop.shape[0], nx, ny, nz), jnp.float32),
        interpret=INTERPRET,
    )(f_pop, g_pop, nb)

    vel = [VELOCITIES[n % 19] for n in range(38)]

    def pick(cond, among=range(38)):
        return [n for n in among if cond(vel[n])]

    x_up = pick(lambda c: c[0] == 1)
    x_dn = pick(lambda c: c[0] == -1)
    y_up = pick(lambda c: c[1] == 1)
    y_dn = pick(lambda c: c[1] == -1)
    z_up = pick(lambda c: c[2] == 1)
    z_dn = pick(lambda c: c[2] == -1)
    xz_up = pick(lambda c: c[2] != 0, x_up)
    xz_dn = pick(lambda c: c[2] != 0, x_dn)
    yz_up = pick(lambda c: c[2] != 0, y_up)
    yz_dn = pick(lambda c: c[2] != 0, y_dn)

    def rows(idx):
        return jnp.stack([post[n] for n in idx])

    hz_m, hz_p = exchange(
        [(rows(z_up)[:, :, :, -1], (0, 0, 1)), (rows(z_dn)[:, :, :, 0], (0, 0, -1))]
    )

    def zhalo(n):
        return hz_m[z_up.index(n)] if vel[n][2] == 1 else hz_p[z_dn.index(n)]

    def lanes(a):
        return jnp.pad(a, ((0, 0), (0, nz - a.shape[1])))

    def packed(face, extra):
        return jnp.concatenate([face.reshape(-1, nz), lanes(jnp.stack(extra))], axis=0)

    send_up = packed(rows(x_up)[:, -1], [zhalo(n)[-1] for n in xz_up])
    send_dn = packed(rows(x_dn)[:, 0], [zhalo(n)[0] for n in xz_dn])
    send_yu = packed(rows(y_up)[:, :, -1], [zhalo(n)[:, -1] for n in yz_up])
    send_yd = packed(rows(y_dn)[:, :, 0], [zhalo(n)[:, 0] for n in yz_dn])
    n_yu, n_yd = send_yu.shape[0], send_yd.shape[0]
    up2, dn2 = exchange(
        [
            (jnp.concatenate([send_yu, send_up]), (0, 1, 0)),
            (jnp.concatenate([send_yd, send_dn]), (0, -1, 0)),
        ]
    )
    hy_m, hy_p = up2[:n_yu], dn2[:n_yd]

    def unpack_x(got, count):
        return got[: count * ny].reshape(count, ny, nz), got[count * ny :, :ny]

    def unpack_y(got, count):
        return got[: count * nx].reshape(count, nx, nz), got[count * nx :, :nx]

    def by_pop(idx, axis_id, shape):
        return jnp.array([vel[n][axis_id] for n in idx], jnp.int32).reshape(shape)

    def pick_y(win, idx):
        cy = by_pop(idx, 1, (-1, 1, 1))
        return jnp.where(cy == 1, win[:, :ny], jnp.where(cy == -1, win[:, 2:], win[:, 1 : ny + 1]))

    def shift_z(planes, idx, edge_cols, edge_idx):
        cz = by_pop(idx, 2, (-1, 1, 1))
        zero = jnp.zeros((1, ny), planes.dtype)
        col = jnp.concatenate([edge_cols, zero])[
            jnp.array([edge_idx.index(n) if n in edge_idx else len(edge_idx) for n in idx])
        ][:, :, None]
        return jnp.where(
            cz == 1,
            jnp.concatenate([col, planes[:, :, :-1]], axis=2),
            jnp.where(cz == -1, jnp.concatenate([planes[:, :, 1:], col], axis=2), planes),
        )

    def window(first, second, idx, edge_idx, start):
        count = len(idx)
        pa, ca = unpack_x(first, count)
        pb, cb = unpack_x(second, count)
        planes = lax.dynamic_slice_in_dim(jnp.concatenate([pa, pb], axis=1), start - 1, ny + 2, 1)
        cols = lax.dynamic_slice_in_dim(jnp.concatenate([ca, cb], axis=1), start, ny, 1)
        return shift_z(pick_y(planes, idx), idx, cols, edge_idx).reshape(-1, nz)

    low2, high2 = exchange(
        [
            (window(up2[n_yu:], send_up, x_up, xz_up, ny - rem), (1, q, 0)),
            (window(send_dn, dn2[n_yd:], x_dn, xz_dn, rem), (-1, -q, 0)),
        ]
    )
    hy_m, cy_m = unpack_y(hy_m, len(y_up))
    hy_p, cy_p = unpack_y(hy_p, len(y_dn))

    xlow = low2.reshape(len(x_up), ny, nz)
    xhigh = high2.reshape(len(x_dn), ny, nz)
    z_any = pick(lambda c: c[2] != 0)
    zh = jnp.concatenate([hz_m, hz_p])[jnp.array([z_up.index(n) if vel[n][2] == 1 else len(z_up) + z_dn.index(n) for n in z_any])]

    def spread(values, idx):
        zero = jnp.zeros((1,) + values.shape[1:], values.dtype)
        both = jnp.concatenate([values, zero])
        return both[jnp.array([idx.index(n) if n in idx else len(idx) for n in z_any])]

    corner_m = spread(cy_m, yz_up)[:, :, None]
    corner_p = spread(cy_p, yz_dn)[:, :, None]
    cy = by_pop(z_any, 1, (-1, 1, 1))
    cx = by_pop(z_any, 0, (-1, 1, 1))
    down = jnp.concatenate([corner_m, zh[:, :, :-1]], axis=2)
    up = jnp.concatenate([zh[:, :, 1:], corner_p], axis=2)
    zy = jnp.where(cy == 1, down, jnp.where(cy == -1, up, zh))
    edge_low = jnp.zeros((len(z_any), 1, ny), jnp.float32)
    edge_high = edge_low
    cols = jnp.where(
        cx == 1,
        jnp.concatenate([edge_low, zy[:, :-1]], axis=1),
        jnp.where(cx == -1, jnp.concatenate([zy[:, 1:], edge_high], axis=1), zy),
    )
    cols = jnp.broadcast_to(cols[:, :, :, None], (len(z_any), nx, ny, nz))
    pops = f_pop.shape[0]
    f_new, g_new = pl.pallas_call(
        stream_kernel,
        out_shape=(
            jax.ShapeDtypeStruct((pops, nx, ny, nz), jnp.float32),
            jax.ShapeDtypeStruct((pops, nx, ny, nz), jnp.float32),
        ),
        interpret=INTERPRET,
    )(post, xlow, xhigh, hy_m, hy_p, cols)
    return (f_new, g_new)


def solution(mesh):
    return jax.shard_map(
        local,
        mesh=mesh,
        in_specs=(P(None, "gx", "gy", "gz"), P(None, "gx", "gy", "gz"), P()),
        out_specs=(P(None, "gx", "gy", "gz"), P(None, "gx", "gy", "gz")),
        check_vma=False,
    )
```

```python
import jax
import jax.numpy as jnp
from jax import lax
from jax.sharding import PartitionSpec as P
from jax.experimental import pallas as pl
from jax.experimental.pallas import tpu as pltpu

VELOCITIES = [
    (0, 0, 0),
    (1, 0, 0),
    (1, 1, 0),
    (1, -1, 0),
    (1, 0, 1),
    (1, 0, -1),
    (-1, 0, 0),
    (-1, -1, 0),
    (-1, 1, 0),
    (-1, 0, -1),
    (-1, 0, 1),
    (0, 1, 0),
    (0, -1, 0),
    (0, 0, 1),
    (0, 0, -1),
    (0, 1, 1),
    (0, -1, -1),
    (0, 1, -1),
    (0, -1, 1),
]
BULK_COEF = 0.5
STIFFNESS = 0.5
TAU_FLUID = 0.8
TAU_ORDER = 0.9
SHIFT_MIN = 33
SHIFT_MAX = 47
AXES = ("gx", "gy", "gz")
INTERPRET = False


def lattice_weight(number):
    steps_sq = sum((abs(comp) for comp in VELOCITIES[number]))
    if steps_sq == 0:
        return 1.0 / 3.0
    if steps_sq == 1:
        return 1.0 / 18.0
    return 1.0 / 36.0


def along(number, values, base):
    result = jnp.zeros_like(base)
    for axis_id in range(3):
        comp = VELOCITIES[number][axis_id]
        if comp != 0:
            result = result + comp * values[axis_id]
    return result


def collide(f_pop, g_pop, order_field, laplace, slopes):
    density = jnp.sum(f_pop, axis=0)
    chemical = (
        BULK_COEF * (order_field * order_field * order_field - order_field) - STIFFNESS * laplace
    )
    forces = [chemical * slope for slope in slopes]
    moments = []
    for axis_id in range(3):
        moment = jnp.zeros_like(density)
        for number in range(19):
            comp = VELOCITIES[number][axis_id]
            if comp != 0:
                moment = moment + comp * f_pop[number]
        moments.append(moment)
    flows = [(moments[axis_id] + 0.5 * forces[axis_id]) / density for axis_id in range(3)]
    speed_sq = flows[0] * flows[0] + flows[1] * flows[1] + flows[2] * flows[2]
    flow_force = flows[0] * forces[0] + flows[1] * forces[1] + flows[2] * forces[2]
    f_posts = []
    g_eqs = []
    for number in range(19):
        weight = lattice_weight(number)
        proj_flow = along(number, flows, density)
        proj_force = along(number, forces, density)
        shape_term = 3.0 * proj_flow + 4.5 * proj_flow * proj_flow - 1.5 * speed_sq
        f_eq = weight * density * (1.0 + shape_term)
        source = (
            (1.0 - 0.5 / TAU_FLUID)
            * weight
            * (3.0 * (proj_force - flow_force) + 9.0 * proj_flow * proj_force)
        )
        f_posts.append(f_pop[number] - (f_pop[number] - f_eq) / TAU_FLUID + source)
        g_eqs.append(weight * (3.0 * chemical + order_field * shape_term))
    rest_eq = order_field
    for number in range(1, 19):
        rest_eq = rest_eq - g_eqs[number]
    g_eqs[0] = rest_eq
    g_posts = [g_pop[number] - (g_pop[number] - g_eqs[number]) / TAU_ORDER for number in range(19)]
    return (jnp.stack(f_posts), jnp.stack(g_posts))


def collide_lists(f_pop, g_pop, order_field, laplace, slopes):
    density = f_pop[0]
    for number in range(1, 19):
        density = density + f_pop[number]
    chemical = (
        BULK_COEF * (order_field * order_field * order_field - order_field) - STIFFNESS * laplace
    )
    forces = [chemical * slope for slope in slopes]
    moments = []
    for axis_id in range(3):
        moment = jnp.zeros_like(density)
        for number in range(19):
            comp = VELOCITIES[number][axis_id]
            if comp != 0:
                moment = moment + comp * f_pop[number]
        moments.append(moment)
    flows = [(moments[axis_id] + 0.5 * forces[axis_id]) / density for axis_id in range(3)]
    speed_sq = flows[0] * flows[0] + flows[1] * flows[1] + flows[2] * flows[2]
    flow_force = flows[0] * forces[0] + flows[1] * forces[1] + flows[2] * forces[2]
    f_posts = []
    g_eqs = []
    for number in range(19):
        weight = lattice_weight(number)
        proj_flow = along(number, flows, density)
        proj_force = along(number, forces, density)
        shape_term = 3.0 * proj_flow + 4.5 * proj_flow * proj_flow - 1.5 * speed_sq
        f_eq = weight * density * (1.0 + shape_term)
        source = (
            (1.0 - 0.5 / TAU_FLUID)
            * weight
            * (3.0 * (proj_force - flow_force) + 9.0 * proj_flow * proj_force)
        )
        f_posts.append(f_pop[number] - (f_pop[number] - f_eq) / TAU_FLUID + source)
        g_eqs.append(weight * (3.0 * chemical + order_field * shape_term))
    rest_eq = order_field
    for number in range(1, 19):
        rest_eq = rest_eq - g_eqs[number]
    g_eqs[0] = rest_eq
    g_posts = [g_pop[number] - (g_pop[number] - g_eqs[number]) / TAU_ORDER for number in range(19)]
    return (f_posts, g_posts)


def pop_groups(pops):
    vel = [VELOCITIES[n % pops] for n in range(2 * pops)]
    groups = {
        name: [n for n in range(2 * pops) if vel[n][axis_id] == sign]
        for name, axis_id, sign in (
            ("x_up", 0, 1), ("x_dn", 0, -1), ("y_up", 1, 1), ("y_dn", 1, -1), ("z_up", 2, 1), ("z_dn", 2, -1)
        )
    }
    order = groups["z_up"] + groups["z_dn"] + [n for n in range(2 * pops) if vel[n][2] == 0]
    slot = {n: i for i, n in enumerate(order)}
    return vel, groups, slot


def collide_kernel(f_ref, g_ref, nb_ref, post_ref, xu_ref, xd_ref, yu_ref, yd_ref):
    pops = f_ref.shape[0]
    nx, ny = f_ref.shape[1], f_ref.shape[2]
    vel, groups, slot = pop_groups(pops)
    for x in range(nx):
        f_planes = [f_ref[n, x] for n in range(pops)]
        g_planes = [g_ref[n, x] for n in range(pops)]
        slopes = [nb_ref[2 + a, x] for a in range(3)]
        f_posts, g_posts = collide_lists(f_planes, g_planes, nb_ref[0, x], nb_ref[1, x], slopes)
        planes = f_posts + g_posts
        for n in range(2 * pops):
            post_ref[slot[n], x] = planes[n]
        if x == nx - 1:
            for k, n in enumerate(groups["x_up"]):
                xu_ref[k] = planes[n]
        if x == 0:
            for k, n in enumerate(groups["x_dn"]):
                xd_ref[k] = planes[n]
        for k, n in enumerate(groups["y_up"]):
            yu_ref[k, pl.ds(x, 1), :] = planes[n][ny - 1 : ny, :]
        for k, n in enumerate(groups["y_dn"]):
            yd_ref[k, pl.ds(x, 1), :] = planes[n][0:1, :]


def stream_kernel(post_ref, xlow_ref, xhigh_ref, hym_ref, hyp_ref, col_ref, f_ref, g_ref):
    pops = f_ref.shape[0]
    nx, ny, nz = f_ref.shape[1:]
    row = lax.broadcasted_iota(jnp.int32, (ny, nz), 0)
    lane = lax.broadcasted_iota(jnp.int32, (ny, nz), 1)
    vel = [VELOCITIES[n % pops] for n in range(2 * pops)]
    x_up = [n for n in range(2 * pops) if vel[n][0] == 1]
    x_dn = [n for n in range(2 * pops) if vel[n][0] == -1]
    y_up = [n for n in range(2 * pops) if vel[n][1] == 1]
    y_dn = [n for n in range(2 * pops) if vel[n][1] == -1]
    z_any = [n for n in range(2 * pops) if vel[n][2] != 0]
    for n in range(2 * pops):
        cx, cy, cz = vel[n]
        out = f_ref if n < pops else g_ref
        for x in range(nx):
            src = x - cx
            if src < 0:
                tile = xlow_ref[x_up.index(n)]
            elif src >= nx:
                tile = xhigh_ref[x_dn.index(n)]
            else:
                tile = post_ref[pop_groups(pops)[2][n], src]
                if cy == 1:
                    edge = jnp.broadcast_to(hym_ref[y_up.index(n), pl.ds(src, 1), :], (ny, nz))
                    tile = jnp.where(row == 0, edge, pltpu.roll(tile, 1, 0))
                elif cy == -1:
                    edge = jnp.broadcast_to(hyp_ref[y_dn.index(n), pl.ds(src, 1), :], (ny, nz))
                    tile = jnp.where(row == ny - 1, edge, pltpu.roll(tile, ny - 1, 0))
            if 0 <= src < nx and cz == 1:
                tile = jnp.where(lane == 0, col_ref[z_any.index(n), x], pltpu.roll(tile, 1, 1))
            elif 0 <= src < nx and cz == -1:
                tile = jnp.where(lane == nz - 1, col_ref[z_any.index(n), x], pltpu.roll(tile, nz - 1, 1))
            out[n % pops, x] = tile


def exchange(sends):
    sizes = [lax.axis_size(a) for a in AXES]
    groups = {}
    order = []
    for index, (value, offset) in enumerate(sends):
        key = (tuple(o % n for o, n in zip(offset, sizes)), value.shape[1:])
        if key not in groups:
            groups[key] = []
            order.append(key)
        groups[key].append(index)
    results = [None] * len(sends)
    for key in order:
        members = groups[key]
        offset = key[0]
        pairs = []
        for i in range(sizes[0]):
            for j in range(sizes[1]):
                for k in range(sizes[2]):
                    src = (i * sizes[1] + j) * sizes[2] + k
                    ti, tj, tk = [(c + o) % n for c, o, n in zip((i, j, k), offset, sizes)]
                    pairs.append((src, (ti * sizes[1] + tj) * sizes[2] + tk))
        payload = [sends[m][0] for m in members]
        joined = payload[0] if len(payload) == 1 else jnp.concatenate(payload, axis=0)
        got = lax.ppermute(joined, AXES, pairs)
        start = 0
        for m in members:
            count = sends[m][0].shape[0]
            results[m] = got[start : start + count]
            start += count
    return results


def local(f_pop, g_pop, displacement):
    shift = displacement[0]
    nx, ny, nz = (f_pop.shape[1], f_pop.shape[2], f_pop.shape[3])
    q = SHIFT_MIN // ny
    assert SHIFT_MAX // ny == q and SHIFT_MIN % ny != 0
    rem = shift - q * ny

    phi = jnp.sum(g_pop, axis=0)
    up1, dn1, pzm, pzp = exchange(
        [
            (jnp.concatenate([phi[:, -1], phi[-1]]), (0, 1, 0)),
            (jnp.concatenate([phi[:, 0], phi[0]]), (0, -1, 0)),
            (phi[:, :, -1][None], (0, 0, 1)),
            (phi[:, :, 0][None], (0, 0, -1)),
        ]
    )
    low_pair, high_pair = exchange(
        [
            (jnp.concatenate([up1[nx:], phi[-1]]), (1, q, 0)),
            (jnp.concatenate([phi[0], dn1[nx:]]), (-1, -q, 0)),
        ]
    )
    low = lax.dynamic_slice_in_dim(low_pair, ny - rem, ny, 0)[None]
    high = lax.dynamic_slice_in_dim(high_pair, rem, ny, 0)[None]
    neigh_xm = jnp.concatenate([low, phi[:-1]], axis=0)
    neigh_xp = jnp.concatenate([phi[1:], high], axis=0)
    neigh_ym = jnp.concatenate([up1[:nx][:, None], phi[:, :-1]], axis=1)
    neigh_yp = jnp.concatenate([phi[:, 1:], dn1[:nx][:, None]], axis=1)
    neigh_zm = jnp.concatenate([pzm[0][:, :, None], phi[:, :, :-1]], axis=2)
    neigh_zp = jnp.concatenate([phi[:, :, 1:], pzp[0][:, :, None]], axis=2)
    laplace = neigh_xm + neigh_xp + neigh_ym + neigh_yp + neigh_zm + neigh_zp - 6.0 * phi
    slopes = [0.5 * (neigh_xp - neigh_xm), 0.5 * (neigh_yp - neigh_ym), 0.5 * (neigh_zp - neigh_zm)]
    nb = jnp.stack([phi, laplace] + slopes)
    pops = f_pop.shape[0]
    _, groups, slot = pop_groups(pops)
    n_xu, n_xd, n_yu, n_yd = (len(groups[k]) for k in ("x_up", "x_dn", "y_up", "y_dn"))
    post, face_xu, face_xd, face_yu, face_yd = pl.pallas_call(
        collide_kernel,
        out_shape=(
            jax.ShapeDtypeStruct((2 * pops, nx, ny, nz), jnp.float32),
            jax.ShapeDtypeStruct((n_xu, ny, nz), jnp.float32),
            jax.ShapeDtypeStruct((n_xd, ny, nz), jnp.float32),
            jax.ShapeDtypeStruct((n_yu, nx, nz), jnp.float32),
            jax.ShapeDtypeStruct((n_yd, nx, nz), jnp.float32),
        ),
        interpret=INTERPRET,
    )(f_pop, g_pop, nb)

    vel = [VELOCITIES[n % 19] for n in range(38)]

    def pick(cond, among=range(38)):
        return [n for n in among if cond(vel[n])]

    x_up = pick(lambda c: c[0] == 1)
    x_dn = pick(lambda c: c[0] == -1)
    y_up = pick(lambda c: c[1] == 1)
    y_dn = pick(lambda c: c[1] == -1)
    z_up = pick(lambda c: c[2] == 1)
    z_dn = pick(lambda c: c[2] == -1)
    xz_up = pick(lambda c: c[2] != 0, x_up)
    xz_dn = pick(lambda c: c[2] != 0, x_dn)
    yz_up = pick(lambda c: c[2] != 0, y_up)
    yz_dn = pick(lambda c: c[2] != 0, y_dn)

    hz_m, hz_p = exchange(
        [
            (post[: len(z_up), :, :, -1], (0, 0, 1)),
            (post[len(z_up) : len(z_up) + len(z_dn), :, :, 0], (0, 0, -1)),
        ]
    )

    def zhalo(n):
        return hz_m[z_up.index(n)] if vel[n][2] == 1 else hz_p[z_dn.index(n)]

    def lanes(a):
        return jnp.pad(a, ((0, 0), (0, nz - a.shape[1])))

    def packed(face, extra):
        return jnp.concatenate([face.reshape(-1, nz), lanes(jnp.stack(extra))], axis=0)

    send_up = packed(face_xu, [zhalo(n)[-1] for n in xz_up])
    send_dn = packed(face_xd, [zhalo(n)[0] for n in xz_dn])
    send_yu = packed(face_yu, [zhalo(n)[:, -1] for n in yz_up])
    send_yd = packed(face_yd, [zhalo(n)[:, 0] for n in yz_dn])
    n_yu, n_yd = send_yu.shape[0], send_yd.shape[0]
    up2, dn2 = exchange(
        [
            (jnp.concatenate([send_yu, send_up]), (0, 1, 0)),
            (jnp.concatenate([send_yd, send_dn]), (0, -1, 0)),
        ]
    )
    hy_m, hy_p = up2[:n_yu], dn2[:n_yd]

    def unpack_x(got, count):
        return got[: count * ny].reshape(count, ny, nz), got[count * ny :, :ny]

    def unpack_y(got, count):
        return got[: count * nx].reshape(count, nx, nz), got[count * nx :, :nx]

    def by_pop(idx, axis_id, shape):
        return jnp.array([vel[n][axis_id] for n in idx], jnp.int32).reshape(shape)

    def pick_y(win, idx):
        cy = by_pop(idx, 1, (-1, 1, 1))
        return jnp.where(cy == 1, win[:, :ny], jnp.where(cy == -1, win[:, 2:], win[:, 1 : ny + 1]))

    def shift_z(planes, idx, edge_cols, edge_idx):
        cz = by_pop(idx, 2, (-1, 1, 1))
        zero = jnp.zeros((1, ny), planes.dtype)
        col = jnp.concatenate([edge_cols, zero])[
            jnp.array([edge_idx.index(n) if n in edge_idx else len(edge_idx) for n in idx])
        ][:, :, None]
        return jnp.where(
            cz == 1,
            jnp.concatenate([col, planes[:, :, :-1]], axis=2),
            jnp.where(cz == -1, jnp.concatenate([planes[:, :, 1:], col], axis=2), planes),
        )

    def window(first, second, idx, edge_idx, start):
        count = len(idx)
        pa, ca = unpack_x(first, count)
        pb, cb = unpack_x(second, count)
        planes = lax.dynamic_slice_in_dim(jnp.concatenate([pa, pb], axis=1), start - 1, ny + 2, 1)
        cols = lax.dynamic_slice_in_dim(jnp.concatenate([ca, cb], axis=1), start, ny, 1)
        return shift_z(pick_y(planes, idx), idx, cols, edge_idx).reshape(-1, nz)

    low2, high2 = exchange(
        [
            (window(up2[n_yu:], send_up, x_up, xz_up, ny - rem), (1, q, 0)),
            (window(send_dn, dn2[n_yd:], x_dn, xz_dn, rem), (-1, -q, 0)),
        ]
    )
    hy_m, cy_m = unpack_y(hy_m, len(y_up))
    hy_p, cy_p = unpack_y(hy_p, len(y_dn))

    xlow = low2.reshape(len(x_up), ny, nz)
    xhigh = high2.reshape(len(x_dn), ny, nz)
    z_any = pick(lambda c: c[2] != 0)
    zh = jnp.concatenate([hz_m, hz_p])[jnp.array([z_up.index(n) if vel[n][2] == 1 else len(z_up) + z_dn.index(n) for n in z_any])]

    def spread(values, idx):
        zero = jnp.zeros((1,) + values.shape[1:], values.dtype)
        both = jnp.concatenate([values, zero])
        return both[jnp.array([idx.index(n) if n in idx else len(idx) for n in z_any])]

    corner_m = spread(cy_m, yz_up)[:, :, None]
    corner_p = spread(cy_p, yz_dn)[:, :, None]
    cy = by_pop(z_any, 1, (-1, 1, 1))
    cx = by_pop(z_any, 0, (-1, 1, 1))
    down = jnp.concatenate([corner_m, zh[:, :, :-1]], axis=2)
    up = jnp.concatenate([zh[:, :, 1:], corner_p], axis=2)
    zy = jnp.where(cy == 1, down, jnp.where(cy == -1, up, zh))
    edge_low = jnp.zeros((len(z_any), 1, ny), jnp.float32)
    edge_high = edge_low
    cols = jnp.where(
        cx == 1,
        jnp.concatenate([edge_low, zy[:, :-1]], axis=1),
        jnp.where(cx == -1, jnp.concatenate([zy[:, 1:], edge_high], axis=1), zy),
    )
    cols = jnp.broadcast_to(cols[:, :, :, None], (len(z_any), nx, ny, nz))
    pops = f_pop.shape[0]
    f_new, g_new = pl.pallas_call(
        stream_kernel,
        out_shape=(
            jax.ShapeDtypeStruct((pops, nx, ny, nz), jnp.float32),
            jax.ShapeDtypeStruct((pops, nx, ny, nz), jnp.float32),
        ),
        interpret=INTERPRET,
    )(post, xlow, xhigh, hy_m, hy_p, cols)
    return (f_new, g_new)


def solution(mesh):
    return jax.shard_map(
        local,
        mesh=mesh,
        in_specs=(P(None, "gx", "gy", "gz"), P(None, "gx", "gy", "gz"), P()),
        out_specs=(P(None, "gx", "gy", "gz"), P(None, "gx", "gy", "gz")),
        check_vma=False,
    )
```

```python
import jax
import jax.numpy as jnp
from jax import lax
from jax.sharding import PartitionSpec as P
from jax.experimental import pallas as pl
from jax.experimental.pallas import tpu as pltpu

VELOCITIES = [
    (0, 0, 0),
    (1, 0, 0),
    (1, 1, 0),
    (1, -1, 0),
    (1, 0, 1),
    (1, 0, -1),
    (-1, 0, 0),
    (-1, -1, 0),
    (-1, 1, 0),
    (-1, 0, -1),
    (-1, 0, 1),
    (0, 1, 0),
    (0, -1, 0),
    (0, 0, 1),
    (0, 0, -1),
    (0, 1, 1),
    (0, -1, -1),
    (0, 1, -1),
    (0, -1, 1),
]
BULK_COEF = 0.5
STIFFNESS = 0.5
TAU_FLUID = 0.8
TAU_ORDER = 0.9
SHIFT_MIN = 33
SHIFT_MAX = 47
AXES = ("gx", "gy", "gz")
INTERPRET = False


def lattice_weight(number):
    steps_sq = sum((abs(comp) for comp in VELOCITIES[number]))
    if steps_sq == 0:
        return 1.0 / 3.0
    if steps_sq == 1:
        return 1.0 / 18.0
    return 1.0 / 36.0


def along(number, values, base):
    result = jnp.zeros_like(base)
    for axis_id in range(3):
        comp = VELOCITIES[number][axis_id]
        if comp != 0:
            result = result + comp * values[axis_id]
    return result


def collide(f_pop, g_pop, order_field, laplace, slopes):
    density = jnp.sum(f_pop, axis=0)
    chemical = (
        BULK_COEF * (order_field * order_field * order_field - order_field) - STIFFNESS * laplace
    )
    forces = [chemical * slope for slope in slopes]
    moments = []
    for axis_id in range(3):
        moment = jnp.zeros_like(density)
        for number in range(19):
            comp = VELOCITIES[number][axis_id]
            if comp != 0:
                moment = moment + comp * f_pop[number]
        moments.append(moment)
    flows = [(moments[axis_id] + 0.5 * forces[axis_id]) / density for axis_id in range(3)]
    speed_sq = flows[0] * flows[0] + flows[1] * flows[1] + flows[2] * flows[2]
    flow_force = flows[0] * forces[0] + flows[1] * forces[1] + flows[2] * forces[2]
    f_posts = []
    g_eqs = []
    for number in range(19):
        weight = lattice_weight(number)
        proj_flow = along(number, flows, density)
        proj_force = along(number, forces, density)
        shape_term = 3.0 * proj_flow + 4.5 * proj_flow * proj_flow - 1.5 * speed_sq
        f_eq = weight * density * (1.0 + shape_term)
        source = (
            (1.0 - 0.5 / TAU_FLUID)
            * weight
            * (3.0 * (proj_force - flow_force) + 9.0 * proj_flow * proj_force)
        )
        f_posts.append(f_pop[number] - (f_pop[number] - f_eq) / TAU_FLUID + source)
        g_eqs.append(weight * (3.0 * chemical + order_field * shape_term))
    rest_eq = order_field
    for number in range(1, 19):
        rest_eq = rest_eq - g_eqs[number]
    g_eqs[0] = rest_eq
    g_posts = [g_pop[number] - (g_pop[number] - g_eqs[number]) / TAU_ORDER for number in range(19)]
    return (jnp.stack(f_posts), jnp.stack(g_posts))


def collide_lists(f_pop, g_pop, order_field, laplace, slopes):
    density = f_pop[0]
    for number in range(1, 19):
        density = density + f_pop[number]
    chemical = (
        BULK_COEF * (order_field * order_field * order_field - order_field) - STIFFNESS * laplace
    )
    forces = [chemical * slope for slope in slopes]
    moments = []
    for axis_id in range(3):
        moment = jnp.zeros_like(density)
        for number in range(19):
            comp = VELOCITIES[number][axis_id]
            if comp != 0:
                moment = moment + comp * f_pop[number]
        moments.append(moment)
    flows = [(moments[axis_id] + 0.5 * forces[axis_id]) / density for axis_id in range(3)]
    speed_sq = flows[0] * flows[0] + flows[1] * flows[1] + flows[2] * flows[2]
    flow_force = flows[0] * forces[0] + flows[1] * forces[1] + flows[2] * forces[2]
    f_posts = []
    g_eqs = []
    for number in range(19):
        weight = lattice_weight(number)
        proj_flow = along(number, flows, density)
        proj_force = along(number, forces, density)
        shape_term = 3.0 * proj_flow + 4.5 * proj_flow * proj_flow - 1.5 * speed_sq
        f_eq = weight * density * (1.0 + shape_term)
        source = (
            (1.0 - 0.5 / TAU_FLUID)
            * weight
            * (3.0 * (proj_force - flow_force) + 9.0 * proj_flow * proj_force)
        )
        f_posts.append(f_pop[number] - (f_pop[number] - f_eq) / TAU_FLUID + source)
        g_eqs.append(weight * (3.0 * chemical + order_field * shape_term))
    rest_eq = order_field
    for number in range(1, 19):
        rest_eq = rest_eq - g_eqs[number]
    g_eqs[0] = rest_eq
    g_posts = [g_pop[number] - (g_pop[number] - g_eqs[number]) / TAU_ORDER for number in range(19)]
    return (f_posts, g_posts)


def pop_groups(pops):
    vel = [VELOCITIES[n % pops] for n in range(2 * pops)]
    groups = {
        name: [n for n in range(2 * pops) if vel[n][axis_id] == sign]
        for name, axis_id, sign in (
            ("x_up", 0, 1), ("x_dn", 0, -1), ("y_up", 1, 1), ("y_dn", 1, -1), ("z_up", 2, 1), ("z_dn", 2, -1)
        )
    }
    order = groups["z_up"] + groups["z_dn"] + [n for n in range(2 * pops) if vel[n][2] == 0]
    slot = {n: i for i, n in enumerate(order)}
    return vel, groups, slot


def collide_kernel(f_ref, g_ref, nb_ref, post_ref, xu_ref, xd_ref, yu_ref, yd_ref):
    pops = f_ref.shape[0]
    nx, ny = f_ref.shape[1], f_ref.shape[2]
    vel, groups, slot = pop_groups(pops)
    for x in range(nx):
        f_planes = [f_ref[n, x] for n in range(pops)]
        g_planes = [g_ref[n, x] for n in range(pops)]
        slopes = [nb_ref[2 + a, x] for a in range(3)]
        f_posts, g_posts = collide_lists(f_planes, g_planes, nb_ref[0, x], nb_ref[1, x], slopes)
        planes = f_posts + g_posts
        for n in range(2 * pops):
            post_ref[slot[n], x] = planes[n]
        if x == nx - 1:
            for k, n in enumerate(groups["x_up"]):
                xu_ref[k] = planes[n]
        if x == 0:
            for k, n in enumerate(groups["x_dn"]):
                xd_ref[k] = planes[n]
        for k, n in enumerate(groups["y_up"]):
            yu_ref[k, pl.ds(x, 1), :] = planes[n][ny - 1 : ny, :]
        for k, n in enumerate(groups["y_dn"]):
            yd_ref[k, pl.ds(x, 1), :] = planes[n][0:1, :]


def stream_kernel(post_ref, xlow_ref, xhigh_ref, hym_ref, hyp_ref, col_ref, f_ref, g_ref):
    pops = f_ref.shape[0]
    nx, ny, nz = f_ref.shape[1:]
    row = lax.broadcasted_iota(jnp.int32, (ny, nz), 0)
    lane = lax.broadcasted_iota(jnp.int32, (ny, nz), 1)
    vel = [VELOCITIES[n % pops] for n in range(2 * pops)]
    x_up = [n for n in range(2 * pops) if vel[n][0] == 1]
    x_dn = [n for n in range(2 * pops) if vel[n][0] == -1]
    y_up = [n for n in range(2 * pops) if vel[n][1] == 1]
    y_dn = [n for n in range(2 * pops) if vel[n][1] == -1]
    z_any = [n for n in range(2 * pops) if vel[n][2] != 0]
    for n in range(2 * pops):
        cx, cy, cz = vel[n]
        out = f_ref if n < pops else g_ref
        for x in range(nx):
            src = x - cx
            if src < 0:
                tile = xlow_ref[x_up.index(n)]
            elif src >= nx:
                tile = xhigh_ref[x_dn.index(n)]
            else:
                tile = post_ref[pop_groups(pops)[2][n], src]
                if cy == 1:
                    edge = jnp.broadcast_to(hym_ref[pl.ds(y_up.index(n) * nx + src, 1), :], (ny, nz))
                    tile = jnp.where(row == 0, edge, pltpu.roll(tile, 1, 0))
                elif cy == -1:
                    edge = jnp.broadcast_to(hyp_ref[pl.ds(y_dn.index(n) * nx + src, 1), :], (ny, nz))
                    tile = jnp.where(row == ny - 1, edge, pltpu.roll(tile, ny - 1, 0))
            if 0 <= src < nx and cz == 1:
                tile = jnp.where(lane == 0, col_ref[z_any.index(n), x], pltpu.roll(tile, 1, 1))
            elif 0 <= src < nx and cz == -1:
                tile = jnp.where(lane == nz - 1, col_ref[z_any.index(n), x], pltpu.roll(tile, nz - 1, 1))
            out[n % pops, x] = tile


def exchange(sends):
    sizes = [lax.axis_size(a) for a in AXES]
    groups = {}
    order = []
    for index, (value, offset) in enumerate(sends):
        key = (tuple(o % n for o, n in zip(offset, sizes)), value.shape[1:])
        if key not in groups:
            groups[key] = []
            order.append(key)
        groups[key].append(index)
    results = [None] * len(sends)
    for key in order:
        members = groups[key]
        offset = key[0]
        pairs = []
        for i in range(sizes[0]):
            for j in range(sizes[1]):
                for k in range(sizes[2]):
                    src = (i * sizes[1] + j) * sizes[2] + k
                    ti, tj, tk = [(c + o) % n for c, o, n in zip((i, j, k), offset, sizes)]
                    pairs.append((src, (ti * sizes[1] + tj) * sizes[2] + tk))
        payload = [sends[m][0] for m in members]
        joined = payload[0] if len(payload) == 1 else jnp.concatenate(payload, axis=0)
        got = lax.ppermute(joined, AXES, pairs)
        start = 0
        for m in members:
            count = sends[m][0].shape[0]
            results[m] = got[start : start + count]
            start += count
    return results


def local(f_pop, g_pop, displacement):
    shift = displacement[0]
    nx, ny, nz = (f_pop.shape[1], f_pop.shape[2], f_pop.shape[3])
    q = SHIFT_MIN // ny
    assert SHIFT_MAX // ny == q and SHIFT_MIN % ny != 0
    rem = shift - q * ny

    phi = jnp.sum(g_pop, axis=0)
    up1, dn1, pzm, pzp = exchange(
        [
            (jnp.concatenate([phi[:, -1], phi[-1]]), (0, 1, 0)),
            (jnp.concatenate([phi[:, 0], phi[0]]), (0, -1, 0)),
            (phi[:, :, -1][None], (0, 0, 1)),
            (phi[:, :, 0][None], (0, 0, -1)),
        ]
    )
    low_pair, high_pair = exchange(
        [
            (jnp.concatenate([up1[nx:], phi[-1]]), (1, q, 0)),
            (jnp.concatenate([phi[0], dn1[nx:]]), (-1, -q, 0)),
        ]
    )
    low = lax.dynamic_slice_in_dim(low_pair, ny - rem, ny, 0)[None]
    high = lax.dynamic_slice_in_dim(high_pair, rem, ny, 0)[None]
    neigh_xm = jnp.concatenate([low, phi[:-1]], axis=0)
    neigh_xp = jnp.concatenate([phi[1:], high], axis=0)
    neigh_ym = jnp.concatenate([up1[:nx][:, None], phi[:, :-1]], axis=1)
    neigh_yp = jnp.concatenate([phi[:, 1:], dn1[:nx][:, None]], axis=1)
    neigh_zm = jnp.concatenate([pzm[0][:, :, None], phi[:, :, :-1]], axis=2)
    neigh_zp = jnp.concatenate([phi[:, :, 1:], pzp[0][:, :, None]], axis=2)
    laplace = neigh_xm + neigh_xp + neigh_ym + neigh_yp + neigh_zm + neigh_zp - 6.0 * phi
    slopes = [0.5 * (neigh_xp - neigh_xm), 0.5 * (neigh_yp - neigh_ym), 0.5 * (neigh_zp - neigh_zm)]
    nb = jnp.stack([phi, laplace] + slopes)
    pops = f_pop.shape[0]
    _, groups, slot = pop_groups(pops)
    n_xu, n_xd, n_yu, n_yd = (len(groups[k]) for k in ("x_up", "x_dn", "y_up", "y_dn"))
    post, face_xu, face_xd, face_yu, face_yd = pl.pallas_call(
        collide_kernel,
        out_shape=(
            jax.ShapeDtypeStruct((2 * pops, nx, ny, nz), jnp.float32),
            jax.ShapeDtypeStruct((n_xu, ny, nz), jnp.float32),
            jax.ShapeDtypeStruct((n_xd, ny, nz), jnp.float32),
            jax.ShapeDtypeStruct((n_yu, nx, nz), jnp.float32),
            jax.ShapeDtypeStruct((n_yd, nx, nz), jnp.float32),
        ),
        interpret=INTERPRET,
    )(f_pop, g_pop, nb)

    vel = [VELOCITIES[n % 19] for n in range(38)]

    def pick(cond, among=range(38)):
        return [n for n in among if cond(vel[n])]

    x_up = pick(lambda c: c[0] == 1)
    x_dn = pick(lambda c: c[0] == -1)
    y_up = pick(lambda c: c[1] == 1)
    y_dn = pick(lambda c: c[1] == -1)
    z_up = pick(lambda c: c[2] == 1)
    z_dn = pick(lambda c: c[2] == -1)
    xz_up = pick(lambda c: c[2] != 0, x_up)
    xz_dn = pick(lambda c: c[2] != 0, x_dn)
    yz_up = pick(lambda c: c[2] != 0, y_up)
    yz_dn = pick(lambda c: c[2] != 0, y_dn)

    hz_m, hz_p = exchange(
        [
            (post[: len(z_up), :, :, -1], (0, 0, 1)),
            (post[len(z_up) : len(z_up) + len(z_dn), :, :, 0], (0, 0, -1)),
        ]
    )

    def zhalo(n):
        return hz_m[z_up.index(n)] if vel[n][2] == 1 else hz_p[z_dn.index(n)]

    def lanes(a):
        return jnp.pad(a, ((0, 0), (0, nz - a.shape[1])))

    def packed(face, extra):
        return jnp.concatenate([face.reshape(-1, nz), lanes(jnp.stack(extra))], axis=0)

    send_up = packed(face_xu, [zhalo(n)[-1] for n in xz_up])
    send_dn = packed(face_xd, [zhalo(n)[0] for n in xz_dn])
    send_yu = packed(face_yu, [zhalo(n)[:, -1] for n in yz_up])
    send_yd = packed(face_yd, [zhalo(n)[:, 0] for n in yz_dn])
    n_yu, n_yd = send_yu.shape[0], send_yd.shape[0]
    up2, dn2 = exchange(
        [
            (jnp.concatenate([send_yu, send_up]), (0, 1, 0)),
            (jnp.concatenate([send_yd, send_dn]), (0, -1, 0)),
        ]
    )
    hy_m, hy_p = up2[:n_yu], dn2[:n_yd]

    def unpack_x(got, count):
        return got[: count * ny].reshape(count, ny, nz), got[count * ny :, :ny]

    def unpack_y(got, count):
        return got[: count * nx].reshape(count, nx, nz), got[count * nx :, :nx]

    def by_pop(idx, axis_id, shape):
        return jnp.array([vel[n][axis_id] for n in idx], jnp.int32).reshape(shape)

    def pick_y(win, idx):
        cy = by_pop(idx, 1, (-1, 1, 1))
        return jnp.where(cy == 1, win[:, :ny], jnp.where(cy == -1, win[:, 2:], win[:, 1 : ny + 1]))

    def shift_z(planes, idx, edge_cols, edge_idx):
        cz = by_pop(idx, 2, (-1, 1, 1))
        zero = jnp.zeros((1, ny), planes.dtype)
        col = jnp.concatenate([edge_cols, zero])[
            jnp.array([edge_idx.index(n) if n in edge_idx else len(edge_idx) for n in idx])
        ][:, :, None]
        return jnp.where(
            cz == 1,
            jnp.concatenate([col, planes[:, :, :-1]], axis=2),
            jnp.where(cz == -1, jnp.concatenate([planes[:, :, 1:], col], axis=2), planes),
        )

    def window(first, second, idx, edge_idx, start):
        count = len(idx)
        pa, ca = unpack_x(first, count)
        pb, cb = unpack_x(second, count)
        planes = lax.dynamic_slice_in_dim(jnp.concatenate([pa, pb], axis=1), start - 1, ny + 2, 1)
        cols = lax.dynamic_slice_in_dim(jnp.concatenate([ca, cb], axis=1), start, ny, 1)
        return shift_z(pick_y(planes, idx), idx, cols, edge_idx).reshape(-1, nz)

    low2, high2 = exchange(
        [
            (window(up2[n_yu:], send_up, x_up, xz_up, ny - rem), (1, q, 0)),
            (window(send_dn, dn2[n_yd:], x_dn, xz_dn, rem), (-1, -q, 0)),
        ]
    )
    hy_m, cy_m = unpack_y(hy_m, len(y_up))
    hy_p, cy_p = unpack_y(hy_p, len(y_dn))

    xlow = low2.reshape(len(x_up), ny, nz)
    xhigh = high2.reshape(len(x_dn), ny, nz)
    z_any = pick(lambda c: c[2] != 0)
    zh = jnp.concatenate([hz_m, hz_p])[jnp.array([z_up.index(n) if vel[n][2] == 1 else len(z_up) + z_dn.index(n) for n in z_any])]

    def spread(values, idx):
        zero = jnp.zeros((1,) + values.shape[1:], values.dtype)
        both = jnp.concatenate([values, zero])
        return both[jnp.array([idx.index(n) if n in idx else len(idx) for n in z_any])]

    corner_m = spread(cy_m, yz_up)[:, :, None]
    corner_p = spread(cy_p, yz_dn)[:, :, None]
    cy = by_pop(z_any, 1, (-1, 1, 1))
    cx = by_pop(z_any, 0, (-1, 1, 1))
    down = jnp.concatenate([corner_m, zh[:, :, :-1]], axis=2)
    up = jnp.concatenate([zh[:, :, 1:], corner_p], axis=2)
    zy = jnp.where(cy == 1, down, jnp.where(cy == -1, up, zh))
    edge_low = jnp.zeros((len(z_any), 1, ny), jnp.float32)
    edge_high = edge_low
    cols = jnp.where(
        cx == 1,
        jnp.concatenate([edge_low, zy[:, :-1]], axis=1),
        jnp.where(cx == -1, jnp.concatenate([zy[:, 1:], edge_high], axis=1), zy),
    )
    cols = jnp.broadcast_to(cols[:, :, :, None], (len(z_any), nx, ny, nz))
    pops = f_pop.shape[0]
    f_new, g_new = pl.pallas_call(
        stream_kernel,
        out_shape=(
            jax.ShapeDtypeStruct((pops, nx, ny, nz), jnp.float32),
            jax.ShapeDtypeStruct((pops, nx, ny, nz), jnp.float32),
        ),
        interpret=INTERPRET,
    )(post, xlow, xhigh, up2, dn2, cols)
    return (f_new, g_new)


def solution(mesh):
    return jax.shard_map(
        local,
        mesh=mesh,
        in_specs=(P(None, "gx", "gy", "gz"), P(None, "gx", "gy", "gz"), P()),
        out_specs=(P(None, "gx", "gy", "gz"), P(None, "gx", "gy", "gz")),
        check_vma=False,
    )
```

```python
import jax
import jax.numpy as jnp
from jax import lax
from jax.sharding import PartitionSpec as P
from jax.experimental import pallas as pl
from jax.experimental.pallas import tpu as pltpu

VELOCITIES = [
    (0, 0, 0),
    (1, 0, 0),
    (1, 1, 0),
    (1, -1, 0),
    (1, 0, 1),
    (1, 0, -1),
    (-1, 0, 0),
    (-1, -1, 0),
    (-1, 1, 0),
    (-1, 0, -1),
    (-1, 0, 1),
    (0, 1, 0),
    (0, -1, 0),
    (0, 0, 1),
    (0, 0, -1),
    (0, 1, 1),
    (0, -1, -1),
    (0, 1, -1),
    (0, -1, 1),
]
BULK_COEF = 0.5
STIFFNESS = 0.5
TAU_FLUID = 0.8
TAU_ORDER = 0.9
SHIFT_MIN = 33
SHIFT_MAX = 47
AXES = ("gx", "gy", "gz")
INTERPRET = False


def lattice_weight(number):
    steps_sq = sum((abs(comp) for comp in VELOCITIES[number]))
    if steps_sq == 0:
        return 1.0 / 3.0
    if steps_sq == 1:
        return 1.0 / 18.0
    return 1.0 / 36.0


def along(number, values, base):
    result = jnp.zeros_like(base)
    for axis_id in range(3):
        comp = VELOCITIES[number][axis_id]
        if comp != 0:
            result = result + comp * values[axis_id]
    return result


def collide(f_pop, g_pop, order_field, laplace, slopes):
    density = jnp.sum(f_pop, axis=0)
    chemical = (
        BULK_COEF * (order_field * order_field * order_field - order_field) - STIFFNESS * laplace
    )
    forces = [chemical * slope for slope in slopes]
    moments = []
    for axis_id in range(3):
        moment = jnp.zeros_like(density)
        for number in range(19):
            comp = VELOCITIES[number][axis_id]
            if comp != 0:
                moment = moment + comp * f_pop[number]
        moments.append(moment)
    flows = [(moments[axis_id] + 0.5 * forces[axis_id]) / density for axis_id in range(3)]
    speed_sq = flows[0] * flows[0] + flows[1] * flows[1] + flows[2] * flows[2]
    flow_force = flows[0] * forces[0] + flows[1] * forces[1] + flows[2] * forces[2]
    f_posts = []
    g_eqs = []
    for number in range(19):
        weight = lattice_weight(number)
        proj_flow = along(number, flows, density)
        proj_force = along(number, forces, density)
        shape_term = 3.0 * proj_flow + 4.5 * proj_flow * proj_flow - 1.5 * speed_sq
        f_eq = weight * density * (1.0 + shape_term)
        source = (
            (1.0 - 0.5 / TAU_FLUID)
            * weight
            * (3.0 * (proj_force - flow_force) + 9.0 * proj_flow * proj_force)
        )
        f_posts.append(f_pop[number] - (f_pop[number] - f_eq) / TAU_FLUID + source)
        g_eqs.append(weight * (3.0 * chemical + order_field * shape_term))
    rest_eq = order_field
    for number in range(1, 19):
        rest_eq = rest_eq - g_eqs[number]
    g_eqs[0] = rest_eq
    g_posts = [g_pop[number] - (g_pop[number] - g_eqs[number]) / TAU_ORDER for number in range(19)]
    return (jnp.stack(f_posts), jnp.stack(g_posts))


def collide_lists(f_pop, g_pop, order_field, laplace, slopes):
    density = f_pop[0]
    for number in range(1, 19):
        density = density + f_pop[number]
    chemical = (
        BULK_COEF * (order_field * order_field * order_field - order_field) - STIFFNESS * laplace
    )
    forces = [chemical * slope for slope in slopes]
    moments = []
    for axis_id in range(3):
        moment = jnp.zeros_like(density)
        for number in range(19):
            comp = VELOCITIES[number][axis_id]
            if comp != 0:
                moment = moment + comp * f_pop[number]
        moments.append(moment)
    flows = [(moments[axis_id] + 0.5 * forces[axis_id]) / density for axis_id in range(3)]
    speed_sq = flows[0] * flows[0] + flows[1] * flows[1] + flows[2] * flows[2]
    flow_force = flows[0] * forces[0] + flows[1] * forces[1] + flows[2] * forces[2]
    f_posts = []
    g_eqs = []
    for number in range(19):
        weight = lattice_weight(number)
        proj_flow = along(number, flows, density)
        proj_force = along(number, forces, density)
        shape_term = 3.0 * proj_flow + 4.5 * proj_flow * proj_flow - 1.5 * speed_sq
        f_eq = weight * density * (1.0 + shape_term)
        source = (
            (1.0 - 0.5 / TAU_FLUID)
            * weight
            * (3.0 * (proj_force - flow_force) + 9.0 * proj_flow * proj_force)
        )
        f_posts.append(f_pop[number] - (f_pop[number] - f_eq) / TAU_FLUID + source)
        g_eqs.append(weight * (3.0 * chemical + order_field * shape_term))
    rest_eq = order_field
    for number in range(1, 19):
        rest_eq = rest_eq - g_eqs[number]
    g_eqs[0] = rest_eq
    g_posts = [g_pop[number] - (g_pop[number] - g_eqs[number]) / TAU_ORDER for number in range(19)]
    return (f_posts, g_posts)


def pop_groups(pops):
    vel = [VELOCITIES[n % pops] for n in range(2 * pops)]
    groups = {
        name: [n for n in range(2 * pops) if vel[n][axis_id] == sign]
        for name, axis_id, sign in (
            ("x_up", 0, 1), ("x_dn", 0, -1), ("y_up", 1, 1), ("y_dn", 1, -1), ("z_up", 2, 1), ("z_dn", 2, -1)
        )
    }
    order = groups["z_up"] + groups["z_dn"] + [n for n in range(2 * pops) if vel[n][2] == 0]
    slot = {n: i for i, n in enumerate(order)}
    return vel, groups, slot


def collide_kernel(f_ref, g_ref, nb_ref, post_ref, xu_ref, xd_ref, yu_ref, yd_ref):
    pops = f_ref.shape[0]
    nx, ny = f_ref.shape[1], f_ref.shape[2]
    vel, groups, slot = pop_groups(pops)
    for x in range(nx):
        f_planes = [f_ref[n, x] for n in range(pops)]
        g_planes = [g_ref[n, x] for n in range(pops)]
        slopes = [nb_ref[2 + a, x] for a in range(3)]
        f_posts, g_posts = collide_lists(f_planes, g_planes, nb_ref[0, x], nb_ref[1, x], slopes)
        planes = f_posts + g_posts
        for n in range(2 * pops):
            post_ref[slot[n], x] = planes[n]
        if x == nx - 1:
            for k, n in enumerate(groups["x_up"]):
                xu_ref[k] = planes[n]
        if x == 0:
            for k, n in enumerate(groups["x_dn"]):
                xd_ref[k] = planes[n]
        for k, n in enumerate(groups["y_up"]):
            yu_ref[k, pl.ds(x, 1), :] = planes[n][ny - 1 : ny, :]
        for k, n in enumerate(groups["y_dn"]):
            yd_ref[k, pl.ds(x, 1), :] = planes[n][0:1, :]


def stream_kernel(post_ref, xlow_ref, xhigh_ref, hym_ref, hyp_ref, col_ref, f_ref, g_ref):
    pops = f_ref.shape[0]
    nx, ny, nz = f_ref.shape[1:]
    row = lax.broadcasted_iota(jnp.int32, (ny, nz), 0)
    lane = lax.broadcasted_iota(jnp.int32, (ny, nz), 1)
    vel = [VELOCITIES[n % pops] for n in range(2 * pops)]
    x_up = [n for n in range(2 * pops) if vel[n][0] == 1]
    x_dn = [n for n in range(2 * pops) if vel[n][0] == -1]
    y_up = [n for n in range(2 * pops) if vel[n][1] == 1]
    y_dn = [n for n in range(2 * pops) if vel[n][1] == -1]
    z_any = [n for n in range(2 * pops) if vel[n][2] != 0]
    for n in range(2 * pops):
        cx, cy, cz = vel[n]
        out = f_ref if n < pops else g_ref
        for x in range(nx):
            src = x - cx
            if src < 0:
                tile = xlow_ref[x_up.index(n)]
            elif src >= nx:
                tile = xhigh_ref[x_dn.index(n)]
            else:
                tile = post_ref[pop_groups(pops)[2][n], src]
                if cy == 1:
                    edge = jnp.broadcast_to(hym_ref[pl.ds(y_up.index(n) * nx + src, 1), :], (ny, nz))
                    tile = jnp.where(row == 0, edge, pltpu.roll(tile, 1, 0))
                elif cy == -1:
                    edge = jnp.broadcast_to(hyp_ref[pl.ds(y_dn.index(n) * nx + src, 1), :], (ny, nz))
                    tile = jnp.where(row == ny - 1, edge, pltpu.roll(tile, ny - 1, 0))
            if 0 <= src < nx and cz == 1:
                tile = jnp.where(lane == 0, col_ref[z_any.index(n), x], pltpu.roll(tile, 1, 1))
            elif 0 <= src < nx and cz == -1:
                tile = jnp.where(lane == nz - 1, col_ref[z_any.index(n), x], pltpu.roll(tile, nz - 1, 1))
            out[n % pops, x] = tile


def exchange(sends):
    sizes = [lax.axis_size(a) for a in AXES]
    groups = {}
    order = []
    for index, (value, offset) in enumerate(sends):
        key = (tuple(o % n for o, n in zip(offset, sizes)), value.shape[1:])
        if key not in groups:
            groups[key] = []
            order.append(key)
        groups[key].append(index)
    results = [None] * len(sends)
    for key in order:
        members = groups[key]
        offset = key[0]
        pairs = []
        for i in range(sizes[0]):
            for j in range(sizes[1]):
                for k in range(sizes[2]):
                    src = (i * sizes[1] + j) * sizes[2] + k
                    ti, tj, tk = [(c + o) % n for c, o, n in zip((i, j, k), offset, sizes)]
                    pairs.append((src, (ti * sizes[1] + tj) * sizes[2] + tk))
        payload = [sends[m][0] for m in members]
        joined = payload[0] if len(payload) == 1 else jnp.concatenate(payload, axis=0)
        got = lax.ppermute(joined, AXES, pairs)
        start = 0
        for m in members:
            count = sends[m][0].shape[0]
            results[m] = got[start : start + count]
            start += count
    return results


def local(f_pop, g_pop, displacement):
    shift = displacement[0]
    nx, ny, nz = (f_pop.shape[1], f_pop.shape[2], f_pop.shape[3])
    q = SHIFT_MIN // ny
    assert SHIFT_MAX // ny == q and SHIFT_MIN % ny != 0
    rem = shift - q * ny

    phi = jnp.sum(g_pop, axis=0)
    face_x_last = jnp.sum(g_pop[:, -1], axis=0)
    face_x_first = jnp.sum(g_pop[:, 0], axis=0)
    up1, dn1, pzm, pzp = exchange(
        [
            (jnp.concatenate([jnp.sum(g_pop[:, :, -1], axis=0), face_x_last]), (0, 1, 0)),
            (jnp.concatenate([jnp.sum(g_pop[:, :, 0], axis=0), face_x_first]), (0, -1, 0)),
            (jnp.sum(g_pop[:, :, :, -1], axis=0)[None], (0, 0, 1)),
            (jnp.sum(g_pop[:, :, :, 0], axis=0)[None], (0, 0, -1)),
        ]
    )
    low_pair, high_pair = exchange(
        [
            (jnp.concatenate([up1[nx:], face_x_last]), (1, q, 0)),
            (jnp.concatenate([face_x_first, dn1[nx:]]), (-1, -q, 0)),
        ]
    )
    low = lax.dynamic_slice_in_dim(low_pair, ny - rem, ny, 0)[None]
    high = lax.dynamic_slice_in_dim(high_pair, rem, ny, 0)[None]
    neigh_xm = jnp.concatenate([low, phi[:-1]], axis=0)
    neigh_xp = jnp.concatenate([phi[1:], high], axis=0)
    neigh_ym = jnp.concatenate([up1[:nx][:, None], phi[:, :-1]], axis=1)
    neigh_yp = jnp.concatenate([phi[:, 1:], dn1[:nx][:, None]], axis=1)
    neigh_zm = jnp.concatenate([pzm[0][:, :, None], phi[:, :, :-1]], axis=2)
    neigh_zp = jnp.concatenate([phi[:, :, 1:], pzp[0][:, :, None]], axis=2)
    laplace = neigh_xm + neigh_xp + neigh_ym + neigh_yp + neigh_zm + neigh_zp - 6.0 * phi
    slopes = [0.5 * (neigh_xp - neigh_xm), 0.5 * (neigh_yp - neigh_ym), 0.5 * (neigh_zp - neigh_zm)]
    nb = jnp.stack([phi, laplace] + slopes)
    pops = f_pop.shape[0]
    _, groups, slot = pop_groups(pops)
    n_xu, n_xd, n_yu, n_yd = (len(groups[k]) for k in ("x_up", "x_dn", "y_up", "y_dn"))
    post, face_xu, face_xd, face_yu, face_yd = pl.pallas_call(
        collide_kernel,
        out_shape=(
            jax.ShapeDtypeStruct((2 * pops, nx, ny, nz), jnp.float32),
            jax.ShapeDtypeStruct((n_xu, ny, nz), jnp.float32),
            jax.ShapeDtypeStruct((n_xd, ny, nz), jnp.float32),
            jax.ShapeDtypeStruct((n_yu, nx, nz), jnp.float32),
            jax.ShapeDtypeStruct((n_yd, nx, nz), jnp.float32),
        ),
        interpret=INTERPRET,
    )(f_pop, g_pop, nb)

    vel = [VELOCITIES[n % 19] for n in range(38)]

    def pick(cond, among=range(38)):
        return [n for n in among if cond(vel[n])]

    x_up = pick(lambda c: c[0] == 1)
    x_dn = pick(lambda c: c[0] == -1)
    y_up = pick(lambda c: c[1] == 1)
    y_dn = pick(lambda c: c[1] == -1)
    z_up = pick(lambda c: c[2] == 1)
    z_dn = pick(lambda c: c[2] == -1)
    xz_up = pick(lambda c: c[2] != 0, x_up)
    xz_dn = pick(lambda c: c[2] != 0, x_dn)
    yz_up = pick(lambda c: c[2] != 0, y_up)
    yz_dn = pick(lambda c: c[2] != 0, y_dn)

    hz_m, hz_p = exchange(
        [
            (post[: len(z_up), :, :, -1], (0, 0, 1)),
            (post[len(z_up) : len(z_up) + len(z_dn), :, :, 0], (0, 0, -1)),
        ]
    )

    def zhalo(n):
        return hz_m[z_up.index(n)] if vel[n][2] == 1 else hz_p[z_dn.index(n)]

    def lanes(a):
        return jnp.pad(a, ((0, 0), (0, nz - a.shape[1])))

    def packed(face, extra):
        return jnp.concatenate([face.reshape(-1, nz), lanes(jnp.stack(extra))], axis=0)

    send_up = packed(face_xu, [zhalo(n)[-1] for n in xz_up])
    send_dn = packed(face_xd, [zhalo(n)[0] for n in xz_dn])
    send_yu = packed(face_yu, [zhalo(n)[:, -1] for n in yz_up])
    send_yd = packed(face_yd, [zhalo(n)[:, 0] for n in yz_dn])
    n_yu, n_yd = send_yu.shape[0], send_yd.shape[0]
    up2, dn2 = exchange(
        [
            (jnp.concatenate([send_yu, send_up]), (0, 1, 0)),
            (jnp.concatenate([send_yd, send_dn]), (0, -1, 0)),
        ]
    )
    hy_m, hy_p = up2[:n_yu], dn2[:n_yd]

    def unpack_x(got, count):
        return got[: count * ny].reshape(count, ny, nz), got[count * ny :, :ny]

    def unpack_y(got, count):
        return got[: count * nx].reshape(count, nx, nz), got[count * nx :, :nx]

    def by_pop(idx, axis_id, shape):
        return jnp.array([vel[n][axis_id] for n in idx], jnp.int32).reshape(shape)

    def pick_y(win, idx):
        cy = by_pop(idx, 1, (-1, 1, 1))
        return jnp.where(cy == 1, win[:, :ny], jnp.where(cy == -1, win[:, 2:], win[:, 1 : ny + 1]))

    def shift_z(planes, idx, edge_cols, edge_idx):
        cz = by_pop(idx, 2, (-1, 1, 1))
        zero = jnp.zeros((1, ny), planes.dtype)
        col = jnp.concatenate([edge_cols, zero])[
            jnp.array([edge_idx.index(n) if n in edge_idx else len(edge_idx) for n in idx])
        ][:, :, None]
        return jnp.where(
            cz == 1,
            jnp.concatenate([col, planes[:, :, :-1]], axis=2),
            jnp.where(cz == -1, jnp.concatenate([planes[:, :, 1:], col], axis=2), planes),
        )

    def window(first, second, idx, edge_idx, start):
        count = len(idx)
        pa, ca = unpack_x(first, count)
        pb, cb = unpack_x(second, count)
        planes = lax.dynamic_slice_in_dim(jnp.concatenate([pa, pb], axis=1), start - 1, ny + 2, 1)
        cols = lax.dynamic_slice_in_dim(jnp.concatenate([ca, cb], axis=1), start, ny, 1)
        return shift_z(pick_y(planes, idx), idx, cols, edge_idx).reshape(-1, nz)

    low2, high2 = exchange(
        [
            (window(up2[n_yu:], send_up, x_up, xz_up, ny - rem), (1, q, 0)),
            (window(send_dn, dn2[n_yd:], x_dn, xz_dn, rem), (-1, -q, 0)),
        ]
    )
    hy_m, cy_m = unpack_y(hy_m, len(y_up))
    hy_p, cy_p = unpack_y(hy_p, len(y_dn))

    xlow = low2.reshape(len(x_up), ny, nz)
    xhigh = high2.reshape(len(x_dn), ny, nz)
    z_any = pick(lambda c: c[2] != 0)
    zh = jnp.concatenate([hz_m, hz_p])[jnp.array([z_up.index(n) if vel[n][2] == 1 else len(z_up) + z_dn.index(n) for n in z_any])]

    def spread(values, idx):
        zero = jnp.zeros((1,) + values.shape[1:], values.dtype)
        both = jnp.concatenate([values, zero])
        return both[jnp.array([idx.index(n) if n in idx else len(idx) for n in z_any])]

    corner_m = spread(cy_m, yz_up)[:, :, None]
    corner_p = spread(cy_p, yz_dn)[:, :, None]
    cy = by_pop(z_any, 1, (-1, 1, 1))
    cx = by_pop(z_any, 0, (-1, 1, 1))
    down = jnp.concatenate([corner_m, zh[:, :, :-1]], axis=2)
    up = jnp.concatenate([zh[:, :, 1:], corner_p], axis=2)
    zy = jnp.where(cy == 1, down, jnp.where(cy == -1, up, zh))
    edge_low = jnp.zeros((len(z_any), 1, ny), jnp.float32)
    edge_high = edge_low
    cols = jnp.where(
        cx == 1,
        jnp.concatenate([edge_low, zy[:, :-1]], axis=1),
        jnp.where(cx == -1, jnp.concatenate([zy[:, 1:], edge_high], axis=1), zy),
    )
    cols = jnp.broadcast_to(cols[:, :, :, None], (len(z_any), nx, ny, nz))
    pops = f_pop.shape[0]
    f_new, g_new = pl.pallas_call(
        stream_kernel,
        out_shape=(
            jax.ShapeDtypeStruct((pops, nx, ny, nz), jnp.float32),
            jax.ShapeDtypeStruct((pops, nx, ny, nz), jnp.float32),
        ),
        interpret=INTERPRET,
    )(post, xlow, xhigh, up2, dn2, cols)
    return (f_new, g_new)


def solution(mesh):
    return jax.shard_map(
        local,
        mesh=mesh,
        in_specs=(P(None, "gx", "gy", "gz"), P(None, "gx", "gy", "gz"), P()),
        out_specs=(P(None, "gx", "gy", "gz"), P(None, "gx", "gy", "gz")),
        check_vma=False,
    )
```

```python
import jax
import jax.numpy as jnp
from jax import lax
from jax.sharding import PartitionSpec as P
from jax.experimental import pallas as pl
from jax.experimental.pallas import tpu as pltpu

VELOCITIES = [
    (0, 0, 0),
    (1, 0, 0),
    (1, 1, 0),
    (1, -1, 0),
    (1, 0, 1),
    (1, 0, -1),
    (-1, 0, 0),
    (-1, -1, 0),
    (-1, 1, 0),
    (-1, 0, -1),
    (-1, 0, 1),
    (0, 1, 0),
    (0, -1, 0),
    (0, 0, 1),
    (0, 0, -1),
    (0, 1, 1),
    (0, -1, -1),
    (0, 1, -1),
    (0, -1, 1),
]
BULK_COEF = 0.5
STIFFNESS = 0.5
TAU_FLUID = 0.8
TAU_ORDER = 0.9
SHIFT_MIN = 33
SHIFT_MAX = 47
AXES = ("gx", "gy", "gz")
INTERPRET = False


def lattice_weight(number):
    steps_sq = sum((abs(comp) for comp in VELOCITIES[number]))
    if steps_sq == 0:
        return 1.0 / 3.0
    if steps_sq == 1:
        return 1.0 / 18.0
    return 1.0 / 36.0


def along(number, values, base):
    result = jnp.zeros_like(base)
    for axis_id in range(3):
        comp = VELOCITIES[number][axis_id]
        if comp != 0:
            result = result + comp * values[axis_id]
    return result


def collide(f_pop, g_pop, order_field, laplace, slopes):
    density = jnp.sum(f_pop, axis=0)
    chemical = (
        BULK_COEF * (order_field * order_field * order_field - order_field) - STIFFNESS * laplace
    )
    forces = [chemical * slope for slope in slopes]
    moments = []
    for axis_id in range(3):
        moment = jnp.zeros_like(density)
        for number in range(19):
            comp = VELOCITIES[number][axis_id]
            if comp != 0:
                moment = moment + comp * f_pop[number]
        moments.append(moment)
    flows = [(moments[axis_id] + 0.5 * forces[axis_id]) / density for axis_id in range(3)]
    speed_sq = flows[0] * flows[0] + flows[1] * flows[1] + flows[2] * flows[2]
    flow_force = flows[0] * forces[0] + flows[1] * forces[1] + flows[2] * forces[2]
    f_posts = []
    g_eqs = []
    for number in range(19):
        weight = lattice_weight(number)
        proj_flow = along(number, flows, density)
        proj_force = along(number, forces, density)
        shape_term = 3.0 * proj_flow + 4.5 * proj_flow * proj_flow - 1.5 * speed_sq
        f_eq = weight * density * (1.0 + shape_term)
        source = (
            (1.0 - 0.5 / TAU_FLUID)
            * weight
            * (3.0 * (proj_force - flow_force) + 9.0 * proj_flow * proj_force)
        )
        f_posts.append(f_pop[number] - (f_pop[number] - f_eq) / TAU_FLUID + source)
        g_eqs.append(weight * (3.0 * chemical + order_field * shape_term))
    rest_eq = order_field
    for number in range(1, 19):
        rest_eq = rest_eq - g_eqs[number]
    g_eqs[0] = rest_eq
    g_posts = [g_pop[number] - (g_pop[number] - g_eqs[number]) / TAU_ORDER for number in range(19)]
    return (jnp.stack(f_posts), jnp.stack(g_posts))


def collide_lists(f_pop, g_pop, order_field, laplace, slopes):
    density = f_pop[0]
    for number in range(1, 19):
        density = density + f_pop[number]
    chemical = (
        BULK_COEF * (order_field * order_field * order_field - order_field) - STIFFNESS * laplace
    )
    forces = [chemical * slope for slope in slopes]
    moments = []
    for axis_id in range(3):
        moment = jnp.zeros_like(density)
        for number in range(19):
            comp = VELOCITIES[number][axis_id]
            if comp != 0:
                moment = moment + comp * f_pop[number]
        moments.append(moment)
    flows = [(moments[axis_id] + 0.5 * forces[axis_id]) / density for axis_id in range(3)]
    speed_sq = flows[0] * flows[0] + flows[1] * flows[1] + flows[2] * flows[2]
    flow_force = flows[0] * forces[0] + flows[1] * forces[1] + flows[2] * forces[2]
    f_posts = []
    g_eqs = []
    for number in range(19):
        weight = lattice_weight(number)
        proj_flow = along(number, flows, density)
        proj_force = along(number, forces, density)
        shape_term = 3.0 * proj_flow + 4.5 * proj_flow * proj_flow - 1.5 * speed_sq
        f_eq = weight * density * (1.0 + shape_term)
        source = (
            (1.0 - 0.5 / TAU_FLUID)
            * weight
            * (3.0 * (proj_force - flow_force) + 9.0 * proj_flow * proj_force)
        )
        f_posts.append(f_pop[number] - (f_pop[number] - f_eq) / TAU_FLUID + source)
        g_eqs.append(weight * (3.0 * chemical + order_field * shape_term))
    rest_eq = order_field
    for number in range(1, 19):
        rest_eq = rest_eq - g_eqs[number]
    g_eqs[0] = rest_eq
    g_posts = [g_pop[number] - (g_pop[number] - g_eqs[number]) / TAU_ORDER for number in range(19)]
    return (f_posts, g_posts)


def pop_groups(pops):
    vel = [VELOCITIES[n % pops] for n in range(2 * pops)]
    groups = {
        name: [n for n in range(2 * pops) if vel[n][axis_id] == sign]
        for name, axis_id, sign in (
            ("x_up", 0, 1), ("x_dn", 0, -1), ("y_up", 1, 1), ("y_dn", 1, -1), ("z_up", 2, 1), ("z_dn", 2, -1)
        )
    }
    order = groups["z_up"] + groups["z_dn"] + [n for n in range(2 * pops) if vel[n][2] == 0]
    slot = {n: i for i, n in enumerate(order)}
    return vel, groups, slot


def collide_kernel(f_ref, g_ref, nb_ref, post_ref, xu_ref, xd_ref, yu_ref, yd_ref):
    pops = f_ref.shape[0]
    nx, ny = f_ref.shape[1], f_ref.shape[2]
    vel, groups, slot = pop_groups(pops)
    for x in range(nx):
        f_planes = [f_ref[n, x] for n in range(pops)]
        g_planes = [g_ref[n, x] for n in range(pops)]
        slopes = [nb_ref[2 + a, x] for a in range(3)]
        f_posts, g_posts = collide_lists(f_planes, g_planes, nb_ref[0, x], nb_ref[1, x], slopes)
        planes = f_posts + g_posts
        for n in range(2 * pops):
            post_ref[slot[n], x] = planes[n]
        if x == nx - 1:
            for k, n in enumerate(groups["x_up"]):
                xu_ref[k] = planes[n]
        if x == 0:
            for k, n in enumerate(groups["x_dn"]):
                xd_ref[k] = planes[n]
        for k, n in enumerate(groups["y_up"]):
            yu_ref[k, pl.ds(x, 1), :] = planes[n][ny - 1 : ny, :]
        for k, n in enumerate(groups["y_dn"]):
            yd_ref[k, pl.ds(x, 1), :] = planes[n][0:1, :]


def stream_kernel(post_ref, xlow_ref, xhigh_ref, hym_ref, hyp_ref, col_ref, f_ref, g_ref):
    pops = f_ref.shape[0]
    nx, ny, nz = f_ref.shape[1:]
    row = lax.broadcasted_iota(jnp.int32, (ny, nz), 0)
    lane = lax.broadcasted_iota(jnp.int32, (ny, nz), 1)
    vel = [VELOCITIES[n % pops] for n in range(2 * pops)]
    x_up = [n for n in range(2 * pops) if vel[n][0] == 1]
    x_dn = [n for n in range(2 * pops) if vel[n][0] == -1]
    y_up = [n for n in range(2 * pops) if vel[n][1] == 1]
    y_dn = [n for n in range(2 * pops) if vel[n][1] == -1]
    z_any = [n for n in range(2 * pops) if vel[n][2] != 0]
    for n in range(2 * pops):
        cx, cy, cz = vel[n]
        out = f_ref if n < pops else g_ref
        for x in range(nx):
            src = x - cx
            if src < 0:
                tile = xlow_ref[x_up.index(n)]
            elif src >= nx:
                tile = xhigh_ref[x_dn.index(n)]
            else:
                tile = post_ref[pop_groups(pops)[2][n], src]
                if cy == 1:
                    edge = jnp.broadcast_to(hym_ref[pl.ds(y_up.index(n) * nx + src, 1), :], (ny, nz))
                    tile = jnp.where(row == 0, edge, pltpu.roll(tile, 1, 0))
                elif cy == -1:
                    edge = jnp.broadcast_to(hyp_ref[pl.ds(y_dn.index(n) * nx + src, 1), :], (ny, nz))
                    tile = jnp.where(row == ny - 1, edge, pltpu.roll(tile, ny - 1, 0))
            if 0 <= src < nx and cz == 1:
                tile = jnp.where(lane == 0, col_ref[z_any.index(n), x], pltpu.roll(tile, 1, 1))
            elif 0 <= src < nx and cz == -1:
                tile = jnp.where(lane == nz - 1, col_ref[z_any.index(n), x], pltpu.roll(tile, nz - 1, 1))
            out[n % pops, x] = tile


def exchange(sends):
    sizes = [lax.axis_size(a) for a in AXES]
    groups = {}
    order = []
    for index, (value, offset) in enumerate(sends):
        key = (tuple(o % n for o, n in zip(offset, sizes)), value.shape[1:])
        if key not in groups:
            groups[key] = []
            order.append(key)
        groups[key].append(index)
    results = [None] * len(sends)
    for key in order:
        members = groups[key]
        offset = key[0]
        pairs = []
        for i in range(sizes[0]):
            for j in range(sizes[1]):
                for k in range(sizes[2]):
                    src = (i * sizes[1] + j) * sizes[2] + k
                    ti, tj, tk = [(c + o) % n for c, o, n in zip((i, j, k), offset, sizes)]
                    pairs.append((src, (ti * sizes[1] + tj) * sizes[2] + tk))
        payload = [sends[m][0] for m in members]
        joined = payload[0] if len(payload) == 1 else jnp.concatenate(payload, axis=0)
        got = lax.ppermute(joined, AXES, pairs)
        start = 0
        for m in members:
            count = sends[m][0].shape[0]
            results[m] = got[start : start + count]
            start += count
    return results


def local(f_pop, g_pop, displacement):
    shift = displacement[0]
    nx, ny, nz = (f_pop.shape[1], f_pop.shape[2], f_pop.shape[3])
    q = SHIFT_MIN // ny
    assert SHIFT_MAX // ny == q and SHIFT_MIN % ny != 0
    rem = shift - q * ny

    phi = jnp.sum(g_pop, axis=0)
    up1, dn1, pzm, pzp = exchange(
        [
            (jnp.concatenate([phi[:, -1], phi[-1]]), (0, 1, 0)),
            (jnp.concatenate([phi[:, 0], phi[0]]), (0, -1, 0)),
            (phi[:, :, -1][None], (0, 0, 1)),
            (phi[:, :, 0][None], (0, 0, -1)),
        ]
    )
    low_pair, high_pair = exchange(
        [
            (jnp.concatenate([up1[nx:], phi[-1]]), (1, q, 0)),
            (jnp.concatenate([phi[0], dn1[nx:]]), (-1, -q, 0)),
        ]
    )
    low = lax.dynamic_slice_in_dim(low_pair, ny - rem, ny, 0)[None]
    high = lax.dynamic_slice_in_dim(high_pair, rem, ny, 0)[None]
    neigh_xm = jnp.concatenate([low, phi[:-1]], axis=0)
    neigh_xp = jnp.concatenate([phi[1:], high], axis=0)
    neigh_ym = jnp.concatenate([up1[:nx][:, None], phi[:, :-1]], axis=1)
    neigh_yp = jnp.concatenate([phi[:, 1:], dn1[:nx][:, None]], axis=1)
    neigh_zm = jnp.concatenate([pzm[0][:, :, None], phi[:, :, :-1]], axis=2)
    neigh_zp = jnp.concatenate([phi[:, :, 1:], pzp[0][:, :, None]], axis=2)
    laplace = neigh_xm + neigh_xp + neigh_ym + neigh_yp + neigh_zm + neigh_zp - 6.0 * phi
    slopes = [0.5 * (neigh_xp - neigh_xm), 0.5 * (neigh_yp - neigh_ym), 0.5 * (neigh_zp - neigh_zm)]
    nb = jnp.stack([phi, laplace] + slopes)
    pops = f_pop.shape[0]
    _, groups, slot = pop_groups(pops)
    n_xu, n_xd, n_yu, n_yd = (len(groups[k]) for k in ("x_up", "x_dn", "y_up", "y_dn"))
    post, face_xu, face_xd, face_yu, face_yd = pl.pallas_call(
        collide_kernel,
        out_shape=(
            jax.ShapeDtypeStruct((2 * pops, nx, ny, nz), jnp.float32),
            jax.ShapeDtypeStruct((n_xu, ny, nz), jnp.float32),
            jax.ShapeDtypeStruct((n_xd, ny, nz), jnp.float32),
            jax.ShapeDtypeStruct((n_yu, nx, nz), jnp.float32),
            jax.ShapeDtypeStruct((n_yd, nx, nz), jnp.float32),
        ),
        interpret=INTERPRET,
    )(f_pop, g_pop, nb)

    vel = [VELOCITIES[n % 19] for n in range(38)]

    def pick(cond, among=range(38)):
        return [n for n in among if cond(vel[n])]

    x_up = pick(lambda c: c[0] == 1)
    x_dn = pick(lambda c: c[0] == -1)
    y_up = pick(lambda c: c[1] == 1)
    y_dn = pick(lambda c: c[1] == -1)
    z_up = pick(lambda c: c[2] == 1)
    z_dn = pick(lambda c: c[2] == -1)
    xz_up = pick(lambda c: c[2] != 0, x_up)
    xz_dn = pick(lambda c: c[2] != 0, x_dn)
    yz_up = pick(lambda c: c[2] != 0, y_up)
    yz_dn = pick(lambda c: c[2] != 0, y_dn)

    def zhalo(n):
        return hz_m[z_up.index(n)] if vel[n][2] == 1 else hz_p[z_dn.index(n)]

    def lanes(a):
        return jnp.pad(a, ((0, 0), (0, nz - a.shape[1])))

    def packed(face, extra):
        return jnp.concatenate([face.reshape(-1, nz), lanes(jnp.stack(extra))], axis=0)

    sends = [
        (post[: len(z_up), :, :, -1], (0, 0, 1)),
        (post[len(z_up) : len(z_up) + len(z_dn), :, :, 0], (0, 0, -1)),
        (jnp.concatenate([face_yu.reshape(-1, nz), face_xu.reshape(-1, nz)]), (0, 1, 0)),
        (jnp.concatenate([face_yd.reshape(-1, nz), face_xd.reshape(-1, nz)]), (0, -1, 0)),
    ]
    diag_keys = []
    for dy in (1, -1):
        for dz in (1, -1):
            ypops = [n for n in (yz_up if dy == 1 else yz_dn) if vel[n][2] == dz]
            xpops = [n for n in (xz_up if dy == 1 else xz_dn) if vel[n][2] == dz]
            yrow, xrow, zl = (ny - 1, nx - 1, nz - 1 if dz == 1 else 0) if dy == 1 else (0, 0, nz - 1 if dz == 1 else 0)
            ys = post[jnp.array([slot[n] for n in ypops]), :, yrow, zl]
            xs = post[jnp.array([slot[n] for n in xpops]), xrow, :, zl]
            sends.append((jnp.concatenate([lanes(ys), lanes(xs)]), (0, dy, dz)))
            diag_keys.append((dy, dz, ypops, xpops))
    got = exchange(sends)
    hz_m, hz_p, up2, dn2 = got[:4]
    diag = dict(((dy, dz), (g, yp, xp)) for (dy, dz, yp, xp), g in zip(diag_keys, got[4:]))

    def edge_rows(dy, idx, kind):
        rows = []
        for n in idx:
            g, yp, xp = diag[(dy, vel[n][2])]
            rows.append(g[yp.index(n)][:nx] if kind == "y" else g[len(yp) + xp.index(n)][:ny])
        return jnp.stack(rows)

    cy_m = edge_rows(1, yz_up, "y")
    cy_p = edge_rows(-1, yz_dn, "y")
    n_face_u, n_face_d = face_yu.shape[0] * nx, face_yd.shape[0] * nx
    send_up = packed(face_xu, [zhalo(n)[-1] for n in xz_up])
    send_dn = packed(face_xd, [zhalo(n)[0] for n in xz_dn])
    from_up = jnp.concatenate([up2[n_face_u:], lanes(edge_rows(1, xz_up, "x"))])
    from_dn = jnp.concatenate([dn2[n_face_d:], lanes(edge_rows(-1, xz_dn, "x"))])

    def unpack_x(got, count):
        return got[: count * ny].reshape(count, ny, nz), got[count * ny :, :ny]

    def unpack_y(got, count):
        return got[: count * nx].reshape(count, nx, nz), got[count * nx :, :nx]

    def by_pop(idx, axis_id, shape):
        return jnp.array([vel[n][axis_id] for n in idx], jnp.int32).reshape(shape)

    def pick_y(win, idx):
        cy = by_pop(idx, 1, (-1, 1, 1))
        return jnp.where(cy == 1, win[:, :ny], jnp.where(cy == -1, win[:, 2:], win[:, 1 : ny + 1]))

    def shift_z(planes, idx, edge_cols, edge_idx):
        cz = by_pop(idx, 2, (-1, 1, 1))
        zero = jnp.zeros((1, ny), planes.dtype)
        col = jnp.concatenate([edge_cols, zero])[
            jnp.array([edge_idx.index(n) if n in edge_idx else len(edge_idx) for n in idx])
        ][:, :, None]
        return jnp.where(
            cz == 1,
            jnp.concatenate([col, planes[:, :, :-1]], axis=2),
            jnp.where(cz == -1, jnp.concatenate([planes[:, :, 1:], col], axis=2), planes),
        )

    def window(first, second, idx, edge_idx, start):
        count = len(idx)
        pa, ca = unpack_x(first, count)
        pb, cb = unpack_x(second, count)
        planes = lax.dynamic_slice_in_dim(jnp.concatenate([pa, pb], axis=1), start - 1, ny + 2, 1)
        cols = lax.dynamic_slice_in_dim(jnp.concatenate([ca, cb], axis=1), start, ny, 1)
        return shift_z(pick_y(planes, idx), idx, cols, edge_idx).reshape(-1, nz)

    low2, high2 = exchange(
        [
            (window(from_up, send_up, x_up, xz_up, ny - rem), (1, q, 0)),
            (window(send_dn, from_dn, x_dn, xz_dn, rem), (-1, -q, 0)),
        ]
    )

    xlow = low2.reshape(len(x_up), ny, nz)
    xhigh = high2.reshape(len(x_dn), ny, nz)
    z_any = pick(lambda c: c[2] != 0)
    zh = jnp.concatenate([hz_m, hz_p])[jnp.array([z_up.index(n) if vel[n][2] == 1 else len(z_up) + z_dn.index(n) for n in z_any])]

    def spread(values, idx):
        zero = jnp.zeros((1,) + values.shape[1:], values.dtype)
        both = jnp.concatenate([values, zero])
        return both[jnp.array([idx.index(n) if n in idx else len(idx) for n in z_any])]

    corner_m = spread(cy_m, yz_up)[:, :, None]
    corner_p = spread(cy_p, yz_dn)[:, :, None]
    cy = by_pop(z_any, 1, (-1, 1, 1))
    cx = by_pop(z_any, 0, (-1, 1, 1))
    down = jnp.concatenate([corner_m, zh[:, :, :-1]], axis=2)
    up = jnp.concatenate([zh[:, :, 1:], corner_p], axis=2)
    zy = jnp.where(cy == 1, down, jnp.where(cy == -1, up, zh))
    edge_low = jnp.zeros((len(z_any), 1, ny), jnp.float32)
    edge_high = edge_low
    cols = jnp.where(
        cx == 1,
        jnp.concatenate([edge_low, zy[:, :-1]], axis=1),
        jnp.where(cx == -1, jnp.concatenate([zy[:, 1:], edge_high], axis=1), zy),
    )
    cols = jnp.broadcast_to(cols[:, :, :, None], (len(z_any), nx, ny, nz))
    pops = f_pop.shape[0]
    f_new, g_new = pl.pallas_call(
        stream_kernel,
        out_shape=(
            jax.ShapeDtypeStruct((pops, nx, ny, nz), jnp.float32),
            jax.ShapeDtypeStruct((pops, nx, ny, nz), jnp.float32),
        ),
        interpret=INTERPRET,
    )(post, xlow, xhigh, up2, dn2, cols)
    return (f_new, g_new)


def solution(mesh):
    return jax.shard_map(
        local,
        mesh=mesh,
        in_specs=(P(None, "gx", "gy", "gz"), P(None, "gx", "gy", "gz"), P()),
        out_specs=(P(None, "gx", "gy", "gz"), P(None, "gx", "gy", "gz")),
        check_vma=False,
    )
```

```python
import jax
import jax.numpy as jnp
from jax import lax
from jax.sharding import PartitionSpec as P
from jax.experimental import pallas as pl
from jax.experimental.pallas import tpu as pltpu

VELOCITIES = [
    (0, 0, 0),
    (1, 0, 0),
    (1, 1, 0),
    (1, -1, 0),
    (1, 0, 1),
    (1, 0, -1),
    (-1, 0, 0),
    (-1, -1, 0),
    (-1, 1, 0),
    (-1, 0, -1),
    (-1, 0, 1),
    (0, 1, 0),
    (0, -1, 0),
    (0, 0, 1),
    (0, 0, -1),
    (0, 1, 1),
    (0, -1, -1),
    (0, 1, -1),
    (0, -1, 1),
]
BULK_COEF = 0.5
STIFFNESS = 0.5
TAU_FLUID = 0.8
TAU_ORDER = 0.9
SHIFT_MIN = 33
SHIFT_MAX = 47
AXES = ("gx", "gy", "gz")
INTERPRET = False


def lattice_weight(number):
    steps_sq = sum((abs(comp) for comp in VELOCITIES[number]))
    if steps_sq == 0:
        return 1.0 / 3.0
    if steps_sq == 1:
        return 1.0 / 18.0
    return 1.0 / 36.0


def along(number, values, base):
    result = jnp.zeros_like(base)
    for axis_id in range(3):
        comp = VELOCITIES[number][axis_id]
        if comp != 0:
            result = result + comp * values[axis_id]
    return result


def collide(f_pop, g_pop, order_field, laplace, slopes):
    density = jnp.sum(f_pop, axis=0)
    chemical = (
        BULK_COEF * (order_field * order_field * order_field - order_field) - STIFFNESS * laplace
    )
    forces = [chemical * slope for slope in slopes]
    moments = []
    for axis_id in range(3):
        moment = jnp.zeros_like(density)
        for number in range(19):
            comp = VELOCITIES[number][axis_id]
            if comp != 0:
                moment = moment + comp * f_pop[number]
        moments.append(moment)
    flows = [(moments[axis_id] + 0.5 * forces[axis_id]) / density for axis_id in range(3)]
    speed_sq = flows[0] * flows[0] + flows[1] * flows[1] + flows[2] * flows[2]
    flow_force = flows[0] * forces[0] + flows[1] * forces[1] + flows[2] * forces[2]
    f_posts = []
    g_eqs = []
    for number in range(19):
        weight = lattice_weight(number)
        proj_flow = along(number, flows, density)
        proj_force = along(number, forces, density)
        shape_term = 3.0 * proj_flow + 4.5 * proj_flow * proj_flow - 1.5 * speed_sq
        f_eq = weight * density * (1.0 + shape_term)
        source = (
            (1.0 - 0.5 / TAU_FLUID)
            * weight
            * (3.0 * (proj_force - flow_force) + 9.0 * proj_flow * proj_force)
        )
        f_posts.append(f_pop[number] - (f_pop[number] - f_eq) / TAU_FLUID + source)
        g_eqs.append(weight * (3.0 * chemical + order_field * shape_term))
    rest_eq = order_field
    for number in range(1, 19):
        rest_eq = rest_eq - g_eqs[number]
    g_eqs[0] = rest_eq
    g_posts = [g_pop[number] - (g_pop[number] - g_eqs[number]) / TAU_ORDER for number in range(19)]
    return (jnp.stack(f_posts), jnp.stack(g_posts))


def collide_lists(f_pop, g_pop, order_field, laplace, slopes):
    density = f_pop[0]
    for number in range(1, 19):
        density = density + f_pop[number]
    chemical = (
        BULK_COEF * (order_field * order_field * order_field - order_field) - STIFFNESS * laplace
    )
    forces = [chemical * slope for slope in slopes]
    moments = []
    for axis_id in range(3):
        moment = jnp.zeros_like(density)
        for number in range(19):
            comp = VELOCITIES[number][axis_id]
            if comp != 0:
                moment = moment + comp * f_pop[number]
        moments.append(moment)
    flows = [(moments[axis_id] + 0.5 * forces[axis_id]) / density for axis_id in range(3)]
    speed_sq = flows[0] * flows[0] + flows[1] * flows[1] + flows[2] * flows[2]
    flow_force = flows[0] * forces[0] + flows[1] * forces[1] + flows[2] * forces[2]
    f_posts = []
    g_eqs = []
    for number in range(19):
        weight = lattice_weight(number)
        proj_flow = along(number, flows, density)
        proj_force = along(number, forces, density)
        shape_term = 3.0 * proj_flow + 4.5 * proj_flow * proj_flow - 1.5 * speed_sq
        f_eq = weight * density * (1.0 + shape_term)
        source = (
            (1.0 - 0.5 / TAU_FLUID)
            * weight
            * (3.0 * (proj_force - flow_force) + 9.0 * proj_flow * proj_force)
        )
        f_posts.append(f_pop[number] - (f_pop[number] - f_eq) / TAU_FLUID + source)
        g_eqs.append(weight * (3.0 * chemical + order_field * shape_term))
    rest_eq = order_field
    for number in range(1, 19):
        rest_eq = rest_eq - g_eqs[number]
    g_eqs[0] = rest_eq
    g_posts = [g_pop[number] - (g_pop[number] - g_eqs[number]) / TAU_ORDER for number in range(19)]
    return (f_posts, g_posts)


def pop_groups(pops):
    vel = [VELOCITIES[n % pops] for n in range(2 * pops)]
    groups = {
        name: [n for n in range(2 * pops) if vel[n][axis_id] == sign]
        for name, axis_id, sign in (
            ("x_up", 0, 1), ("x_dn", 0, -1), ("y_up", 1, 1), ("y_dn", 1, -1), ("z_up", 2, 1), ("z_dn", 2, -1)
        )
    }
    order = groups["z_up"] + groups["z_dn"] + [n for n in range(2 * pops) if vel[n][2] == 0]
    slot = {n: i for i, n in enumerate(order)}
    return vel, groups, slot


def collide_kernel(f_ref, g_ref, nb_ref, post_ref, xu_ref, xd_ref, yu_ref, yd_ref):
    pops = f_ref.shape[0]
    nx, ny = f_ref.shape[1], f_ref.shape[2]
    vel, groups, slot = pop_groups(pops)
    for x in range(nx):
        f_planes = [f_ref[n, x] for n in range(pops)]
        g_planes = [g_ref[n, x] for n in range(pops)]
        slopes = [nb_ref[2 + a, x] for a in range(3)]
        f_posts, g_posts = collide_lists(f_planes, g_planes, nb_ref[0, x], nb_ref[1, x], slopes)
        planes = f_posts + g_posts
        for n in range(2 * pops):
            post_ref[slot[n], x] = planes[n]
        if x == nx - 1:
            for k, n in enumerate(groups["x_up"]):
                xu_ref[k] = planes[n]
        if x == 0:
            for k, n in enumerate(groups["x_dn"]):
                xd_ref[k] = planes[n]
        for k, n in enumerate(groups["y_up"]):
            yu_ref[k, pl.ds(x, 1), :] = planes[n][ny - 1 : ny, :]
        for k, n in enumerate(groups["y_dn"]):
            yd_ref[k, pl.ds(x, 1), :] = planes[n][0:1, :]


def stream_kernel(post_ref, xlow_ref, xhigh_ref, hym_ref, hyp_ref, col_ref, f_ref, g_ref):
    pops = f_ref.shape[0]
    nx, ny, nz = f_ref.shape[1:]
    row = lax.broadcasted_iota(jnp.int32, (ny, nz), 0)
    lane = lax.broadcasted_iota(jnp.int32, (ny, nz), 1)
    vel = [VELOCITIES[n % pops] for n in range(2 * pops)]
    x_up = [n for n in range(2 * pops) if vel[n][0] == 1]
    x_dn = [n for n in range(2 * pops) if vel[n][0] == -1]
    y_up = [n for n in range(2 * pops) if vel[n][1] == 1]
    y_dn = [n for n in range(2 * pops) if vel[n][1] == -1]
    z_any = [n for n in range(2 * pops) if vel[n][2] != 0]
    for n in range(2 * pops):
        cx, cy, cz = vel[n]
        out = f_ref if n < pops else g_ref
        for x in range(nx):
            src = x - cx
            if src < 0:
                tile = xlow_ref[x_up.index(n)]
            elif src >= nx:
                tile = xhigh_ref[x_dn.index(n)]
            else:
                tile = post_ref[pop_groups(pops)[2][n], src]
                if cy == 1:
                    edge = jnp.broadcast_to(hym_ref[pl.ds(y_up.index(n) * nx + src, 1), :], (ny, nz))
                    tile = jnp.where(row == 0, edge, pltpu.roll(tile, 1, 0))
                elif cy == -1:
                    edge = jnp.broadcast_to(hyp_ref[pl.ds(y_dn.index(n) * nx + src, 1), :], (ny, nz))
                    tile = jnp.where(row == ny - 1, edge, pltpu.roll(tile, ny - 1, 0))
            if 0 <= src < nx and cz == 1:
                tile = jnp.where(lane == 0, col_ref[z_any.index(n), x], pltpu.roll(tile, 1, 1))
            elif 0 <= src < nx and cz == -1:
                tile = jnp.where(lane == nz - 1, col_ref[z_any.index(n), x], pltpu.roll(tile, nz - 1, 1))
            out[n % pops, x] = tile


def exchange(sends):
    sizes = [lax.axis_size(a) for a in AXES]
    groups = {}
    order = []
    for index, (value, offset) in enumerate(sends):
        key = (tuple(o % n for o, n in zip(offset, sizes)), value.shape[1:])
        if key not in groups:
            groups[key] = []
            order.append(key)
        groups[key].append(index)
    results = [None] * len(sends)
    for key in order:
        members = groups[key]
        offset = key[0]
        pairs = []
        for i in range(sizes[0]):
            for j in range(sizes[1]):
                for k in range(sizes[2]):
                    src = (i * sizes[1] + j) * sizes[2] + k
                    ti, tj, tk = [(c + o) % n for c, o, n in zip((i, j, k), offset, sizes)]
                    pairs.append((src, (ti * sizes[1] + tj) * sizes[2] + tk))
        payload = [sends[m][0] for m in members]
        joined = payload[0] if len(payload) == 1 else jnp.concatenate(payload, axis=0)
        got = lax.ppermute(joined, AXES, pairs)
        start = 0
        for m in members:
            count = sends[m][0].shape[0]
            results[m] = got[start : start + count]
            start += count
    return results


def local(f_pop, g_pop, displacement):
    shift = displacement[0]
    nx, ny, nz = (f_pop.shape[1], f_pop.shape[2], f_pop.shape[3])
    q = SHIFT_MIN // ny
    assert SHIFT_MAX // ny == q and SHIFT_MIN % ny != 0
    rem = shift - q * ny

    phi = jnp.sum(g_pop, axis=0)
    up1, dn1, pzm, pzp = exchange(
        [
            (jnp.concatenate([phi[:, -1], phi[-1]]), (0, 1, 0)),
            (jnp.concatenate([phi[:, 0], phi[0]]), (0, -1, 0)),
            (phi[:, :, -1][None], (0, 0, 1)),
            (phi[:, :, 0][None], (0, 0, -1)),
        ]
    )
    low_pair, high_pair = exchange(
        [
            (jnp.concatenate([up1[nx:], phi[-1]]), (1, q, 0)),
            (jnp.concatenate([phi[0], dn1[nx:]]), (-1, -q, 0)),
        ]
    )
    low = lax.dynamic_slice_in_dim(low_pair, ny - rem, ny, 0)[None]
    high = lax.dynamic_slice_in_dim(high_pair, rem, ny, 0)[None]
    neigh_xm = jnp.concatenate([low, phi[:-1]], axis=0)
    neigh_xp = jnp.concatenate([phi[1:], high], axis=0)
    neigh_ym = jnp.concatenate([up1[:nx][:, None], phi[:, :-1]], axis=1)
    neigh_yp = jnp.concatenate([phi[:, 1:], dn1[:nx][:, None]], axis=1)
    neigh_zm = jnp.concatenate([pzm[0][:, :, None], phi[:, :, :-1]], axis=2)
    neigh_zp = jnp.concatenate([phi[:, :, 1:], pzp[0][:, :, None]], axis=2)
    laplace = neigh_xm + neigh_xp + neigh_ym + neigh_yp + neigh_zm + neigh_zp - 6.0 * phi
    slopes = [0.5 * (neigh_xp - neigh_xm), 0.5 * (neigh_yp - neigh_ym), 0.5 * (neigh_zp - neigh_zm)]
    nb = jnp.stack([phi, laplace] + slopes)
    pops = f_pop.shape[0]
    _, groups, slot = pop_groups(pops)
    n_xu, n_xd, n_yu, n_yd = (len(groups[k]) for k in ("x_up", "x_dn", "y_up", "y_dn"))
    post, face_xu, face_xd, face_yu, face_yd = pl.pallas_call(
        collide_kernel,
        out_shape=(
            jax.ShapeDtypeStruct((2 * pops, nx, ny, nz), jnp.float32),
            jax.ShapeDtypeStruct((n_xu, ny, nz), jnp.float32),
            jax.ShapeDtypeStruct((n_xd, ny, nz), jnp.float32),
            jax.ShapeDtypeStruct((n_yu, nx, nz), jnp.float32),
            jax.ShapeDtypeStruct((n_yd, nx, nz), jnp.float32),
        ),
        interpret=INTERPRET,
    )(f_pop, g_pop, nb)

    vel = [VELOCITIES[n % 19] for n in range(38)]

    def pick(cond, among=range(38)):
        return [n for n in among if cond(vel[n])]

    x_up = pick(lambda c: c[0] == 1)
    x_dn = pick(lambda c: c[0] == -1)
    y_up = pick(lambda c: c[1] == 1)
    y_dn = pick(lambda c: c[1] == -1)
    z_up = pick(lambda c: c[2] == 1)
    z_dn = pick(lambda c: c[2] == -1)
    xz_up = pick(lambda c: c[2] != 0, x_up)
    xz_dn = pick(lambda c: c[2] != 0, x_dn)
    yz_up = pick(lambda c: c[2] != 0, y_up)
    yz_dn = pick(lambda c: c[2] != 0, y_dn)

    def zhalo(n):
        return hz_m[z_up.index(n)] if vel[n][2] == 1 else hz_p[z_dn.index(n)]

    def lanes(a):
        return jnp.pad(a, ((0, 0), (0, nz - a.shape[1])))

    def packed(face, extra):
        return jnp.concatenate([face.reshape(-1, nz), lanes(jnp.stack(extra))], axis=0)

    sends = [
        (post[: len(z_up), :, :, -1], (0, 0, 1)),
        (post[len(z_up) : len(z_up) + len(z_dn), :, :, 0], (0, 0, -1)),
        (jnp.concatenate([face_yu.reshape(-1, nz), face_xu.reshape(-1, nz)]), (0, 1, 0)),
        (jnp.concatenate([face_yd.reshape(-1, nz), face_xd.reshape(-1, nz)]), (0, -1, 0)),
    ]
    diag_keys = []
    for dy in (1, -1):
        for dz in (1, -1):
            ypops = [n for n in (yz_up if dy == 1 else yz_dn) if vel[n][2] == dz]
            xpops = [n for n in (xz_up if dy == 1 else xz_dn) if vel[n][2] == dz]
            yrow, xrow, zl = (ny - 1, nx - 1, nz - 1 if dz == 1 else 0) if dy == 1 else (0, 0, nz - 1 if dz == 1 else 0)
            ys = jnp.stack([post[slot[n], :, yrow, zl] for n in ypops])
            xs = jnp.stack([post[slot[n], xrow, :, zl] for n in xpops])
            sends.append((jnp.concatenate([lanes(ys), lanes(xs)]), (0, dy, dz)))
            diag_keys.append((dy, dz, ypops, xpops))
    got = exchange(sends)
    hz_m, hz_p, up2, dn2 = got[:4]
    diag = dict(((dy, dz), (g, yp, xp)) for (dy, dz, yp, xp), g in zip(diag_keys, got[4:]))

    def edge_rows(dy, idx, kind):
        rows = []
        for n in idx:
            g, yp, xp = diag[(dy, vel[n][2])]
            rows.append(g[yp.index(n)][:nx] if kind == "y" else g[len(yp) + xp.index(n)][:ny])
        return jnp.stack(rows)

    cy_m = edge_rows(1, yz_up, "y")
    cy_p = edge_rows(-1, yz_dn, "y")
    n_face_u, n_face_d = face_yu.shape[0] * nx, face_yd.shape[0] * nx
    send_up = packed(face_xu, [zhalo(n)[-1] for n in xz_up])
    send_dn = packed(face_xd, [zhalo(n)[0] for n in xz_dn])
    from_up = jnp.concatenate([up2[n_face_u:], lanes(edge_rows(1, xz_up, "x"))])
    from_dn = jnp.concatenate([dn2[n_face_d:], lanes(edge_rows(-1, xz_dn, "x"))])

    def unpack_x(got, count):
        return got[: count * ny].reshape(count, ny, nz), got[count * ny :, :ny]

    def unpack_y(got, count):
        return got[: count * nx].reshape(count, nx, nz), got[count * nx :, :nx]

    def by_pop(idx, axis_id, shape):
        return jnp.array([vel[n][axis_id] for n in idx], jnp.int32).reshape(shape)

    def pick_y(win, idx):
        cy = by_pop(idx, 1, (-1, 1, 1))
        return jnp.where(cy == 1, win[:, :ny], jnp.where(cy == -1, win[:, 2:], win[:, 1 : ny + 1]))

    def shift_z(planes, idx, edge_cols, edge_idx):
        cz = by_pop(idx, 2, (-1, 1, 1))
        zero = jnp.zeros((1, ny), planes.dtype)
        col = jnp.concatenate([edge_cols, zero])[
            jnp.array([edge_idx.index(n) if n in edge_idx else len(edge_idx) for n in idx])
        ][:, :, None]
        return jnp.where(
            cz == 1,
            jnp.concatenate([col, planes[:, :, :-1]], axis=2),
            jnp.where(cz == -1, jnp.concatenate([planes[:, :, 1:], col], axis=2), planes),
        )

    def window(first, second, idx, edge_idx, start):
        count = len(idx)
        pa, ca = unpack_x(first, count)
        pb, cb = unpack_x(second, count)
        planes = lax.dynamic_slice_in_dim(jnp.concatenate([pa, pb], axis=1), start - 1, ny + 2, 1)
        cols = lax.dynamic_slice_in_dim(jnp.concatenate([ca, cb], axis=1), start, ny, 1)
        return shift_z(pick_y(planes, idx), idx, cols, edge_idx).reshape(-1, nz)

    low2, high2 = exchange(
        [
            (window(from_up, send_up, x_up, xz_up, ny - rem), (1, q, 0)),
            (window(send_dn, from_dn, x_dn, xz_dn, rem), (-1, -q, 0)),
        ]
    )

    xlow = low2.reshape(len(x_up), ny, nz)
    xhigh = high2.reshape(len(x_dn), ny, nz)
    z_any = pick(lambda c: c[2] != 0)
    zh = jnp.concatenate([hz_m, hz_p])[jnp.array([z_up.index(n) if vel[n][2] == 1 else len(z_up) + z_dn.index(n) for n in z_any])]

    def spread(values, idx):
        zero = jnp.zeros((1,) + values.shape[1:], values.dtype)
        both = jnp.concatenate([values, zero])
        return both[jnp.array([idx.index(n) if n in idx else len(idx) for n in z_any])]

    corner_m = spread(cy_m, yz_up)[:, :, None]
    corner_p = spread(cy_p, yz_dn)[:, :, None]
    cy = by_pop(z_any, 1, (-1, 1, 1))
    cx = by_pop(z_any, 0, (-1, 1, 1))
    down = jnp.concatenate([corner_m, zh[:, :, :-1]], axis=2)
    up = jnp.concatenate([zh[:, :, 1:], corner_p], axis=2)
    zy = jnp.where(cy == 1, down, jnp.where(cy == -1, up, zh))
    edge_low = jnp.zeros((len(z_any), 1, ny), jnp.float32)
    edge_high = edge_low
    cols = jnp.where(
        cx == 1,
        jnp.concatenate([edge_low, zy[:, :-1]], axis=1),
        jnp.where(cx == -1, jnp.concatenate([zy[:, 1:], edge_high], axis=1), zy),
    )
    cols = jnp.broadcast_to(cols[:, :, :, None], (len(z_any), nx, ny, nz))
    pops = f_pop.shape[0]
    f_new, g_new = pl.pallas_call(
        stream_kernel,
        out_shape=(
            jax.ShapeDtypeStruct((pops, nx, ny, nz), jnp.float32),
            jax.ShapeDtypeStruct((pops, nx, ny, nz), jnp.float32),
        ),
        interpret=INTERPRET,
    )(post, xlow, xhigh, up2, dn2, cols)
    return (f_new, g_new)


def solution(mesh):
    return jax.shard_map(
        local,
        mesh=mesh,
        in_specs=(P(None, "gx", "gy", "gz"), P(None, "gx", "gy", "gz"), P()),
        out_specs=(P(None, "gx", "gy", "gz"), P(None, "gx", "gy", "gz")),
        check_vma=False,
    )
```

```python
import jax
import jax.numpy as jnp
from jax import lax
from jax.sharding import PartitionSpec as P
from jax.experimental import pallas as pl
from jax.experimental.pallas import tpu as pltpu

VELOCITIES = [
    (0, 0, 0),
    (1, 0, 0),
    (1, 1, 0),
    (1, -1, 0),
    (1, 0, 1),
    (1, 0, -1),
    (-1, 0, 0),
    (-1, -1, 0),
    (-1, 1, 0),
    (-1, 0, -1),
    (-1, 0, 1),
    (0, 1, 0),
    (0, -1, 0),
    (0, 0, 1),
    (0, 0, -1),
    (0, 1, 1),
    (0, -1, -1),
    (0, 1, -1),
    (0, -1, 1),
]
BULK_COEF = 0.5
STIFFNESS = 0.5
TAU_FLUID = 0.8
TAU_ORDER = 0.9
SHIFT_MIN = 33
SHIFT_MAX = 47
AXES = ("gx", "gy", "gz")
INTERPRET = False


def lattice_weight(number):
    steps_sq = sum((abs(comp) for comp in VELOCITIES[number]))
    if steps_sq == 0:
        return 1.0 / 3.0
    if steps_sq == 1:
        return 1.0 / 18.0
    return 1.0 / 36.0


def along(number, values, base):
    result = jnp.zeros_like(base)
    for axis_id in range(3):
        comp = VELOCITIES[number][axis_id]
        if comp != 0:
            result = result + comp * values[axis_id]
    return result


def collide(f_pop, g_pop, order_field, laplace, slopes):
    density = jnp.sum(f_pop, axis=0)
    chemical = (
        BULK_COEF * (order_field * order_field * order_field - order_field) - STIFFNESS * laplace
    )
    forces = [chemical * slope for slope in slopes]
    moments = []
    for axis_id in range(3):
        moment = jnp.zeros_like(density)
        for number in range(19):
            comp = VELOCITIES[number][axis_id]
            if comp != 0:
                moment = moment + comp * f_pop[number]
        moments.append(moment)
    flows = [(moments[axis_id] + 0.5 * forces[axis_id]) / density for axis_id in range(3)]
    speed_sq = flows[0] * flows[0] + flows[1] * flows[1] + flows[2] * flows[2]
    flow_force = flows[0] * forces[0] + flows[1] * forces[1] + flows[2] * forces[2]
    f_posts = []
    g_eqs = []
    for number in range(19):
        weight = lattice_weight(number)
        proj_flow = along(number, flows, density)
        proj_force = along(number, forces, density)
        shape_term = 3.0 * proj_flow + 4.5 * proj_flow * proj_flow - 1.5 * speed_sq
        f_eq = weight * density * (1.0 + shape_term)
        source = (
            (1.0 - 0.5 / TAU_FLUID)
            * weight
            * (3.0 * (proj_force - flow_force) + 9.0 * proj_flow * proj_force)
        )
        f_posts.append(f_pop[number] - (f_pop[number] - f_eq) / TAU_FLUID + source)
        g_eqs.append(weight * (3.0 * chemical + order_field * shape_term))
    rest_eq = order_field
    for number in range(1, 19):
        rest_eq = rest_eq - g_eqs[number]
    g_eqs[0] = rest_eq
    g_posts = [g_pop[number] - (g_pop[number] - g_eqs[number]) / TAU_ORDER for number in range(19)]
    return (jnp.stack(f_posts), jnp.stack(g_posts))


def collide_lists(f_pop, g_pop, order_field, laplace, slopes):
    density = f_pop[0]
    for number in range(1, 19):
        density = density + f_pop[number]
    chemical = (
        BULK_COEF * (order_field * order_field * order_field - order_field) - STIFFNESS * laplace
    )
    forces = [chemical * slope for slope in slopes]
    moments = []
    for axis_id in range(3):
        moment = jnp.zeros_like(density)
        for number in range(19):
            comp = VELOCITIES[number][axis_id]
            if comp != 0:
                moment = moment + comp * f_pop[number]
        moments.append(moment)
    flows = [(moments[axis_id] + 0.5 * forces[axis_id]) / density for axis_id in range(3)]
    speed_sq = flows[0] * flows[0] + flows[1] * flows[1] + flows[2] * flows[2]
    flow_force = flows[0] * forces[0] + flows[1] * forces[1] + flows[2] * forces[2]
    f_posts = []
    g_eqs = []
    for number in range(19):
        weight = lattice_weight(number)
        proj_flow = along(number, flows, density)
        proj_force = along(number, forces, density)
        shape_term = 3.0 * proj_flow + 4.5 * proj_flow * proj_flow - 1.5 * speed_sq
        f_eq = weight * density * (1.0 + shape_term)
        source = (
            (1.0 - 0.5 / TAU_FLUID)
            * weight
            * (3.0 * (proj_force - flow_force) + 9.0 * proj_flow * proj_force)
        )
        f_posts.append(f_pop[number] - (f_pop[number] - f_eq) / TAU_FLUID + source)
        g_eqs.append(weight * (3.0 * chemical + order_field * shape_term))
    rest_eq = order_field
    for number in range(1, 19):
        rest_eq = rest_eq - g_eqs[number]
    g_eqs[0] = rest_eq
    g_posts = [g_pop[number] - (g_pop[number] - g_eqs[number]) / TAU_ORDER for number in range(19)]
    return (f_posts, g_posts)


def pop_groups(pops):
    vel = [VELOCITIES[n % pops] for n in range(2 * pops)]
    groups = {
        name: [n for n in range(2 * pops) if vel[n][axis_id] == sign]
        for name, axis_id, sign in (
            ("x_up", 0, 1), ("x_dn", 0, -1), ("y_up", 1, 1), ("y_dn", 1, -1), ("z_up", 2, 1), ("z_dn", 2, -1)
        )
    }
    order = groups["z_up"] + groups["z_dn"] + [n for n in range(2 * pops) if vel[n][2] == 0]
    slot = {n: i for i, n in enumerate(order)}
    return vel, groups, slot


def collide_kernel(f_ref, g_ref, nb_ref, post_ref, xu_ref, xd_ref, yu_ref, yd_ref):
    pops = f_ref.shape[0]
    ny = f_ref.shape[2]
    nx = pl.num_programs(0)
    x = pl.program_id(0)
    vel, groups, slot = pop_groups(pops)
    f_planes = [f_ref[n, 0] for n in range(pops)]
    g_planes = [g_ref[n, 0] for n in range(pops)]
    slopes = [nb_ref[2 + a, 0] for a in range(3)]
    f_posts, g_posts = collide_lists(f_planes, g_planes, nb_ref[0, 0], nb_ref[1, 0], slopes)
    planes = f_posts + g_posts
    for n in range(2 * pops):
        post_ref[slot[n], 0] = planes[n]

    @pl.when(x == nx - 1)
    def _():
        for k, n in enumerate(groups["x_up"]):
            xu_ref[k] = planes[n]

    @pl.when(x == 0)
    def _():
        for k, n in enumerate(groups["x_dn"]):
            xd_ref[k] = planes[n]

    for k, n in enumerate(groups["y_up"]):
        yu_ref[0, pl.ds(k, 1), :] = planes[n][ny - 1 : ny, :]
    for k, n in enumerate(groups["y_dn"]):
        yd_ref[0, pl.ds(k, 1), :] = planes[n][0:1, :]


def stream_kernel(post_ref, xlow_ref, xhigh_ref, hym_ref, hyp_ref, col_ref, f_ref, g_ref):
    pops = f_ref.shape[0]
    nx, ny, nz = f_ref.shape[1:]
    row = lax.broadcasted_iota(jnp.int32, (ny, nz), 0)
    lane = lax.broadcasted_iota(jnp.int32, (ny, nz), 1)
    vel = [VELOCITIES[n % pops] for n in range(2 * pops)]
    x_up = [n for n in range(2 * pops) if vel[n][0] == 1]
    x_dn = [n for n in range(2 * pops) if vel[n][0] == -1]
    y_up = [n for n in range(2 * pops) if vel[n][1] == 1]
    y_dn = [n for n in range(2 * pops) if vel[n][1] == -1]
    z_any = [n for n in range(2 * pops) if vel[n][2] != 0]
    for n in range(2 * pops):
        cx, cy, cz = vel[n]
        out = f_ref if n < pops else g_ref
        for x in range(nx):
            src = x - cx
            if src < 0:
                tile = xlow_ref[x_up.index(n)]
            elif src >= nx:
                tile = xhigh_ref[x_dn.index(n)]
            else:
                tile = post_ref[pop_groups(pops)[2][n], src]
                if cy == 1:
                    edge = jnp.broadcast_to(hym_ref[pl.ds(src * len(y_up) + y_up.index(n), 1), :], (ny, nz))
                    tile = jnp.where(row == 0, edge, pltpu.roll(tile, 1, 0))
                elif cy == -1:
                    edge = jnp.broadcast_to(hyp_ref[pl.ds(src * len(y_dn) + y_dn.index(n), 1), :], (ny, nz))
                    tile = jnp.where(row == ny - 1, edge, pltpu.roll(tile, ny - 1, 0))
            if 0 <= src < nx and cz == 1:
                tile = jnp.where(lane == 0, col_ref[z_any.index(n), x], pltpu.roll(tile, 1, 1))
            elif 0 <= src < nx and cz == -1:
                tile = jnp.where(lane == nz - 1, col_ref[z_any.index(n), x], pltpu.roll(tile, nz - 1, 1))
            out[n % pops, x] = tile


def exchange(sends):
    sizes = [lax.axis_size(a) for a in AXES]
    groups = {}
    order = []
    for index, (value, offset) in enumerate(sends):
        key = (tuple(o % n for o, n in zip(offset, sizes)), value.shape[1:])
        if key not in groups:
            groups[key] = []
            order.append(key)
        groups[key].append(index)
    results = [None] * len(sends)
    for key in order:
        members = groups[key]
        offset = key[0]
        pairs = []
        for i in range(sizes[0]):
            for j in range(sizes[1]):
                for k in range(sizes[2]):
                    src = (i * sizes[1] + j) * sizes[2] + k
                    ti, tj, tk = [(c + o) % n for c, o, n in zip((i, j, k), offset, sizes)]
                    pairs.append((src, (ti * sizes[1] + tj) * sizes[2] + tk))
        payload = [sends[m][0] for m in members]
        joined = payload[0] if len(payload) == 1 else jnp.concatenate(payload, axis=0)
        got = lax.ppermute(joined, AXES, pairs)
        start = 0
        for m in members:
            count = sends[m][0].shape[0]
            results[m] = got[start : start + count]
            start += count
    return results


def local(f_pop, g_pop, displacement):
    shift = displacement[0]
    nx, ny, nz = (f_pop.shape[1], f_pop.shape[2], f_pop.shape[3])
    q = SHIFT_MIN // ny
    assert SHIFT_MAX // ny == q and SHIFT_MIN % ny != 0
    rem = shift - q * ny

    phi = jnp.sum(g_pop, axis=0)
    up1, dn1, pzm, pzp = exchange(
        [
            (jnp.concatenate([phi[:, -1], phi[-1]]), (0, 1, 0)),
            (jnp.concatenate([phi[:, 0], phi[0]]), (0, -1, 0)),
            (phi[:, :, -1][None], (0, 0, 1)),
            (phi[:, :, 0][None], (0, 0, -1)),
        ]
    )
    low_pair, high_pair = exchange(
        [
            (jnp.concatenate([up1[nx:], phi[-1]]), (1, q, 0)),
            (jnp.concatenate([phi[0], dn1[nx:]]), (-1, -q, 0)),
        ]
    )
    low = lax.dynamic_slice_in_dim(low_pair, ny - rem, ny, 0)[None]
    high = lax.dynamic_slice_in_dim(high_pair, rem, ny, 0)[None]
    neigh_xm = jnp.concatenate([low, phi[:-1]], axis=0)
    neigh_xp = jnp.concatenate([phi[1:], high], axis=0)
    neigh_ym = jnp.concatenate([up1[:nx][:, None], phi[:, :-1]], axis=1)
    neigh_yp = jnp.concatenate([phi[:, 1:], dn1[:nx][:, None]], axis=1)
    neigh_zm = jnp.concatenate([pzm[0][:, :, None], phi[:, :, :-1]], axis=2)
    neigh_zp = jnp.concatenate([phi[:, :, 1:], pzp[0][:, :, None]], axis=2)
    laplace = neigh_xm + neigh_xp + neigh_ym + neigh_yp + neigh_zm + neigh_zp - 6.0 * phi
    slopes = [0.5 * (neigh_xp - neigh_xm), 0.5 * (neigh_yp - neigh_ym), 0.5 * (neigh_zp - neigh_zm)]
    nb = jnp.stack([phi, laplace] + slopes)
    pops = f_pop.shape[0]
    _, groups, slot = pop_groups(pops)
    n_xu, n_xd, n_yu, n_yd = (len(groups[k]) for k in ("x_up", "x_dn", "y_up", "y_dn"))
    def plane_block(count):
        return pl.BlockSpec((count, 1, ny, nz), lambda x: (0, x, 0, 0))

    def whole(shape):
        return pl.BlockSpec(shape, lambda x: (0,) * len(shape))

    post, face_xu, face_xd, face_yu, face_yd = pl.pallas_call(
        collide_kernel,
        grid=(nx,),
        in_specs=[plane_block(pops), plane_block(pops), plane_block(nb.shape[0])],
        out_specs=(
            plane_block(2 * pops),
            whole((n_xu, ny, nz)),
            whole((n_xd, ny, nz)),
            pl.BlockSpec((1, n_yu, nz), lambda x: (x, 0, 0)),
            pl.BlockSpec((1, n_yd, nz), lambda x: (x, 0, 0)),
        ),
        out_shape=(
            jax.ShapeDtypeStruct((2 * pops, nx, ny, nz), jnp.float32),
            jax.ShapeDtypeStruct((n_xu, ny, nz), jnp.float32),
            jax.ShapeDtypeStruct((n_xd, ny, nz), jnp.float32),
            jax.ShapeDtypeStruct((nx, n_yu, nz), jnp.float32),
            jax.ShapeDtypeStruct((nx, n_yd, nz), jnp.float32),
        ),
        interpret=INTERPRET,
    )(f_pop, g_pop, nb)

    vel = [VELOCITIES[n % 19] for n in range(38)]

    def pick(cond, among=range(38)):
        return [n for n in among if cond(vel[n])]

    x_up = pick(lambda c: c[0] == 1)
    x_dn = pick(lambda c: c[0] == -1)
    y_up = pick(lambda c: c[1] == 1)
    y_dn = pick(lambda c: c[1] == -1)
    z_up = pick(lambda c: c[2] == 1)
    z_dn = pick(lambda c: c[2] == -1)
    xz_up = pick(lambda c: c[2] != 0, x_up)
    xz_dn = pick(lambda c: c[2] != 0, x_dn)
    yz_up = pick(lambda c: c[2] != 0, y_up)
    yz_dn = pick(lambda c: c[2] != 0, y_dn)

    hz_m, hz_p = exchange(
        [
            (post[: len(z_up), :, :, -1], (0, 0, 1)),
            (post[len(z_up) : len(z_up) + len(z_dn), :, :, 0], (0, 0, -1)),
        ]
    )

    def zhalo(n):
        return hz_m[z_up.index(n)] if vel[n][2] == 1 else hz_p[z_dn.index(n)]

    def lanes(a):
        return jnp.pad(a, ((0, 0), (0, nz - a.shape[1])))

    def packed(face, extra):
        return jnp.concatenate([face.reshape(-1, nz), lanes(jnp.stack(extra))], axis=0)

    send_up = packed(face_xu, [zhalo(n)[-1] for n in xz_up])
    send_dn = packed(face_xd, [zhalo(n)[0] for n in xz_dn])
    send_yu = packed(face_yu, [zhalo(n)[:, -1] for n in yz_up])
    send_yd = packed(face_yd, [zhalo(n)[:, 0] for n in yz_dn])
    n_yu, n_yd = send_yu.shape[0], send_yd.shape[0]
    up2, dn2 = exchange(
        [
            (jnp.concatenate([send_yu, send_up]), (0, 1, 0)),
            (jnp.concatenate([send_yd, send_dn]), (0, -1, 0)),
        ]
    )
    hy_m, hy_p = up2[:n_yu], dn2[:n_yd]

    def unpack_x(got, count):
        return got[: count * ny].reshape(count, ny, nz), got[count * ny :, :ny]

    def unpack_y(got, count):
        return got[: count * nx].reshape(count, nx, nz), got[count * nx :, :nx]

    def by_pop(idx, axis_id, shape):
        return jnp.array([vel[n][axis_id] for n in idx], jnp.int32).reshape(shape)

    def pick_y(win, idx):
        cy = by_pop(idx, 1, (-1, 1, 1))
        return jnp.where(cy == 1, win[:, :ny], jnp.where(cy == -1, win[:, 2:], win[:, 1 : ny + 1]))

    def shift_z(planes, idx, edge_cols, edge_idx):
        cz = by_pop(idx, 2, (-1, 1, 1))
        zero = jnp.zeros((1, ny), planes.dtype)
        col = jnp.concatenate([edge_cols, zero])[
            jnp.array([edge_idx.index(n) if n in edge_idx else len(edge_idx) for n in idx])
        ][:, :, None]
        return jnp.where(
            cz == 1,
            jnp.concatenate([col, planes[:, :, :-1]], axis=2),
            jnp.where(cz == -1, jnp.concatenate([planes[:, :, 1:], col], axis=2), planes),
        )

    def window(first, second, idx, edge_idx, start):
        count = len(idx)
        pa, ca = unpack_x(first, count)
        pb, cb = unpack_x(second, count)
        planes = lax.dynamic_slice_in_dim(jnp.concatenate([pa, pb], axis=1), start - 1, ny + 2, 1)
        cols = lax.dynamic_slice_in_dim(jnp.concatenate([ca, cb], axis=1), start, ny, 1)
        return shift_z(pick_y(planes, idx), idx, cols, edge_idx).reshape(-1, nz)

    low2, high2 = exchange(
        [
            (window(up2[n_yu:], send_up, x_up, xz_up, ny - rem), (1, q, 0)),
            (window(send_dn, dn2[n_yd:], x_dn, xz_dn, rem), (-1, -q, 0)),
        ]
    )
    hy_m, cy_m = unpack_y(hy_m, len(y_up))
    hy_p, cy_p = unpack_y(hy_p, len(y_dn))

    xlow = low2.reshape(len(x_up), ny, nz)
    xhigh = high2.reshape(len(x_dn), ny, nz)
    z_any = pick(lambda c: c[2] != 0)
    zh = jnp.concatenate([hz_m, hz_p])[jnp.array([z_up.index(n) if vel[n][2] == 1 else len(z_up) + z_dn.index(n) for n in z_any])]

    def spread(values, idx):
        zero = jnp.zeros((1,) + values.shape[1:], values.dtype)
        both = jnp.concatenate([values, zero])
        return both[jnp.array([idx.index(n) if n in idx else len(idx) for n in z_any])]

    corner_m = spread(cy_m, yz_up)[:, :, None]
    corner_p = spread(cy_p, yz_dn)[:, :, None]
    cy = by_pop(z_any, 1, (-1, 1, 1))
    cx = by_pop(z_any, 0, (-1, 1, 1))
    down = jnp.concatenate([corner_m, zh[:, :, :-1]], axis=2)
    up = jnp.concatenate([zh[:, :, 1:], corner_p], axis=2)
    zy = jnp.where(cy == 1, down, jnp.where(cy == -1, up, zh))
    edge_low = jnp.zeros((len(z_any), 1, ny), jnp.float32)
    edge_high = edge_low
    cols = jnp.where(
        cx == 1,
        jnp.concatenate([edge_low, zy[:, :-1]], axis=1),
        jnp.where(cx == -1, jnp.concatenate([zy[:, 1:], edge_high], axis=1), zy),
    )
    cols = jnp.broadcast_to(cols[:, :, :, None], (len(z_any), nx, ny, nz))
    pops = f_pop.shape[0]
    f_new, g_new = pl.pallas_call(
        stream_kernel,
        out_shape=(
            jax.ShapeDtypeStruct((pops, nx, ny, nz), jnp.float32),
            jax.ShapeDtypeStruct((pops, nx, ny, nz), jnp.float32),
        ),
        interpret=INTERPRET,
    )(post, xlow, xhigh, up2, dn2, cols)
    return (f_new, g_new)


def solution(mesh):
    return jax.shard_map(
        local,
        mesh=mesh,
        in_specs=(P(None, "gx", "gy", "gz"), P(None, "gx", "gy", "gz"), P()),
        out_specs=(P(None, "gx", "gy", "gz"), P(None, "gx", "gy", "gz")),
        check_vma=False,
    )
```

```python
import jax
import jax.numpy as jnp
from jax import lax
from jax.sharding import PartitionSpec as P
from jax.experimental import pallas as pl
from jax.experimental.pallas import tpu as pltpu

VELOCITIES = [
    (0, 0, 0),
    (1, 0, 0),
    (1, 1, 0),
    (1, -1, 0),
    (1, 0, 1),
    (1, 0, -1),
    (-1, 0, 0),
    (-1, -1, 0),
    (-1, 1, 0),
    (-1, 0, -1),
    (-1, 0, 1),
    (0, 1, 0),
    (0, -1, 0),
    (0, 0, 1),
    (0, 0, -1),
    (0, 1, 1),
    (0, -1, -1),
    (0, 1, -1),
    (0, -1, 1),
]
BULK_COEF = 0.5
STIFFNESS = 0.5
TAU_FLUID = 0.8
TAU_ORDER = 0.9
SHIFT_MIN = 33
SHIFT_MAX = 47
AXES = ("gx", "gy", "gz")
INTERPRET = False


def lattice_weight(number):
    steps_sq = sum((abs(comp) for comp in VELOCITIES[number]))
    if steps_sq == 0:
        return 1.0 / 3.0
    if steps_sq == 1:
        return 1.0 / 18.0
    return 1.0 / 36.0


def along(number, values, base):
    result = jnp.zeros_like(base)
    for axis_id in range(3):
        comp = VELOCITIES[number][axis_id]
        if comp != 0:
            result = result + comp * values[axis_id]
    return result


def collide(f_pop, g_pop, order_field, laplace, slopes):
    density = jnp.sum(f_pop, axis=0)
    chemical = (
        BULK_COEF * (order_field * order_field * order_field - order_field) - STIFFNESS * laplace
    )
    forces = [chemical * slope for slope in slopes]
    moments = []
    for axis_id in range(3):
        moment = jnp.zeros_like(density)
        for number in range(19):
            comp = VELOCITIES[number][axis_id]
            if comp != 0:
                moment = moment + comp * f_pop[number]
        moments.append(moment)
    flows = [(moments[axis_id] + 0.5 * forces[axis_id]) / density for axis_id in range(3)]
    speed_sq = flows[0] * flows[0] + flows[1] * flows[1] + flows[2] * flows[2]
    flow_force = flows[0] * forces[0] + flows[1] * forces[1] + flows[2] * forces[2]
    f_posts = []
    g_eqs = []
    for number in range(19):
        weight = lattice_weight(number)
        proj_flow = along(number, flows, density)
        proj_force = along(number, forces, density)
        shape_term = 3.0 * proj_flow + 4.5 * proj_flow * proj_flow - 1.5 * speed_sq
        f_eq = weight * density * (1.0 + shape_term)
        source = (
            (1.0 - 0.5 / TAU_FLUID)
            * weight
            * (3.0 * (proj_force - flow_force) + 9.0 * proj_flow * proj_force)
        )
        f_posts.append(f_pop[number] - (f_pop[number] - f_eq) / TAU_FLUID + source)
        g_eqs.append(weight * (3.0 * chemical + order_field * shape_term))
    rest_eq = order_field
    for number in range(1, 19):
        rest_eq = rest_eq - g_eqs[number]
    g_eqs[0] = rest_eq
    g_posts = [g_pop[number] - (g_pop[number] - g_eqs[number]) / TAU_ORDER for number in range(19)]
    return (jnp.stack(f_posts), jnp.stack(g_posts))


def collide_lists(f_pop, g_pop, order_field, laplace, slopes):
    density = f_pop[0]
    for number in range(1, 19):
        density = density + f_pop[number]
    chemical = (
        BULK_COEF * (order_field * order_field * order_field - order_field) - STIFFNESS * laplace
    )
    forces = [chemical * slope for slope in slopes]
    moments = []
    for axis_id in range(3):
        moment = jnp.zeros_like(density)
        for number in range(19):
            comp = VELOCITIES[number][axis_id]
            if comp != 0:
                moment = moment + comp * f_pop[number]
        moments.append(moment)
    flows = [(moments[axis_id] + 0.5 * forces[axis_id]) / density for axis_id in range(3)]
    speed_sq = flows[0] * flows[0] + flows[1] * flows[1] + flows[2] * flows[2]
    flow_force = flows[0] * forces[0] + flows[1] * forces[1] + flows[2] * forces[2]
    f_posts = []
    g_eqs = []
    for number in range(19):
        weight = lattice_weight(number)
        proj_flow = along(number, flows, density)
        proj_force = along(number, forces, density)
        shape_term = 3.0 * proj_flow + 4.5 * proj_flow * proj_flow - 1.5 * speed_sq
        f_eq = weight * density * (1.0 + shape_term)
        source = (
            (1.0 - 0.5 / TAU_FLUID)
            * weight
            * (3.0 * (proj_force - flow_force) + 9.0 * proj_flow * proj_force)
        )
        f_posts.append(f_pop[number] - (f_pop[number] - f_eq) / TAU_FLUID + source)
        g_eqs.append(weight * (3.0 * chemical + order_field * shape_term))
    rest_eq = order_field
    for number in range(1, 19):
        rest_eq = rest_eq - g_eqs[number]
    g_eqs[0] = rest_eq
    g_posts = [g_pop[number] - (g_pop[number] - g_eqs[number]) / TAU_ORDER for number in range(19)]
    return (f_posts, g_posts)


def pop_groups(pops):
    vel = [VELOCITIES[n % pops] for n in range(2 * pops)]
    groups = {
        name: [n for n in range(2 * pops) if vel[n][axis_id] == sign]
        for name, axis_id, sign in (
            ("x_up", 0, 1), ("x_dn", 0, -1), ("y_up", 1, 1), ("y_dn", 1, -1), ("z_up", 2, 1), ("z_dn", 2, -1)
        )
    }
    order = groups["z_up"] + groups["z_dn"] + [n for n in range(2 * pops) if vel[n][2] == 0]
    slot = {n: i for i, n in enumerate(order)}
    return vel, groups, slot


def collide_kernel(f_ref, g_ref, nb_ref, post_ref, xu_ref, xd_ref, yu_ref, yd_ref):
    pops = f_ref.shape[0]
    nx, ny = f_ref.shape[1], f_ref.shape[2]
    vel, groups, slot = pop_groups(pops)
    for x in range(nx):
        f_planes = [f_ref[n, x] for n in range(pops)]
        g_planes = [g_ref[n, x] for n in range(pops)]
        slopes = [nb_ref[2 + a, x] for a in range(3)]
        f_posts, g_posts = collide_lists(f_planes, g_planes, nb_ref[0, x], nb_ref[1, x], slopes)
        planes = f_posts + g_posts
        for n in range(2 * pops):
            post_ref[slot[n], x] = planes[n]
        if x == nx - 1:
            for k, n in enumerate(groups["x_up"]):
                xu_ref[k] = planes[n]
        if x == 0:
            for k, n in enumerate(groups["x_dn"]):
                xd_ref[k] = planes[n]
        for k, n in enumerate(groups["y_up"]):
            yu_ref[k, pl.ds(x, 1), :] = planes[n][ny - 1 : ny, :]
        for k, n in enumerate(groups["y_dn"]):
            yd_ref[k, pl.ds(x, 1), :] = planes[n][0:1, :]


def stream_kernel(post_ref, xlow_ref, xhigh_ref, hym_ref, hyp_ref, col_ref, f_ref, g_ref):
    pops = f_ref.shape[0]
    nx, ny, nz = f_ref.shape[1:]
    row = lax.broadcasted_iota(jnp.int32, (ny, nz), 0)
    lane = lax.broadcasted_iota(jnp.int32, (ny, nz), 1)
    vel = [VELOCITIES[n % pops] for n in range(2 * pops)]
    x_up = [n for n in range(2 * pops) if vel[n][0] == 1]
    x_dn = [n for n in range(2 * pops) if vel[n][0] == -1]
    y_up = [n for n in range(2 * pops) if vel[n][1] == 1]
    y_dn = [n for n in range(2 * pops) if vel[n][1] == -1]
    z_any = [n for n in range(2 * pops) if vel[n][2] != 0]
    for n in range(2 * pops):
        cx, cy, cz = vel[n]
        out = f_ref if n < pops else g_ref
        for x in range(nx):
            src = x - cx
            if src < 0:
                tile = xlow_ref[x_up.index(n)]
            elif src >= nx:
                tile = xhigh_ref[x_dn.index(n)]
            else:
                tile = post_ref[pop_groups(pops)[2][n], src]
                if cy == 1:
                    edge = jnp.broadcast_to(hym_ref[pl.ds(y_up.index(n) * nx + src, 1), :], (ny, nz))
                    tile = jnp.where(row == 0, edge, pltpu.roll(tile, 1, 0))
                elif cy == -1:
                    edge = jnp.broadcast_to(hyp_ref[pl.ds(y_dn.index(n) * nx + src, 1), :], (ny, nz))
                    tile = jnp.where(row == ny - 1, edge, pltpu.roll(tile, ny - 1, 0))
            if 0 <= src < nx and cz == 1:
                tile = jnp.where(lane == 0, col_ref[z_any.index(n), x], pltpu.roll(tile, 1, 1))
            elif 0 <= src < nx and cz == -1:
                tile = jnp.where(lane == nz - 1, col_ref[z_any.index(n), x], pltpu.roll(tile, nz - 1, 1))
            out[n % pops, x] = tile


def exchange(sends):
    sizes = [lax.axis_size(a) for a in AXES]
    groups = {}
    order = []
    for index, (value, offset) in enumerate(sends):
        key = (tuple(o % n for o, n in zip(offset, sizes)), value.shape[1:])
        if key not in groups:
            groups[key] = []
            order.append(key)
        groups[key].append(index)
    results = [None] * len(sends)
    for key in order:
        members = groups[key]
        offset = key[0]
        pairs = []
        for i in range(sizes[0]):
            for j in range(sizes[1]):
                for k in range(sizes[2]):
                    src = (i * sizes[1] + j) * sizes[2] + k
                    ti, tj, tk = [(c + o) % n for c, o, n in zip((i, j, k), offset, sizes)]
                    pairs.append((src, (ti * sizes[1] + tj) * sizes[2] + tk))
        payload = [sends[m][0] for m in members]
        joined = payload[0] if len(payload) == 1 else jnp.concatenate(payload, axis=0)
        got = lax.ppermute(joined, AXES, pairs)
        start = 0
        for m in members:
            count = sends[m][0].shape[0]
            results[m] = got[start : start + count]
            start += count
    return results


def local(f_pop, g_pop, displacement):
    shift = displacement[0]
    nx, ny, nz = (f_pop.shape[1], f_pop.shape[2], f_pop.shape[3])
    q = SHIFT_MIN // ny
    assert SHIFT_MAX // ny == q and SHIFT_MIN % ny != 0
    rem = shift - q * ny

    phi = jnp.sum(g_pop, axis=0)
    up1, dn1, pzm, pzp = exchange(
        [
            (jnp.concatenate([phi[:, -1], phi[0]]), (0, 1, 0)),
            (jnp.concatenate([phi[:, 0], phi[-1]]), (0, -1, 0)),
            (phi[:, :, -1][None], (0, 0, 1)),
            (phi[:, :, 0][None], (0, 0, -1)),
        ]
    )
    low_pair, high_pair = exchange(
        [
            (jnp.concatenate([phi[-1], dn1[nx:]]), (1, q + 1, 0)),
            (jnp.concatenate([up1[nx:], phi[0]]), (-1, -q - 1, 0)),
        ]
    )
    low = lax.dynamic_slice_in_dim(low_pair, ny - rem, ny, 0)[None]
    high = lax.dynamic_slice_in_dim(high_pair, rem, ny, 0)[None]
    neigh_xm = jnp.concatenate([low, phi[:-1]], axis=0)
    neigh_xp = jnp.concatenate([phi[1:], high], axis=0)
    neigh_ym = jnp.concatenate([up1[:nx][:, None], phi[:, :-1]], axis=1)
    neigh_yp = jnp.concatenate([phi[:, 1:], dn1[:nx][:, None]], axis=1)
    neigh_zm = jnp.concatenate([pzm[0][:, :, None], phi[:, :, :-1]], axis=2)
    neigh_zp = jnp.concatenate([phi[:, :, 1:], pzp[0][:, :, None]], axis=2)
    laplace = neigh_xm + neigh_xp + neigh_ym + neigh_yp + neigh_zm + neigh_zp - 6.0 * phi
    slopes = [0.5 * (neigh_xp - neigh_xm), 0.5 * (neigh_yp - neigh_ym), 0.5 * (neigh_zp - neigh_zm)]
    nb = jnp.stack([phi, laplace] + slopes)
    pops = f_pop.shape[0]
    _, groups, slot = pop_groups(pops)
    n_xu, n_xd, n_yu, n_yd = (len(groups[k]) for k in ("x_up", "x_dn", "y_up", "y_dn"))
    post, face_xu, face_xd, face_yu, face_yd = pl.pallas_call(
        collide_kernel,
        out_shape=(
            jax.ShapeDtypeStruct((2 * pops, nx, ny, nz), jnp.float32),
            jax.ShapeDtypeStruct((n_xu, ny, nz), jnp.float32),
            jax.ShapeDtypeStruct((n_xd, ny, nz), jnp.float32),
            jax.ShapeDtypeStruct((n_yu, nx, nz), jnp.float32),
            jax.ShapeDtypeStruct((n_yd, nx, nz), jnp.float32),
        ),
        interpret=INTERPRET,
    )(f_pop, g_pop, nb)

    vel = [VELOCITIES[n % 19] for n in range(38)]

    def pick(cond, among=range(38)):
        return [n for n in among if cond(vel[n])]

    x_up = pick(lambda c: c[0] == 1)
    x_dn = pick(lambda c: c[0] == -1)
    y_up = pick(lambda c: c[1] == 1)
    y_dn = pick(lambda c: c[1] == -1)
    z_up = pick(lambda c: c[2] == 1)
    z_dn = pick(lambda c: c[2] == -1)
    xz_up = pick(lambda c: c[2] != 0, x_up)
    xz_dn = pick(lambda c: c[2] != 0, x_dn)
    yz_up = pick(lambda c: c[2] != 0, y_up)
    yz_dn = pick(lambda c: c[2] != 0, y_dn)

    hz_m, hz_p = exchange(
        [
            (post[: len(z_up), :, :, -1], (0, 0, 1)),
            (post[len(z_up) : len(z_up) + len(z_dn), :, :, 0], (0, 0, -1)),
        ]
    )

    def zhalo(n):
        return hz_m[z_up.index(n)] if vel[n][2] == 1 else hz_p[z_dn.index(n)]

    def lanes(a):
        return jnp.pad(a, ((0, 0), (0, nz - a.shape[1])))

    def packed(face, extra):
        return jnp.concatenate([face.reshape(-1, nz), lanes(jnp.stack(extra))], axis=0)

    send_up = packed(face_xu, [zhalo(n)[-1] for n in xz_up])
    send_dn = packed(face_xd, [zhalo(n)[0] for n in xz_dn])
    send_yu = packed(face_yu, [zhalo(n)[:, -1] for n in yz_up])
    send_yd = packed(face_yd, [zhalo(n)[:, 0] for n in yz_dn])
    n_yu, n_yd = send_yu.shape[0], send_yd.shape[0]
    up2, dn2 = exchange(
        [
            (jnp.concatenate([send_yu, send_dn]), (0, 1, 0)),
            (jnp.concatenate([send_yd, send_up]), (0, -1, 0)),
        ]
    )
    hy_m, hy_p = up2[:n_yu], dn2[:n_yd]

    def unpack_x(got, count):
        return got[: count * ny].reshape(count, ny, nz), got[count * ny :, :ny]

    def unpack_y(got, count):
        return got[: count * nx].reshape(count, nx, nz), got[count * nx :, :nx]

    def by_pop(idx, axis_id, shape):
        return jnp.array([vel[n][axis_id] for n in idx], jnp.int32).reshape(shape)

    def pick_y(win, idx):
        cy = by_pop(idx, 1, (-1, 1, 1))
        return jnp.where(cy == 1, win[:, :ny], jnp.where(cy == -1, win[:, 2:], win[:, 1 : ny + 1]))

    def shift_z(planes, idx, edge_cols, edge_idx):
        cz = by_pop(idx, 2, (-1, 1, 1))
        zero = jnp.zeros((1, ny), planes.dtype)
        col = jnp.concatenate([edge_cols, zero])[
            jnp.array([edge_idx.index(n) if n in edge_idx else len(edge_idx) for n in idx])
        ][:, :, None]
        return jnp.where(
            cz == 1,
            jnp.concatenate([col, planes[:, :, :-1]], axis=2),
            jnp.where(cz == -1, jnp.concatenate([planes[:, :, 1:], col], axis=2), planes),
        )

    def window(first, second, idx, edge_idx, start):
        count = len(idx)
        pa, ca = unpack_x(first, count)
        pb, cb = unpack_x(second, count)
        planes = lax.dynamic_slice_in_dim(jnp.concatenate([pa, pb], axis=1), start - 1, ny + 2, 1)
        cols = lax.dynamic_slice_in_dim(jnp.concatenate([ca, cb], axis=1), start, ny, 1)
        return shift_z(pick_y(planes, idx), idx, cols, edge_idx).reshape(-1, nz)

    low2, high2 = exchange(
        [
            (window(send_up, dn2[n_yd:], x_up, xz_up, ny - rem), (1, q + 1, 0)),
            (window(up2[n_yu:], send_dn, x_dn, xz_dn, rem), (-1, -q - 1, 0)),
        ]
    )
    hy_m, cy_m = unpack_y(hy_m, len(y_up))
    hy_p, cy_p = unpack_y(hy_p, len(y_dn))

    xlow = low2.reshape(len(x_up), ny, nz)
    xhigh = high2.reshape(len(x_dn), ny, nz)
    z_any = pick(lambda c: c[2] != 0)
    zh = jnp.concatenate([hz_m, hz_p])[jnp.array([z_up.index(n) if vel[n][2] == 1 else len(z_up) + z_dn.index(n) for n in z_any])]

    def spread(values, idx):
        zero = jnp.zeros((1,) + values.shape[1:], values.dtype)
        both = jnp.concatenate([values, zero])
        return both[jnp.array([idx.index(n) if n in idx else len(idx) for n in z_any])]

    corner_m = spread(cy_m, yz_up)[:, :, None]
    corner_p = spread(cy_p, yz_dn)[:, :, None]
    cy = by_pop(z_any, 1, (-1, 1, 1))
    cx = by_pop(z_any, 0, (-1, 1, 1))
    down = jnp.concatenate([corner_m, zh[:, :, :-1]], axis=2)
    up = jnp.concatenate([zh[:, :, 1:], corner_p], axis=2)
    zy = jnp.where(cy == 1, down, jnp.where(cy == -1, up, zh))
    edge_low = jnp.zeros((len(z_any), 1, ny), jnp.float32)
    edge_high = edge_low
    cols = jnp.where(
        cx == 1,
        jnp.concatenate([edge_low, zy[:, :-1]], axis=1),
        jnp.where(cx == -1, jnp.concatenate([zy[:, 1:], edge_high], axis=1), zy),
    )
    cols = jnp.broadcast_to(cols[:, :, :, None], (len(z_any), nx, ny, nz))
    pops = f_pop.shape[0]
    f_new, g_new = pl.pallas_call(
        stream_kernel,
        out_shape=(
            jax.ShapeDtypeStruct((pops, nx, ny, nz), jnp.float32),
            jax.ShapeDtypeStruct((pops, nx, ny, nz), jnp.float32),
        ),
        interpret=INTERPRET,
    )(post, xlow, xhigh, up2, dn2, cols)
    return (f_new, g_new)


def solution(mesh):
    return jax.shard_map(
        local,
        mesh=mesh,
        in_specs=(P(None, "gx", "gy", "gz"), P(None, "gx", "gy", "gz"), P()),
        out_specs=(P(None, "gx", "gy", "gz"), P(None, "gx", "gy", "gz")),
        check_vma=False,
    )
```
